32 devices in a mesh: dp: 8 (over y, x, core), tensor: 4 (over z).
Axes of the slice: x: 2, y: 2, z: 4, core: 2. Of those that a mesh axis runs over, the one named last changes fastest.
Arguments:
- teacher_master: float32 [256, 16384], P('dp', 'tensor'), as said below
- student_weight: bfloat16 [256, 16384], P('dp', 'tensor'), may hold values from -6 to 6
- teacher_feat: bfloat16 [2048, 256], P('dp'), as said below
- student_feat: bfloat16 [2048, 256], P('dp'), may hold values from -6 to 6
- center: float32 [16384], P('tensor'), may hold values from -0.3 to 0.3
Outputs:
- master_new: float32 [256, 16384], P('dp', 'tensor')
- student_grad: float32 [256, 16384], P('dp', 'tensor')
- new_center: float32 [16384], P('tensor')
The draws below stay inside these ranges and needn't reach their ends.
Inputs may be any that keep to these rules, and one draw needn't show every extreme that they name: `teacher_feat`: rows of teacher features are real-valued and of order one. `teacher_master`: entries of the teacher master are real-valued and of order one.
All inputs are finite; a program needn't handle non-finite values.
Results may differ from the reference program's by a relative error of at most 0.014.
Values may be sent and summed in bfloat16 or wider, within the bound.
No kernel may reach another device: no remote copies, remote signals or barrier semaphores. Data moves between devices by JAX's collectives and lax.ppermute only.
A program may use at most 64 MiB of HBM per device.

```python
import jax
import jax.numpy as jnp
from jax import lax

BOT = 256
B_DEV = 256
PROTO = 16384
IMAGES = 2048


def common_direction(key):
    return jax.random.normal(jax.random.fold_in(key, 12), (BOT,), jnp.float32)


def draw_teacher_feat(key, part):
    noise_key = jax.random.fold_in(key, 11)
    noise = jax.random.normal(noise_key, (IMAGES, BOT), jnp.float32)
    lift = 2.0
    direction = common_direction(key)
    strength = 0.1 + 0.9 * jnp.arange(IMAGES, dtype=jnp.float32) / IMAGES
    return (noise + lift * strength[:, None] * direction[None, :]).astype(jnp.bfloat16)


def draw_teacher_master(key, part):
    noise_key = jax.random.fold_in(key, 21)
    coef_key = jax.random.fold_in(key, 22)
    noise = jax.random.normal(noise_key, (BOT, PROTO), jnp.float32)
    coef = jax.random.uniform(coef_key, (PROTO,), jnp.float32, -1.0, 1.0)
    direction = common_direction(key)
    return (noise + coef[None, :] * direction[:, None]).astype(jnp.float32)


def spiked(drawn, stream_key, source, target, shards_of, factor):
    def block_of(dim):
        return (jnp.arange(drawn.shape[dim]) // (drawn.shape[dim] // shards_of)).reshape((-1,) + (1,) * (drawn.ndim - 1 - dim))

    near = jax.random.permutation(stream_key, shards_of)[block_of(target)]
    far = (block_of(target) + shards_of // 2) % shards_of
    return jnp.where((block_of(source) == near) | (block_of(source) == far), factor * drawn, drawn)


def block_levels(stream_key, extent, cuts, smallest, high):
    factor_of = 1.0
    for position, parts in cuts:
        steps = jax.random.uniform(jax.random.fold_in(jax.random.fold_in(stream_key, 6), position), (parts,), jnp.float32, smallest / len(cuts), high / len(cuts))
        factor_of = factor_of * jnp.repeat(jnp.exp(steps), extent[position] // parts).reshape((-1,) + (1,) * (len(extent) - 1 - position))
    return factor_of


def scatter_about(stream_key, extent, deviation, reach, cuts=(), kind=jnp.bfloat16):
    factor_of = block_levels(stream_key, extent, cuts, -0.22, 0.18) if cuts else 1.0
    drawn = jax.random.normal(stream_key, extent, jnp.float32) * deviation * factor_of
    return jnp.minimum(jnp.maximum(drawn, -reach), reach).astype(kind)


def bell_draw_with(rng, extent, scale, bound, pieces, heavy, held_as=jnp.bfloat16):
    values = scale * jax.random.normal(rng, extent, jnp.float32)
    if pieces:
        values = values * block_levels(rng, extent, pieces, -0.22, 0.18)
    return jnp.clip(spiked(values, jax.random.fold_in(rng, 3), *heavy), -bound, bound).astype(held_as)


def setup_inputs(seed: int = 0) -> dict:
    key_list = jax.random.split(jax.random.key(seed), 6)
    return {
        "teacher_master": draw_teacher_master(jax.random.fold_in(key_list[5], 71), 0),
        "student_weight": scatter_about(key_list[1], (BOT, PROTO), 1.0, 6.0, ((0, 8), (1, 4))),
        "teacher_feat": draw_teacher_feat(jax.random.fold_in(key_list[5], 71), 0),
        "student_feat": bell_draw_with(key_list[3], (IMAGES, BOT), 1.0, 6.0, ((0, 8),), (0, 1, 8, 2.0)),
        "center": jnp.clip(jax.random.uniform(key_list[4], (PROTO,), jnp.float32, -0.3, 0.3) * block_levels(key_list[4], (PROTO,), ((0, 4),), -0.4, 0.0), -0.3, 0.3),
    }


def unit_rows(feat):
    wide = feat.astype(jnp.float32)
    return (wide * lax.rsqrt(lax.optimization_barrier(jnp.sum(wide * wide, 1, keepdims=True)) + 1e-06)).astype(jnp.bfloat16)

def reference(teacher_master, student_weight, teacher_feat, student_feat, center):
    master_new = 0.996 * teacher_master + 0.004 * student_weight.astype(jnp.float32)
    teacher_weight = master_new.astype(jnp.bfloat16)
    t_norm = jnp.sqrt(lax.optimization_barrier(jnp.sum(jnp.square(teacher_weight.astype(jnp.float32)), 0)) + 1e-06)
    s_norm = jnp.sqrt(lax.optimization_barrier(jnp.sum(jnp.square(student_weight.astype(jnp.float32)), 0)) + 1e-06)
    blocks = IMAGES // B_DEV
    t_blocks = teacher_feat.reshape(blocks, B_DEV, BOT)
    s_blocks = student_feat.reshape(blocks, B_DEV, BOT)

    def step(carry, pair):
        grad_acc, r_acc, cos_acc = carry
        zt = unit_rows(pair[0])
        zs = unit_rows(pair[1])
        t_cos = jnp.dot(zt, teacher_weight, preferred_element_type=jnp.float32) / t_norm
        s_cos = jnp.dot(zs, student_weight, preferred_element_type=jnp.float32) / s_norm
        t_exp = jnp.exp((t_cos - center) / 0.04)
        t_prob = t_exp / lax.optimization_barrier(jnp.sum(t_exp, 1, keepdims=True))
        s_exp = jnp.exp(s_cos / 0.1)
        s_prob = s_exp / lax.optimization_barrier(jnp.sum(s_exp, 1, keepdims=True))
        dlog = ((s_prob - t_prob) / 0.1).astype(jnp.bfloat16)
        r_acc = r_acc + lax.optimization_barrier(jnp.sum(dlog.astype(jnp.float32) * s_cos, 0))
        grad_acc = grad_acc + jnp.dot(zs.T, dlog, preferred_element_type=jnp.float32)
        cos_acc = cos_acc + lax.optimization_barrier(jnp.sum(t_cos, 0))
        return ((grad_acc, r_acc, cos_acc), None)
    init = (jnp.zeros((BOT, PROTO), jnp.float32), jnp.zeros((PROTO,), jnp.float32), jnp.zeros((PROTO,), jnp.float32))
    (grad_acc, r_acc, cos_acc), _ = lax.scan(step, init, (t_blocks, s_blocks))
    student_grad = (grad_acc - student_weight.astype(jnp.float32) * (r_acc / s_norm)) / s_norm
    new_center = 0.5 * center + 0.5 * (cos_acc / IMAGES)
    return (master_new, student_grad, new_center)
```

```python
import jax
import jax.numpy as jnp
from jax import lax
from jax.sharding import PartitionSpec as P


def unit_rows(feat):
    wide = feat.astype(jnp.float32)
    return (wide * lax.rsqrt(jnp.sum(wide * wide, 1, keepdims=True) + 1e-06)).astype(jnp.bfloat16)


def weight_plan(teacher_master, student_weight, teacher_feat, student_feat, center):
    zt = unit_rows(teacher_feat)
    zs = unit_rows(student_feat)
    images_all = teacher_feat.shape[0] * lax.axis_size("dp")
    student_full = lax.all_gather(student_weight, "dp", axis=0, tiled=True)
    master_new = 0.996 * teacher_master + 0.004 * student_weight.astype(jnp.float32)
    weight = lax.all_gather(master_new.astype(jnp.bfloat16), "dp", axis=0, tiled=True)
    raw = jnp.dot(zt, weight, preferred_element_type=jnp.float32)
    t_norm = jnp.sqrt(jnp.sum(jnp.square(weight.astype(jnp.float32)), 0) + 1e-06)
    t_cos = raw / t_norm
    s_norm = jnp.sqrt(jnp.sum(jnp.square(student_full.astype(jnp.float32)), 0) + 1e-06)
    s_cos = jnp.dot(zs, student_full, preferred_element_type=jnp.float32) / s_norm
    t_exp = jnp.exp((t_cos - center) / 0.04)
    s_exp = jnp.exp(s_cos / 0.1)
    t_total, s_total = lax.psum(
        (jnp.sum(t_exp, 1, keepdims=True), jnp.sum(s_exp, 1, keepdims=True)), "tensor"
    )
    cos_mean = lax.psum(jnp.sum(t_cos, 0), "dp") / images_all
    new_center = 0.5 * center + 0.5 * cos_mean
    dlog = ((s_exp / s_total - t_exp / t_total) / 0.1).astype(jnp.bfloat16)
    scaled = jnp.sum(dlog.astype(jnp.float32) * s_cos, 0) / s_norm
    product = lax.dot_general(
        zs, dlog, (((0,), (0,)), ((), ())), preferred_element_type=jnp.float32
    )
    student_grad = lax.psum_scatter(
        (product - student_full.astype(jnp.float32) * scaled) / s_norm,
        "dp",
        scatter_dimension=0,
        tiled=True,
    )
    return (master_new, student_grad, new_center)


def feature_plan(teacher_master, student_weight, teacher_feat, student_feat, center):
    ndp = lax.axis_size("dp")
    bot = teacher_feat.shape[1]
    images_all = teacher_feat.shape[0] * ndp
    cols = center.shape[0] // ndp
    master_new = 0.996 * teacher_master + 0.004 * student_weight.astype(jnp.float32)
    both = jnp.stack([student_weight, master_new.astype(jnp.bfloat16)])
    both = lax.all_to_all(both, "dp", 2, 1, tiled=True)
    sw, tw = both[0], both[1]
    feats = jnp.concatenate([unit_rows(teacher_feat), unit_rows(student_feat)], axis=1)
    feats = lax.all_gather(feats, "dp", axis=0, tiled=True)
    zt, zs = feats[:, :bot], feats[:, bot:]
    c = lax.dynamic_slice_in_dim(center, lax.axis_index("dp") * cols, cols)
    t_norm = jnp.sqrt(jnp.sum(jnp.square(tw.astype(jnp.float32)), 0) + 1e-06)
    s_norm = jnp.sqrt(jnp.sum(jnp.square(sw.astype(jnp.float32)), 0) + 1e-06)
    t_cos = jnp.dot(zt, tw, preferred_element_type=jnp.float32) / t_norm
    s_cos = jnp.dot(zs, sw, preferred_element_type=jnp.float32) / s_norm
    t_exp = jnp.exp((t_cos - c) / 0.04)
    s_exp = jnp.exp(s_cos / 0.1)
    totals = lax.psum(
        jnp.stack([jnp.sum(t_exp, 1), jnp.sum(s_exp, 1)], axis=1), ("dp", "tensor")
    )
    t_total, s_total = totals[:, 0:1], totals[:, 1:2]
    part_center = 0.5 * c + 0.5 * (jnp.sum(t_cos, 0) / images_all)
    new_center = lax.all_gather(part_center, "dp", axis=0, tiled=True)
    dlog = ((s_exp / s_total - t_exp / t_total) / 0.1).astype(jnp.bfloat16)
    scaled = jnp.sum(dlog.astype(jnp.float32) * s_cos, 0) / s_norm
    product = lax.dot_general(
        zs, dlog, (((0,), (0,)), ((), ())), preferred_element_type=jnp.float32
    )
    grad = (product - sw.astype(jnp.float32) * scaled) / s_norm
    student_grad = lax.all_to_all(grad, "dp", 0, 1, tiled=True)
    return (master_new, student_grad, new_center)


def solution(mesh):
    placed = (P("dp", "tensor"), P("dp", "tensor"), P("dp", None), P("dp", None), P("tensor"))
    return jax.shard_map(
        shards_for(mesh),
        mesh=mesh,
        in_specs=placed,
        out_specs=(P("dp", "tensor"), P("dp", "tensor"), P("tensor")),
        check_vma=False,
    )


def shards_for(mesh):
    ndp = mesh.shape["dp"]

    def shards(teacher_master, student_weight, teacher_feat, student_feat, center):
        images_all = teacher_feat.shape[0] * ndp
        cols = center.shape[0]
        if images_all < cols and cols % ndp == 0:
            return feature_plan(teacher_master, student_weight, teacher_feat, student_feat, center)
        return weight_plan(teacher_master, student_weight, teacher_feat, student_feat, center)

    return shards
```

```python
import jax
import jax.numpy as jnp
from jax import lax
from jax.sharding import PartitionSpec as P


def unit_rows(feat):
    wide = feat.astype(jnp.float32)
    return (wide * lax.rsqrt(jnp.sum(wide * wide, 1, keepdims=True) + 1e-06)).astype(jnp.bfloat16)


def weight_plan(teacher_master, student_weight, teacher_feat, student_feat, center):
    zt = unit_rows(teacher_feat)
    zs = unit_rows(student_feat)
    images_all = teacher_feat.shape[0] * lax.axis_size("dp")
    student_full = lax.all_gather(student_weight, "dp", axis=0, tiled=True)
    master_new = 0.996 * teacher_master + 0.004 * student_weight.astype(jnp.float32)
    weight = lax.all_gather(master_new.astype(jnp.bfloat16), "dp", axis=0, tiled=True)
    raw = jnp.dot(zt, weight, preferred_element_type=jnp.float32)
    t_norm = jnp.sqrt(jnp.sum(jnp.square(weight.astype(jnp.float32)), 0) + 1e-06)
    t_cos = raw / t_norm
    s_norm = jnp.sqrt(jnp.sum(jnp.square(student_full.astype(jnp.float32)), 0) + 1e-06)
    s_cos = jnp.dot(zs, student_full, preferred_element_type=jnp.float32) / s_norm
    t_exp = jnp.exp((t_cos - center) / 0.04)
    s_exp = jnp.exp(s_cos / 0.1)
    t_total, s_total = lax.psum(
        (jnp.sum(t_exp, 1, keepdims=True), jnp.sum(s_exp, 1, keepdims=True)), "tensor"
    )
    cos_mean = lax.psum(jnp.sum(t_cos, 0), "dp") / images_all
    new_center = 0.5 * center + 0.5 * cos_mean
    dlog = ((s_exp / s_total - t_exp / t_total) / 0.1).astype(jnp.bfloat16)
    scaled = jnp.sum(dlog.astype(jnp.float32) * s_cos, 0) / s_norm
    product = lax.dot_general(
        zs, dlog, (((0,), (0,)), ((), ())), preferred_element_type=jnp.float32
    )
    student_grad = lax.psum_scatter(
        (product - student_full.astype(jnp.float32) * scaled) / s_norm,
        "dp",
        scatter_dimension=0,
        tiled=True,
    )
    return (master_new, student_grad, new_center)


def feature_plan(teacher_master, student_weight, teacher_feat, student_feat, center):
    ndp = lax.axis_size("dp")
    bot = teacher_feat.shape[1]
    images_all = teacher_feat.shape[0] * ndp
    cols = center.shape[0] // ndp
    master_new = 0.996 * teacher_master + 0.004 * student_weight.astype(jnp.float32)
    both = jnp.stack([student_weight, master_new.astype(jnp.bfloat16)])
    both = lax.all_to_all(both, "dp", 2, 1, tiled=True)
    sw, tw = both[0], both[1]
    feats = jnp.concatenate([unit_rows(teacher_feat), unit_rows(student_feat)], axis=1)
    feats = lax.all_gather(feats, "dp", axis=0, tiled=True)
    zt, zs = feats[:, :bot], feats[:, bot:]
    c = lax.dynamic_slice_in_dim(center, lax.axis_index("dp") * cols, cols)
    t_norm = jnp.sqrt(jnp.sum(jnp.square(tw.astype(jnp.float32)), 0) + 1e-06)
    s_norm = jnp.sqrt(jnp.sum(jnp.square(sw.astype(jnp.float32)), 0) + 1e-06)
    t_cos = jnp.dot(zt, tw, preferred_element_type=jnp.float32) / t_norm
    s_cos = jnp.dot(zs, sw, preferred_element_type=jnp.float32) / s_norm
    t_exp = jnp.exp((t_cos - c) / 0.04)
    s_exp = jnp.exp(s_cos / 0.1)
    totals = lax.psum(jnp.stack([jnp.sum(t_exp, 1), jnp.sum(s_exp, 1)]), ("dp", "tensor"))
    t_total, s_total = totals[0][:, None], totals[1][:, None]
    part_center = 0.5 * c + 0.5 * (jnp.sum(t_cos, 0) / images_all)
    dlog = ((s_exp / s_total - t_exp / t_total) / 0.1).astype(jnp.bfloat16)
    scaled = jnp.sum(dlog.astype(jnp.float32) * s_cos, 0) / s_norm
    product = lax.dot_general(
        zs, dlog, (((0,), (0,)), ((), ())), preferred_element_type=jnp.float32
    )
    grad = (product - sw.astype(jnp.float32) * scaled) / s_norm
    rows = grad.shape[0] // ndp
    sent = jnp.concatenate(
        [grad.reshape(ndp, rows, cols), jnp.broadcast_to(part_center, (ndp, 1, cols))], axis=1
    )
    got = lax.all_to_all(sent, "dp", 0, 2, tiled=True)
    got = got.reshape(rows + 1, ndp * cols)
    return (master_new, got[:rows], got[rows])


def solution(mesh):
    placed = (P("dp", "tensor"), P("dp", "tensor"), P("dp", None), P("dp", None), P("tensor"))
    return jax.shard_map(
        shards_for(mesh),
        mesh=mesh,
        in_specs=placed,
        out_specs=(P("dp", "tensor"), P("dp", "tensor"), P("tensor")),
        check_vma=False,
    )


def shards_for(mesh):
    ndp = mesh.shape["dp"]

    def shards(teacher_master, student_weight, teacher_feat, student_feat, center):
        images_all = teacher_feat.shape[0] * ndp
        cols = center.shape[0]
        if images_all < cols and cols % ndp == 0:
            return feature_plan(teacher_master, student_weight, teacher_feat, student_feat, center)
        return weight_plan(teacher_master, student_weight, teacher_feat, student_feat, center)

    return shards
```

```python
import jax
import jax.numpy as jnp
from jax import lax
from jax.sharding import PartitionSpec as P


def unit_rows(feat):
    wide = feat.astype(jnp.float32)
    return (wide * lax.rsqrt(jnp.sum(wide * wide, 1, keepdims=True) + 1e-06)).astype(jnp.bfloat16)


def weight_plan(teacher_master, student_weight, teacher_feat, student_feat, center):
    zt = unit_rows(teacher_feat)
    zs = unit_rows(student_feat)
    images_all = teacher_feat.shape[0] * lax.axis_size("dp")
    student_full = lax.all_gather(student_weight, "dp", axis=0, tiled=True)
    master_new = 0.996 * teacher_master + 0.004 * student_weight.astype(jnp.float32)
    weight = lax.all_gather(master_new.astype(jnp.bfloat16), "dp", axis=0, tiled=True)
    raw = jnp.dot(zt, weight, preferred_element_type=jnp.float32)
    t_norm = jnp.sqrt(jnp.sum(jnp.square(weight.astype(jnp.float32)), 0) + 1e-06)
    t_cos = raw / t_norm
    s_norm = jnp.sqrt(jnp.sum(jnp.square(student_full.astype(jnp.float32)), 0) + 1e-06)
    s_cos = jnp.dot(zs, student_full, preferred_element_type=jnp.float32) / s_norm
    t_exp = jnp.exp((t_cos - center) / 0.04)
    s_exp = jnp.exp(s_cos / 0.1)
    t_total, s_total = lax.psum(
        (jnp.sum(t_exp, 1, keepdims=True), jnp.sum(s_exp, 1, keepdims=True)), "tensor"
    )
    cos_mean = lax.psum(jnp.sum(t_cos, 0), "dp") / images_all
    new_center = 0.5 * center + 0.5 * cos_mean
    dlog = ((s_exp / s_total - t_exp / t_total) / 0.1).astype(jnp.bfloat16)
    scaled = jnp.sum(dlog.astype(jnp.float32) * s_cos, 0) / s_norm
    product = lax.dot_general(
        zs, dlog, (((0,), (0,)), ((), ())), preferred_element_type=jnp.float32
    )
    student_grad = lax.psum_scatter(
        (product - student_full.astype(jnp.float32) * scaled) / s_norm,
        "dp",
        scatter_dimension=0,
        tiled=True,
    )
    return (master_new, student_grad, new_center)


def exchange_sum(x, axis, n):
    if n & (n - 1):
        return lax.psum(x, axis)
    step = 1
    while step < n:
        x = x + lax.ppermute(x, axis, [(i, i ^ step) for i in range(n)])
        step *= 2
    return x


def feature_plan(teacher_master, student_weight, teacher_feat, student_feat, center):
    ndp = lax.axis_size("dp")
    bot = teacher_feat.shape[1]
    images_all = teacher_feat.shape[0] * ndp
    cols = center.shape[0] // ndp
    master_new = 0.996 * teacher_master + 0.004 * student_weight.astype(jnp.float32)
    both = jnp.stack([student_weight, master_new.astype(jnp.bfloat16)])
    both = lax.all_to_all(both, "dp", 2, 1, tiled=True)
    sw, tw = both[0], both[1]
    feats = jnp.concatenate([unit_rows(teacher_feat), unit_rows(student_feat)], axis=1)
    feats = lax.all_gather(feats, "dp", axis=0, tiled=True)
    zt, zs = feats[:, :bot], feats[:, bot:]
    c = lax.dynamic_slice_in_dim(center, lax.axis_index("dp") * cols, cols)
    t_norm = jnp.sqrt(jnp.sum(jnp.square(tw.astype(jnp.float32)), 0) + 1e-06)
    s_norm = jnp.sqrt(jnp.sum(jnp.square(sw.astype(jnp.float32)), 0) + 1e-06)
    t_cos = jnp.dot(zt, tw, preferred_element_type=jnp.float32) / t_norm
    s_cos = jnp.dot(zs, sw, preferred_element_type=jnp.float32) / s_norm
    t_exp = jnp.exp((t_cos - c) / 0.04)
    s_exp = jnp.exp(s_cos / 0.1)
    totals = jnp.stack([jnp.sum(t_exp, 1), jnp.sum(s_exp, 1)])
    totals = exchange_sum(exchange_sum(totals, "dp", ndp), "tensor", lax.axis_size("tensor"))
    t_total, s_total = totals[0][:, None], totals[1][:, None]
    part_center = 0.5 * c + 0.5 * (jnp.sum(t_cos, 0) / images_all)
    dlog = ((s_exp / s_total - t_exp / t_total) / 0.1).astype(jnp.bfloat16)
    scaled = jnp.sum(dlog.astype(jnp.float32) * s_cos, 0) / s_norm
    product = lax.dot_general(
        zs, dlog, (((0,), (0,)), ((), ())), preferred_element_type=jnp.float32
    )
    grad = (product - sw.astype(jnp.float32) * scaled) / s_norm
    rows = grad.shape[0] // ndp
    sent = jnp.concatenate(
        [grad.reshape(ndp, rows, cols), jnp.broadcast_to(part_center, (ndp, 1, cols))], axis=1
    )
    got = lax.all_to_all(sent, "dp", 0, 2, tiled=True)
    got = got.reshape(rows + 1, ndp * cols)
    return (master_new, got[:rows], got[rows])


def solution(mesh):
    placed = (P("dp", "tensor"), P("dp", "tensor"), P("dp", None), P("dp", None), P("tensor"))
    return jax.shard_map(
        shards_for(mesh),
        mesh=mesh,
        in_specs=placed,
        out_specs=(P("dp", "tensor"), P("dp", "tensor"), P("tensor")),
        check_vma=False,
    )


def shards_for(mesh):
    ndp = mesh.shape["dp"]

    def shards(teacher_master, student_weight, teacher_feat, student_feat, center):
        images_all = teacher_feat.shape[0] * ndp
        cols = center.shape[0]
        if images_all < cols and cols % ndp == 0:
            return feature_plan(teacher_master, student_weight, teacher_feat, student_feat, center)
        return weight_plan(teacher_master, student_weight, teacher_feat, student_feat, center)

    return shards
```

```python
import jax
import jax.numpy as jnp
from jax import lax
from jax.sharding import PartitionSpec as P


def unit_rows(feat):
    wide = feat.astype(jnp.float32)
    return (wide * lax.rsqrt(jnp.sum(wide * wide, 1, keepdims=True) + 1e-06)).astype(jnp.bfloat16)


def weight_plan(teacher_master, student_weight, teacher_feat, student_feat, center):
    zt = unit_rows(teacher_feat)
    zs = unit_rows(student_feat)
    images_all = teacher_feat.shape[0] * lax.axis_size("dp")
    student_full = lax.all_gather(student_weight, "dp", axis=0, tiled=True)
    master_new = 0.996 * teacher_master + 0.004 * student_weight.astype(jnp.float32)
    weight = lax.all_gather(master_new.astype(jnp.bfloat16), "dp", axis=0, tiled=True)
    raw = jnp.dot(zt, weight, preferred_element_type=jnp.float32)
    t_norm = jnp.sqrt(jnp.sum(jnp.square(weight.astype(jnp.float32)), 0) + 1e-06)
    t_cos = raw / t_norm
    s_norm = jnp.sqrt(jnp.sum(jnp.square(student_full.astype(jnp.float32)), 0) + 1e-06)
    s_cos = jnp.dot(zs, student_full, preferred_element_type=jnp.float32) / s_norm
    t_exp = jnp.exp((t_cos - center) / 0.04)
    s_exp = jnp.exp(s_cos / 0.1)
    t_total, s_total = lax.psum(
        (jnp.sum(t_exp, 1, keepdims=True), jnp.sum(s_exp, 1, keepdims=True)), "tensor"
    )
    cos_mean = lax.psum(jnp.sum(t_cos, 0), "dp") / images_all
    new_center = 0.5 * center + 0.5 * cos_mean
    dlog = ((s_exp / s_total - t_exp / t_total) / 0.1).astype(jnp.bfloat16)
    scaled = jnp.sum(dlog.astype(jnp.float32) * s_cos, 0) / s_norm
    product = lax.dot_general(
        zs, dlog, (((0,), (0,)), ((), ())), preferred_element_type=jnp.float32
    )
    student_grad = lax.psum_scatter(
        (product - student_full.astype(jnp.float32) * scaled) / s_norm,
        "dp",
        scatter_dimension=0,
        tiled=True,
    )
    return (master_new, student_grad, new_center)


def exchange_sum(x, axis, n):
    if n & (n - 1):
        return lax.psum(x, axis)
    step = 1
    while step < n:
        x = x + lax.ppermute(x, axis, [(i, i ^ step) for i in range(n)])
        step *= 2
    return x


def feature_plan(teacher_master, student_weight, teacher_feat, student_feat, center):
    n = lax.axis_size("dp")
    me = lax.axis_index("dp")
    rows, width = teacher_master.shape
    bot = teacher_feat.shape[1]
    images = teacher_feat.shape[0]
    cols = width // n
    master_new = 0.996 * teacher_master + 0.004 * student_weight.astype(jnp.float32)
    local = jnp.stack([student_weight, master_new.astype(jnp.bfloat16)])
    feat = jnp.concatenate([unit_rows(teacher_feat), unit_rows(student_feat)], axis=1)
    feats, blocks = [feat], [lax.dynamic_slice_in_dim(local, me * cols, cols, axis=2)]
    for k in range(1, n):
        part = lax.dynamic_slice_in_dim(local, (me ^ k) * cols, cols, axis=2)
        got_feat, got_part = lax.ppermute((feat, part), "dp", [(i, i ^ k) for i in range(n)])
        feats.append(got_feat)
        blocks.append(got_part)
    feats = jnp.concatenate(feats, axis=0)
    order = me ^ jnp.arange(n)
    both = jnp.take(jnp.stack(blocks, axis=1), order, axis=1).reshape(2, n * rows, cols)
    sw, tw = both[0], both[1]
    zt, zs = feats[:, :bot], feats[:, bot:]
    c = lax.dynamic_slice_in_dim(center, me * cols, cols)
    t_norm = jnp.sqrt(jnp.sum(jnp.square(tw.astype(jnp.float32)), 0) + 1e-06)
    s_norm = jnp.sqrt(jnp.sum(jnp.square(sw.astype(jnp.float32)), 0) + 1e-06)
    t_cos = jnp.dot(zt, tw, preferred_element_type=jnp.float32) / t_norm
    s_cos = jnp.dot(zs, sw, preferred_element_type=jnp.float32) / s_norm
    t_exp = jnp.exp((t_cos - c) / 0.04)
    s_exp = jnp.exp(s_cos / 0.1)
    totals = jnp.stack([jnp.sum(t_exp, 1), jnp.sum(s_exp, 1)])
    step = 1
    while step < n:
        got = lax.ppermute(totals, "dp", [(i, i ^ step) for i in range(n)])
        got = got.reshape(2, n // (2 * step), 2, step, images)[:, :, ::-1]
        totals = totals + got.reshape(2, n * images)
        step *= 2
    totals = exchange_sum(totals, "tensor", lax.axis_size("tensor"))
    t_total, s_total = totals[0][:, None], totals[1][:, None]
    part_center = 0.5 * c + 0.5 * (jnp.sum(t_cos, 0) / (images * n))
    dlog = ((s_exp / s_total - t_exp / t_total) / 0.1).astype(jnp.bfloat16)
    scaled = jnp.sum(dlog.astype(jnp.float32) * s_cos, 0) / s_norm
    product = lax.dot_general(
        zs, dlog, (((0,), (0,)), ((), ())), preferred_element_type=jnp.float32
    )
    grad = (product - sw.astype(jnp.float32) * scaled) / s_norm
    sent = jnp.concatenate(
        [grad.reshape(n, rows, cols), jnp.broadcast_to(part_center, (n, 1, cols))], axis=1
    )
    back = [sent[me]]
    for k in range(1, n):
        back.append(lax.ppermute(sent[me ^ k], "dp", [(i, i ^ k) for i in range(n)]))
    got = jnp.take(jnp.stack(back, axis=1), order, axis=1).reshape(rows + 1, n * cols)
    return (master_new, got[:rows], got[rows])


def solution(mesh):
    placed = (P("dp", "tensor"), P("dp", "tensor"), P("dp", None), P("dp", None), P("tensor"))
    return jax.shard_map(
        shards_for(mesh),
        mesh=mesh,
        in_specs=placed,
        out_specs=(P("dp", "tensor"), P("dp", "tensor"), P("tensor")),
        check_vma=False,
    )


def shards_for(mesh):
    ndp = mesh.shape["dp"]

    def shards(teacher_master, student_weight, teacher_feat, student_feat, center):
        images_all = teacher_feat.shape[0] * ndp
        cols = center.shape[0]
        if images_all < cols and cols % ndp == 0 and ndp & (ndp - 1) == 0:
            return feature_plan(teacher_master, student_weight, teacher_feat, student_feat, center)
        return weight_plan(teacher_master, student_weight, teacher_feat, student_feat, center)

    return shards
```

```python
import jax
import jax.numpy as jnp
from jax import lax
from jax.sharding import PartitionSpec as P


def unit_rows(feat):
    wide = feat.astype(jnp.float32)
    return (wide * lax.rsqrt(jnp.sum(wide * wide, 1, keepdims=True) + 1e-06)).astype(jnp.bfloat16)


def weight_plan(teacher_master, student_weight, teacher_feat, student_feat, center):
    zt = unit_rows(teacher_feat)
    zs = unit_rows(student_feat)
    images_all = teacher_feat.shape[0] * lax.axis_size("dp")
    student_full = lax.all_gather(student_weight, "dp", axis=0, tiled=True)
    master_new = 0.996 * teacher_master + 0.004 * student_weight.astype(jnp.float32)
    weight = lax.all_gather(master_new.astype(jnp.bfloat16), "dp", axis=0, tiled=True)
    raw = jnp.dot(zt, weight, preferred_element_type=jnp.float32)
    t_norm = jnp.sqrt(jnp.sum(jnp.square(weight.astype(jnp.float32)), 0) + 1e-06)
    t_cos = raw / t_norm
    s_norm = jnp.sqrt(jnp.sum(jnp.square(student_full.astype(jnp.float32)), 0) + 1e-06)
    s_cos = jnp.dot(zs, student_full, preferred_element_type=jnp.float32) / s_norm
    t_exp = jnp.exp((t_cos - center) / 0.04)
    s_exp = jnp.exp(s_cos / 0.1)
    t_total, s_total = lax.psum(
        (jnp.sum(t_exp, 1, keepdims=True), jnp.sum(s_exp, 1, keepdims=True)), "tensor"
    )
    cos_mean = lax.psum(jnp.sum(t_cos, 0), "dp") / images_all
    new_center = 0.5 * center + 0.5 * cos_mean
    dlog = ((s_exp / s_total - t_exp / t_total) / 0.1).astype(jnp.bfloat16)
    scaled = jnp.sum(dlog.astype(jnp.float32) * s_cos, 0) / s_norm
    product = lax.dot_general(
        zs, dlog, (((0,), (0,)), ((), ())), preferred_element_type=jnp.float32
    )
    student_grad = lax.psum_scatter(
        (product - student_full.astype(jnp.float32) * scaled) / s_norm,
        "dp",
        scatter_dimension=0,
        tiled=True,
    )
    return (master_new, student_grad, new_center)


def exchange_sum(x, axis, n):
    if n & (n - 1):
        return lax.psum(x, axis)
    step = 1
    while step < n:
        x = x + lax.ppermute(x, axis, [(i, i ^ step) for i in range(n)])
        step *= 2
    return x


def exchange_all(x, axis, n):
    total = x
    for k in range(1, n):
        total = total + lax.ppermute(x, axis, [(i, (i + k) % n) for i in range(n)])
    return total


def feature_plan(teacher_master, student_weight, teacher_feat, student_feat, center):
    ndp = lax.axis_size("dp")
    bot = teacher_feat.shape[1]
    images_all = teacher_feat.shape[0] * ndp
    cols = center.shape[0] // ndp
    master_new = 0.996 * teacher_master + 0.004 * student_weight.astype(jnp.float32)
    both = jnp.stack([student_weight, master_new.astype(jnp.bfloat16)])
    both = lax.all_to_all(both, "dp", 2, 1, tiled=True)
    sw, tw = both[0], both[1]
    feats = jnp.concatenate([unit_rows(teacher_feat), unit_rows(student_feat)], axis=1)
    feats = lax.all_gather(feats, "dp", axis=0, tiled=True)
    zt, zs = feats[:, :bot], feats[:, bot:]
    c = lax.dynamic_slice_in_dim(center, lax.axis_index("dp") * cols, cols)
    t_norm = jnp.sqrt(jnp.sum(jnp.square(tw.astype(jnp.float32)), 0) + 1e-06)
    s_norm = jnp.sqrt(jnp.sum(jnp.square(sw.astype(jnp.float32)), 0) + 1e-06)
    t_cos = jnp.dot(zt, tw, preferred_element_type=jnp.float32) / t_norm
    s_cos = jnp.dot(zs, sw, preferred_element_type=jnp.float32) / s_norm
    t_exp = jnp.exp((t_cos - c) / 0.04)
    s_exp = jnp.exp(s_cos / 0.1)
    totals = jnp.stack([jnp.sum(t_exp, 1), jnp.sum(s_exp, 1)])
    totals = exchange_all(exchange_all(totals, "dp", ndp), "tensor", lax.axis_size("tensor"))
    t_total, s_total = totals[0][:, None], totals[1][:, None]
    part_center = 0.5 * c + 0.5 * (jnp.sum(t_cos, 0) / images_all)
    dlog = ((s_exp / s_total - t_exp / t_total) / 0.1).astype(jnp.bfloat16)
    scaled = jnp.sum(dlog.astype(jnp.float32) * s_cos, 0) / s_norm
    product = lax.dot_general(
        zs, dlog, (((0,), (0,)), ((), ())), preferred_element_type=jnp.float32
    )
    grad = (product - sw.astype(jnp.float32) * scaled) / s_norm
    rows = grad.shape[0] // ndp
    high = part_center.astype(jnp.bfloat16)
    low = (part_center - high.astype(jnp.float32)).astype(jnp.bfloat16)
    sent = jnp.concatenate(
        [
            grad.astype(jnp.bfloat16).reshape(ndp, rows, cols),
            jnp.broadcast_to(jnp.stack([high, low]), (ndp, 2, cols)),
        ],
        axis=1,
    )
    got = lax.all_to_all(sent, "dp", 0, 2, tiled=True)
    got = got.reshape(rows + 2, ndp * cols).astype(jnp.float32)
    return (master_new, got[:rows], got[rows] + got[rows + 1])


def solution(mesh):
    placed = (P("dp", "tensor"), P("dp", "tensor"), P("dp", None), P("dp", None), P("tensor"))
    return jax.shard_map(
        shards_for(mesh),
        mesh=mesh,
        in_specs=placed,
        out_specs=(P("dp", "tensor"), P("dp", "tensor"), P("tensor")),
        check_vma=False,
    )


def shards_for(mesh):
    ndp = mesh.shape["dp"]

    def shards(teacher_master, student_weight, teacher_feat, student_feat, center):
        images_all = teacher_feat.shape[0] * ndp
        cols = center.shape[0]
        if images_all < cols and cols % ndp == 0:
            return feature_plan(teacher_master, student_weight, teacher_feat, student_feat, center)
        return weight_plan(teacher_master, student_weight, teacher_feat, student_feat, center)

    return shards
```

```python
import jax
import jax.numpy as jnp
from jax import lax
from jax.sharding import PartitionSpec as P


def unit_rows(feat):
    wide = feat.astype(jnp.float32)
    return (wide * lax.rsqrt(jnp.sum(wide * wide, 1, keepdims=True) + 1e-06)).astype(jnp.bfloat16)


def weight_plan(teacher_master, student_weight, teacher_feat, student_feat, center):
    zt = unit_rows(teacher_feat)
    zs = unit_rows(student_feat)
    images_all = teacher_feat.shape[0] * lax.axis_size("dp")
    student_full = lax.all_gather(student_weight, "dp", axis=0, tiled=True)
    master_new = 0.996 * teacher_master + 0.004 * student_weight.astype(jnp.float32)
    weight = lax.all_gather(master_new.astype(jnp.bfloat16), "dp", axis=0, tiled=True)
    raw = jnp.dot(zt, weight, preferred_element_type=jnp.float32)
    t_norm = jnp.sqrt(jnp.sum(jnp.square(weight.astype(jnp.float32)), 0) + 1e-06)
    t_cos = raw / t_norm
    s_norm = jnp.sqrt(jnp.sum(jnp.square(student_full.astype(jnp.float32)), 0) + 1e-06)
    s_cos = jnp.dot(zs, student_full, preferred_element_type=jnp.float32) / s_norm
    t_exp = jnp.exp((t_cos - center) / 0.04)
    s_exp = jnp.exp(s_cos / 0.1)
    t_total, s_total = lax.psum(
        (jnp.sum(t_exp, 1, keepdims=True), jnp.sum(s_exp, 1, keepdims=True)), "tensor"
    )
    cos_mean = lax.psum(jnp.sum(t_cos, 0), "dp") / images_all
    new_center = 0.5 * center + 0.5 * cos_mean
    dlog = ((s_exp / s_total - t_exp / t_total) / 0.1).astype(jnp.bfloat16)
    scaled = jnp.sum(dlog.astype(jnp.float32) * s_cos, 0) / s_norm
    product = lax.dot_general(
        zs, dlog, (((0,), (0,)), ((), ())), preferred_element_type=jnp.float32
    )
    student_grad = lax.psum_scatter(
        (product - student_full.astype(jnp.float32) * scaled) / s_norm,
        "dp",
        scatter_dimension=0,
        tiled=True,
    )
    return (master_new, student_grad, new_center)


def exchange_sum(x, axis, n):
    if n & (n - 1):
        return lax.psum(x, axis)
    step = 1
    while step < n:
        x = x + lax.ppermute(x, axis, [(i, i ^ step) for i in range(n)])
        step *= 2
    return x


def exchange_all(x, axis, n):
    total = x
    for k in range(1, n):
        total = total + lax.ppermute(x, axis, [(i, (i + k) % n) for i in range(n)])
    return total


def feature_plan(teacher_master, student_weight, teacher_feat, student_feat, center):
    ndp = lax.axis_size("dp")
    bot = teacher_feat.shape[1]
    images_all = teacher_feat.shape[0] * ndp
    cols = center.shape[0] // ndp
    master_new = 0.996 * teacher_master + 0.004 * student_weight.astype(jnp.float32)
    both = jnp.stack([student_weight, master_new.astype(jnp.bfloat16)])
    both = lax.all_to_all(both, "dp", 2, 1, tiled=True)
    sw, tw = both[0], both[1]
    feats = jnp.concatenate([unit_rows(teacher_feat), unit_rows(student_feat)], axis=1)
    feats = lax.all_gather(feats, "dp", axis=0, tiled=True)
    zt, zs = feats[:, :bot], feats[:, bot:]
    c = lax.dynamic_slice_in_dim(center, lax.axis_index("dp") * cols, cols)
    t_norm = jnp.sqrt(jnp.sum(jnp.square(tw.astype(jnp.float32)), 0) + 1e-06)
    s_norm = jnp.sqrt(jnp.sum(jnp.square(sw.astype(jnp.float32)), 0) + 1e-06)
    t_cos = jnp.dot(zt, tw, preferred_element_type=jnp.float32) / t_norm
    s_cos = jnp.dot(zs, sw, preferred_element_type=jnp.float32) / s_norm
    t_exp = jnp.exp((t_cos - c) / 0.04)
    s_exp = jnp.exp(s_cos / 0.1)
    totals = jnp.stack([jnp.sum(t_exp, 1), jnp.sum(s_exp, 1)])
    everyone = ndp * lax.axis_size("tensor")
    totals = jnp.broadcast_to(totals[None], (everyone,) + totals.shape)
    totals = jnp.sum(lax.all_to_all(totals, ("dp", "tensor"), 0, 0, tiled=True), 0)
    t_total, s_total = totals[0][:, None], totals[1][:, None]
    part_center = 0.5 * c + 0.5 * (jnp.sum(t_cos, 0) / images_all)
    dlog = ((s_exp / s_total - t_exp / t_total) / 0.1).astype(jnp.bfloat16)
    scaled = jnp.sum(dlog.astype(jnp.float32) * s_cos, 0) / s_norm
    product = lax.dot_general(
        zs, dlog, (((0,), (0,)), ((), ())), preferred_element_type=jnp.float32
    )
    grad = (product - sw.astype(jnp.float32) * scaled) / s_norm
    rows = grad.shape[0] // ndp
    high = part_center.astype(jnp.bfloat16)
    low = (part_center - high.astype(jnp.float32)).astype(jnp.bfloat16)
    sent = jnp.concatenate(
        [
            grad.astype(jnp.bfloat16).reshape(ndp, rows, cols),
            jnp.broadcast_to(jnp.stack([high, low]), (ndp, 2, cols)),
        ],
        axis=1,
    )
    got = lax.all_to_all(sent, "dp", 0, 2, tiled=True)
    got = got.reshape(rows + 2, ndp * cols).astype(jnp.float32)
    return (master_new, got[:rows], got[rows] + got[rows + 1])


def solution(mesh):
    placed = (P("dp", "tensor"), P("dp", "tensor"), P("dp", None), P("dp", None), P("tensor"))
    return jax.shard_map(
        shards_for(mesh),
        mesh=mesh,
        in_specs=placed,
        out_specs=(P("dp", "tensor"), P("dp", "tensor"), P("tensor")),
        check_vma=False,
    )


def shards_for(mesh):
    ndp = mesh.shape["dp"]

    def shards(teacher_master, student_weight, teacher_feat, student_feat, center):
        images_all = teacher_feat.shape[0] * ndp
        cols = center.shape[0]
        if images_all < cols and cols % ndp == 0:
            return feature_plan(teacher_master, student_weight, teacher_feat, student_feat, center)
        return weight_plan(teacher_master, student_weight, teacher_feat, student_feat, center)

    return shards
```

```python
import jax
import jax.numpy as jnp
from jax import lax
from jax.sharding import PartitionSpec as P


def unit_rows(feat):
    wide = feat.astype(jnp.float32)
    return (wide * lax.rsqrt(jnp.sum(wide * wide, 1, keepdims=True) + 1e-06)).astype(jnp.bfloat16)


def weight_plan(teacher_master, student_weight, teacher_feat, student_feat, center):
    zt = unit_rows(teacher_feat)
    zs = unit_rows(student_feat)
    images_all = teacher_feat.shape[0] * lax.axis_size("dp")
    student_full = lax.all_gather(student_weight, "dp", axis=0, tiled=True)
    master_new = 0.996 * teacher_master + 0.004 * student_weight.astype(jnp.float32)
    weight = lax.all_gather(master_new.astype(jnp.bfloat16), "dp", axis=0, tiled=True)
    raw = jnp.dot(zt, weight, preferred_element_type=jnp.float32)
    t_norm = jnp.sqrt(jnp.sum(jnp.square(weight.astype(jnp.float32)), 0) + 1e-06)
    t_cos = raw / t_norm
    s_norm = jnp.sqrt(jnp.sum(jnp.square(student_full.astype(jnp.float32)), 0) + 1e-06)
    s_cos = jnp.dot(zs, student_full, preferred_element_type=jnp.float32) / s_norm
    t_exp = jnp.exp((t_cos - center) / 0.04)
    s_exp = jnp.exp(s_cos / 0.1)
    t_total, s_total = lax.psum(
        (jnp.sum(t_exp, 1, keepdims=True), jnp.sum(s_exp, 1, keepdims=True)), "tensor"
    )
    cos_mean = lax.psum(jnp.sum(t_cos, 0), "dp") / images_all
    new_center = 0.5 * center + 0.5 * cos_mean
    dlog = ((s_exp / s_total - t_exp / t_total) / 0.1).astype(jnp.bfloat16)
    scaled = jnp.sum(dlog.astype(jnp.float32) * s_cos, 0) / s_norm
    product = lax.dot_general(
        zs, dlog, (((0,), (0,)), ((), ())), preferred_element_type=jnp.float32
    )
    student_grad = lax.psum_scatter(
        (product - student_full.astype(jnp.float32) * scaled) / s_norm,
        "dp",
        scatter_dimension=0,
        tiled=True,
    )
    return (master_new, student_grad, new_center)


def exchange_sum(x, axis, n):
    if n & (n - 1):
        return lax.psum(x, axis)
    step = 1
    while step < n:
        x = x + lax.ppermute(x, axis, [(i, i ^ step) for i in range(n)])
        step *= 2
    return x


def exchange_all(x, axis, n):
    total = x
    for k in range(1, n):
        total = total + lax.ppermute(x, axis, [(i, (i + k) % n) for i in range(n)])
    return total


def feature_plan(teacher_master, student_weight, teacher_feat, student_feat, center):
    ndp = lax.axis_size("dp")
    bot = teacher_feat.shape[1]
    images_all = teacher_feat.shape[0] * ndp
    cols = center.shape[0] // ndp
    master_new = 0.996 * teacher_master + 0.004 * student_weight.astype(jnp.float32)
    rows = teacher_master.shape[0]
    both = jnp.stack([student_weight, master_new.astype(jnp.bfloat16)])
    both = both.reshape(2, rows, ndp, cols).transpose(2, 0, 1, 3).reshape(ndp, 2 * rows, cols)
    both = lax.all_to_all(both, "dp", 0, 0, tiled=True)
    sw = both[:, :rows].reshape(ndp * rows, cols)
    tw = both[:, rows:].reshape(ndp * rows, cols)
    feats = jnp.concatenate([unit_rows(teacher_feat), unit_rows(student_feat)], axis=1)
    feats = lax.all_gather(feats, "dp", axis=0, tiled=True)
    zt, zs = feats[:, :bot], feats[:, bot:]
    c = lax.dynamic_slice_in_dim(center, lax.axis_index("dp") * cols, cols)
    t_norm = jnp.sqrt(jnp.sum(jnp.square(tw.astype(jnp.float32)), 0) + 1e-06)
    s_norm = jnp.sqrt(jnp.sum(jnp.square(sw.astype(jnp.float32)), 0) + 1e-06)
    t_cos = jnp.dot(zt, tw, preferred_element_type=jnp.float32) / t_norm
    s_cos = jnp.dot(zs, sw, preferred_element_type=jnp.float32) / s_norm
    t_exp = jnp.exp((t_cos - c) / 0.04)
    s_exp = jnp.exp(s_cos / 0.1)
    totals = jnp.stack([jnp.sum(t_exp, 1), jnp.sum(s_exp, 1)])
    totals = exchange_all(exchange_all(totals, "dp", ndp), "tensor", lax.axis_size("tensor"))
    t_total, s_total = totals[0][:, None], totals[1][:, None]
    part_center = 0.5 * c + 0.5 * (jnp.sum(t_cos, 0) / images_all)
    dlog = ((s_exp / s_total - t_exp / t_total) / 0.1).astype(jnp.bfloat16)
    scaled = jnp.sum(dlog.astype(jnp.float32) * s_cos, 0) / s_norm
    product = lax.dot_general(
        zs, dlog, (((0,), (0,)), ((), ())), preferred_element_type=jnp.float32
    )
    grad = (product - sw.astype(jnp.float32) * scaled) / s_norm
    high = part_center.astype(jnp.bfloat16)
    low = (part_center - high.astype(jnp.float32)).astype(jnp.bfloat16)
    sent = jnp.concatenate(
        [
            grad.astype(jnp.bfloat16).reshape(ndp, rows, cols),
            jnp.broadcast_to(jnp.stack([high, low]), (ndp, 2, cols)),
        ],
        axis=1,
    )
    got = lax.all_to_all(sent, "dp", 0, 2, tiled=True)
    got = got.reshape(rows + 2, ndp * cols).astype(jnp.float32)
    return (master_new, got[:rows], got[rows] + got[rows + 1])


def solution(mesh):
    placed = (P("dp", "tensor"), P("dp", "tensor"), P("dp", None), P("dp", None), P("tensor"))
    return jax.shard_map(
        shards_for(mesh),
        mesh=mesh,
        in_specs=placed,
        out_specs=(P("dp", "tensor"), P("dp", "tensor"), P("tensor")),
        check_vma=False,
    )


def shards_for(mesh):
    ndp = mesh.shape["dp"]

    def shards(teacher_master, student_weight, teacher_feat, student_feat, center):
        images_all = teacher_feat.shape[0] * ndp
        cols = center.shape[0]
        if images_all < cols and cols % ndp == 0:
            return feature_plan(teacher_master, student_weight, teacher_feat, student_feat, center)
        return weight_plan(teacher_master, student_weight, teacher_feat, student_feat, center)

    return shards
```

```python
import jax
import jax.numpy as jnp
from jax import lax
from jax.sharding import PartitionSpec as P


def unit_rows(feat):
    wide = feat.astype(jnp.float32)
    return (wide * lax.rsqrt(jnp.sum(wide * wide, 1, keepdims=True) + 1e-06)).astype(jnp.bfloat16)


def weight_plan(teacher_master, student_weight, teacher_feat, student_feat, center):
    zt = unit_rows(teacher_feat)
    zs = unit_rows(student_feat)
    images_all = teacher_feat.shape[0] * lax.axis_size("dp")
    student_full = lax.all_gather(student_weight, "dp", axis=0, tiled=True)
    master_new = 0.996 * teacher_master + 0.004 * student_weight.astype(jnp.float32)
    weight = lax.all_gather(master_new.astype(jnp.bfloat16), "dp", axis=0, tiled=True)
    raw = jnp.dot(zt, weight, preferred_element_type=jnp.float32)
    t_norm = jnp.sqrt(jnp.sum(jnp.square(weight.astype(jnp.float32)), 0) + 1e-06)
    t_cos = raw / t_norm
    s_norm = jnp.sqrt(jnp.sum(jnp.square(student_full.astype(jnp.float32)), 0) + 1e-06)
    s_cos = jnp.dot(zs, student_full, preferred_element_type=jnp.float32) / s_norm
    t_exp = jnp.exp((t_cos - center) / 0.04)
    s_exp = jnp.exp(s_cos / 0.1)
    t_total, s_total = lax.psum(
        (jnp.sum(t_exp, 1, keepdims=True), jnp.sum(s_exp, 1, keepdims=True)), "tensor"
    )
    cos_mean = lax.psum(jnp.sum(t_cos, 0), "dp") / images_all
    new_center = 0.5 * center + 0.5 * cos_mean
    dlog = ((s_exp / s_total - t_exp / t_total) / 0.1).astype(jnp.bfloat16)
    scaled = jnp.sum(dlog.astype(jnp.float32) * s_cos, 0) / s_norm
    product = lax.dot_general(
        zs, dlog, (((0,), (0,)), ((), ())), preferred_element_type=jnp.float32
    )
    student_grad = lax.psum_scatter(
        (product - student_full.astype(jnp.float32) * scaled) / s_norm,
        "dp",
        scatter_dimension=0,
        tiled=True,
    )
    return (master_new, student_grad, new_center)


def exchange_sum(x, axis, n):
    if n & (n - 1):
        return lax.psum(x, axis)
    step = 1
    while step < n:
        x = x + lax.ppermute(x, axis, [(i, i ^ step) for i in range(n)])
        step *= 2
    return x


def exchange_all(x, axis, n):
    total = x
    for k in range(1, n):
        total = total + lax.ppermute(x, axis, [(i, (i + k) % n) for i in range(n)])
    return total


def feature_plan(teacher_master, student_weight, teacher_feat, student_feat, center):
    ndp = lax.axis_size("dp")
    bot = teacher_feat.shape[1]
    images_all = teacher_feat.shape[0] * ndp
    cols = center.shape[0] // ndp
    master_new = 0.996 * teacher_master + 0.004 * student_weight.astype(jnp.float32)
    rows = teacher_master.shape[0]
    both = jnp.stack([student_weight, master_new.astype(jnp.bfloat16)])
    both = both.reshape(2, rows, ndp, cols).transpose(2, 0, 1, 3).reshape(ndp, 2 * rows, cols)
    both = lax.all_to_all(both, "dp", 0, 0, tiled=True)
    sw = both[:, :rows].reshape(ndp * rows, cols)
    tw = both[:, rows:].reshape(ndp * rows, cols)
    feats = jnp.concatenate([unit_rows(teacher_feat), unit_rows(student_feat)], axis=1)
    groups = [[2 * t + core for t in range(ndp // 2)] for core in range(2)]
    half = lax.all_gather(feats, "dp", axis=0, tiled=True, axis_index_groups=groups)
    feats = jnp.concatenate([half, lax.ppermute(half, "dp", [(i, i ^ 1) for i in range(ndp)])])
    zt, zs = feats[:, :bot], feats[:, bot:]
    c = lax.dynamic_slice_in_dim(center, lax.axis_index("dp") * cols, cols)
    t_norm = jnp.sqrt(jnp.sum(jnp.square(tw.astype(jnp.float32)), 0) + 1e-06)
    s_norm = jnp.sqrt(jnp.sum(jnp.square(sw.astype(jnp.float32)), 0) + 1e-06)
    t_cos = jnp.dot(zt, tw, preferred_element_type=jnp.float32) / t_norm
    s_cos = jnp.dot(zs, sw, preferred_element_type=jnp.float32) / s_norm
    t_exp = jnp.exp((t_cos - c) / 0.04)
    s_exp = jnp.exp(s_cos / 0.1)
    totals = jnp.stack([jnp.sum(t_exp, 1), jnp.sum(s_exp, 1)])
    summed = totals
    for k in range(1, ndp):
        got = lax.ppermute(totals, "dp", [(i, i ^ k) for i in range(ndp)])
        if k % 2:
            got = got.reshape(2, 2, -1)[:, ::-1].reshape(totals.shape)
        summed = summed + got
    totals = exchange_all(summed, "tensor", lax.axis_size("tensor"))
    t_total, s_total = totals[0][:, None], totals[1][:, None]
    part_center = 0.5 * c + 0.5 * (jnp.sum(t_cos, 0) / images_all)
    dlog = ((s_exp / s_total - t_exp / t_total) / 0.1).astype(jnp.bfloat16)
    scaled = jnp.sum(dlog.astype(jnp.float32) * s_cos, 0) / s_norm
    product = lax.dot_general(
        zs, dlog, (((0,), (0,)), ((), ())), preferred_element_type=jnp.float32
    )
    grad = (product - sw.astype(jnp.float32) * scaled) / s_norm
    high = part_center.astype(jnp.bfloat16)
    low = (part_center - high.astype(jnp.float32)).astype(jnp.bfloat16)
    sent = jnp.concatenate(
        [
            grad.astype(jnp.bfloat16).reshape(ndp, rows, cols),
            jnp.broadcast_to(jnp.stack([high, low]), (ndp, 2, cols)),
        ],
        axis=1,
    )
    got = lax.all_to_all(sent, "dp", 0, 2, tiled=True)
    got = got.reshape(rows + 2, ndp * cols).astype(jnp.float32)
    return (master_new, got[:rows], got[rows] + got[rows + 1])


def solution(mesh):
    placed = (P("dp", "tensor"), P("dp", "tensor"), P("dp", None), P("dp", None), P("tensor"))
    return jax.shard_map(
        shards_for(mesh),
        mesh=mesh,
        in_specs=placed,
        out_specs=(P("dp", "tensor"), P("dp", "tensor"), P("tensor")),
        check_vma=False,
    )


def shards_for(mesh):
    ndp = mesh.shape["dp"]

    def shards(teacher_master, student_weight, teacher_feat, student_feat, center):
        images_all = teacher_feat.shape[0] * ndp
        cols = center.shape[0]
        if images_all < cols and cols % ndp == 0 and ndp > 1 and ndp & (ndp - 1) == 0:
            return feature_plan(teacher_master, student_weight, teacher_feat, student_feat, center)
        return weight_plan(teacher_master, student_weight, teacher_feat, student_feat, center)

    return shards
```

```python
import jax
import jax.numpy as jnp
from jax import lax
from jax.sharding import PartitionSpec as P


def unit_rows(feat):
    wide = feat.astype(jnp.float32)
    return (wide * lax.rsqrt(jnp.sum(wide * wide, 1, keepdims=True) + 1e-06)).astype(jnp.bfloat16)


def weight_plan(teacher_master, student_weight, teacher_feat, student_feat, center):
    zt = unit_rows(teacher_feat)
    zs = unit_rows(student_feat)
    images_all = teacher_feat.shape[0] * lax.axis_size("dp")
    student_full = lax.all_gather(student_weight, "dp", axis=0, tiled=True)
    master_new = 0.996 * teacher_master + 0.004 * student_weight.astype(jnp.float32)
    weight = lax.all_gather(master_new.astype(jnp.bfloat16), "dp", axis=0, tiled=True)
    raw = jnp.dot(zt, weight, preferred_element_type=jnp.float32)
    t_norm = jnp.sqrt(jnp.sum(jnp.square(weight.astype(jnp.float32)), 0) + 1e-06)
    t_cos = raw / t_norm
    s_norm = jnp.sqrt(jnp.sum(jnp.square(student_full.astype(jnp.float32)), 0) + 1e-06)
    s_cos = jnp.dot(zs, student_full, preferred_element_type=jnp.float32) / s_norm
    t_exp = jnp.exp((t_cos - center) / 0.04)
    s_exp = jnp.exp(s_cos / 0.1)
    t_total, s_total = lax.psum(
        (jnp.sum(t_exp, 1, keepdims=True), jnp.sum(s_exp, 1, keepdims=True)), "tensor"
    )
    cos_mean = lax.psum(jnp.sum(t_cos, 0), "dp") / images_all
    new_center = 0.5 * center + 0.5 * cos_mean
    dlog = ((s_exp / s_total - t_exp / t_total) / 0.1).astype(jnp.bfloat16)
    scaled = jnp.sum(dlog.astype(jnp.float32) * s_cos, 0) / s_norm
    product = lax.dot_general(
        zs, dlog, (((0,), (0,)), ((), ())), preferred_element_type=jnp.float32
    )
    student_grad = lax.psum_scatter(
        (product - student_full.astype(jnp.float32) * scaled) / s_norm,
        "dp",
        scatter_dimension=0,
        tiled=True,
    )
    return (master_new, student_grad, new_center)


def exchange_sum(x, axis, n):
    if n & (n - 1):
        return lax.psum(x, axis)
    step = 1
    while step < n:
        x = x + lax.ppermute(x, axis, [(i, i ^ step) for i in range(n)])
        step *= 2
    return x


def exchange_all(x, axis, n):
    total = x
    for k in range(1, n):
        total = total + lax.ppermute(x, axis, [(i, (i + k) % n) for i in range(n)])
    return total


def feature_plan(teacher_master, student_weight, teacher_feat, student_feat, center):
    n = lax.axis_size("dp")
    me = lax.axis_index("dp")
    rows, width = teacher_master.shape
    bot = teacher_feat.shape[1]
    images = teacher_feat.shape[0]
    cols = width // n
    nbits = n.bit_length() - 1
    master_new = 0.996 * teacher_master + 0.004 * student_weight.astype(jnp.float32)
    both = jnp.stack([student_weight, master_new.astype(jnp.bfloat16)])
    both = both.reshape(2, rows, n, cols).transpose(2, 0, 1, 3).reshape(n, 2 * rows, cols)
    order = me ^ jnp.arange(n)
    held = jnp.take(both, order, axis=0).reshape((2,) * nbits + (2 * rows, cols))
    feats = jnp.concatenate([unit_rows(teacher_feat), unit_rows(student_feat)], axis=1)
    bits = list(range(1, nbits)) + [0]
    for b in bits:
        dim = nbits - 1 - b
        keep = lax.index_in_dim(held, 0, dim, keepdims=False)
        away = lax.index_in_dim(held, 1, dim, keepdims=False)
        flat_feats = feats.reshape(-1, 2 * bot)
        pairs = [(i, i ^ (1 << b)) for i in range(n)]
        if 2 * bot == cols:
            payload = jnp.concatenate([flat_feats, away.reshape(-1, cols)], axis=0)
            got = lax.ppermute(payload, "dp", pairs)
            got_feats = got[: flat_feats.shape[0]].reshape(feats.shape)
            got_held = got[flat_feats.shape[0]:].reshape(away.shape)
        else:
            got_feats, got_held = lax.ppermute((feats, away), "dp", pairs)
        feats = jnp.stack([feats, got_feats])
        held = jnp.stack([keep, got_held], axis=dim)
    feats = feats.reshape(-1, 2 * bot)
    held = jnp.take(held.reshape(n, 2 * rows, cols), order, axis=0)
    sw = held[:, :rows].reshape(n * rows, cols)
    tw = held[:, rows:].reshape(n * rows, cols)
    zt, zs = feats[:, :bot], feats[:, bot:]
    c = lax.dynamic_slice_in_dim(center, me * cols, cols)
    t_norm = jnp.sqrt(jnp.sum(jnp.square(tw.astype(jnp.float32)), 0) + 1e-06)
    s_norm = jnp.sqrt(jnp.sum(jnp.square(sw.astype(jnp.float32)), 0) + 1e-06)
    t_cos = jnp.dot(zt, tw, preferred_element_type=jnp.float32) / t_norm
    s_cos = jnp.dot(zs, sw, preferred_element_type=jnp.float32) / s_norm
    t_exp = jnp.exp((t_cos - c) / 0.04)
    s_exp = jnp.exp(s_cos / 0.1)
    totals = jnp.stack([jnp.sum(t_exp, 1), jnp.sum(s_exp, 1)])
    round_dims = {b: nbits - 1 - pos for pos, b in enumerate(bits)}
    for b in bits:
        got = lax.ppermute(totals, "dp", [(i, i ^ (1 << b)) for i in range(n)])
        got = jnp.flip(got.reshape((2,) + (2,) * nbits + (images,)), 1 + round_dims[b])
        totals = totals + got.reshape(totals.shape)
    totals = exchange_all(totals, "tensor", lax.axis_size("tensor"))
    t_total, s_total = totals[0][:, None], totals[1][:, None]
    part_center = 0.5 * c + 0.5 * (jnp.sum(t_cos, 0) / (images * n))
    dlog = ((s_exp / s_total - t_exp / t_total) / 0.1).astype(jnp.bfloat16)
    scaled = jnp.sum(dlog.astype(jnp.float32) * s_cos, 0) / s_norm
    product = lax.dot_general(
        zs, dlog, (((0,), (0,)), ((), ())), preferred_element_type=jnp.float32
    )
    grad = (product - sw.astype(jnp.float32) * scaled) / s_norm
    high = part_center.astype(jnp.bfloat16)
    low = (part_center - high.astype(jnp.float32)).astype(jnp.bfloat16)
    sent = jnp.concatenate(
        [
            grad.astype(jnp.bfloat16).reshape(n, rows, cols),
            jnp.broadcast_to(jnp.stack([high, low]), (n, 2, cols)),
        ],
        axis=1,
    )
    got = lax.all_to_all(sent, "dp", 0, 2, tiled=True)
    got = got.reshape(rows + 2, n * cols).astype(jnp.float32)
    return (master_new, got[:rows], got[rows] + got[rows + 1])


def solution(mesh):
    placed = (P("dp", "tensor"), P("dp", "tensor"), P("dp", None), P("dp", None), P("tensor"))
    return jax.shard_map(
        shards_for(mesh),
        mesh=mesh,
        in_specs=placed,
        out_specs=(P("dp", "tensor"), P("dp", "tensor"), P("tensor")),
        check_vma=False,
    )


def shards_for(mesh):
    ndp = mesh.shape["dp"]

    def shards(teacher_master, student_weight, teacher_feat, student_feat, center):
        images_all = teacher_feat.shape[0] * ndp
        cols = center.shape[0]
        if images_all < cols and cols % ndp == 0 and ndp > 1 and ndp & (ndp - 1) == 0:
            return feature_plan(teacher_master, student_weight, teacher_feat, student_feat, center)
        return weight_plan(teacher_master, student_weight, teacher_feat, student_feat, center)

    return shards
```

```python
import jax
import jax.numpy as jnp
from jax import lax
from jax.sharding import PartitionSpec as P


def unit_rows(feat):
    wide = feat.astype(jnp.float32)
    return (wide * lax.rsqrt(jnp.sum(wide * wide, 1, keepdims=True) + 1e-06)).astype(jnp.bfloat16)


def weight_plan(teacher_master, student_weight, teacher_feat, student_feat, center):
    zt = unit_rows(teacher_feat)
    zs = unit_rows(student_feat)
    images_all = teacher_feat.shape[0] * lax.axis_size("dp")
    student_full = lax.all_gather(student_weight, "dp", axis=0, tiled=True)
    master_new = 0.996 * teacher_master + 0.004 * student_weight.astype(jnp.float32)
    weight = lax.all_gather(master_new.astype(jnp.bfloat16), "dp", axis=0, tiled=True)
    raw = jnp.dot(zt, weight, preferred_element_type=jnp.float32)
    t_norm = jnp.sqrt(jnp.sum(jnp.square(weight.astype(jnp.float32)), 0) + 1e-06)
    t_cos = raw / t_norm
    s_norm = jnp.sqrt(jnp.sum(jnp.square(student_full.astype(jnp.float32)), 0) + 1e-06)
    s_cos = jnp.dot(zs, student_full, preferred_element_type=jnp.float32) / s_norm
    t_exp = jnp.exp((t_cos - center) / 0.04)
    s_exp = jnp.exp(s_cos / 0.1)
    t_total, s_total = lax.psum(
        (jnp.sum(t_exp, 1, keepdims=True), jnp.sum(s_exp, 1, keepdims=True)), "tensor"
    )
    cos_mean = lax.psum(jnp.sum(t_cos, 0), "dp") / images_all
    new_center = 0.5 * center + 0.5 * cos_mean
    dlog = ((s_exp / s_total - t_exp / t_total) / 0.1).astype(jnp.bfloat16)
    scaled = jnp.sum(dlog.astype(jnp.float32) * s_cos, 0) / s_norm
    product = lax.dot_general(
        zs, dlog, (((0,), (0,)), ((), ())), preferred_element_type=jnp.float32
    )
    student_grad = lax.psum_scatter(
        (product - student_full.astype(jnp.float32) * scaled) / s_norm,
        "dp",
        scatter_dimension=0,
        tiled=True,
    )
    return (master_new, student_grad, new_center)


def exchange_sum(x, axis, n):
    if n & (n - 1):
        return lax.psum(x, axis)
    step = 1
    while step < n:
        x = x + lax.ppermute(x, axis, [(i, i ^ step) for i in range(n)])
        step *= 2
    return x


def exchange_all(x, axis, n):
    total = x
    for k in range(1, n):
        total = total + lax.ppermute(x, axis, [(i, (i + k) % n) for i in range(n)])
    return total


def feature_plan(teacher_master, student_weight, teacher_feat, student_feat, center):
    n = lax.axis_size("dp")
    me = lax.axis_index("dp")
    rows, width = teacher_master.shape
    bot = teacher_feat.shape[1]
    images = teacher_feat.shape[0]
    cols = width // n
    nbits = n.bit_length() - 1
    odd = me % 2
    up = list(range(1, nbits))
    down = up[::-1]
    dim_bits = [jnp.where(odd == 1, down[r], up[r]) for r in range(nbits - 1)][::-1]
    master_new = 0.996 * teacher_master + 0.004 * student_weight.astype(jnp.float32)
    both = jnp.stack([student_weight, master_new.astype(jnp.bfloat16)])
    both = both.reshape(2, rows, n, cols).transpose(2, 0, 1, 3).reshape(n, 2 * rows, cols)
    pos = jnp.arange(n)
    rel = (pos >> (nbits - 1)) & 1
    for d, bit in enumerate(dim_bits):
        rel = rel | (((pos >> (nbits - 2 - d)) & 1) << bit)
    held = jnp.take(both, me ^ rel, axis=0).reshape((2,) * nbits + (2 * rows, cols))
    feats = jnp.concatenate([unit_rows(teacher_feat), unit_rows(student_feat)], axis=1)
    cross_rev = list(range(nbits - 2, -1, -1))

    def swap(pairs_up, pairs_down):
        return [(i, i ^ (1 << (pairs_down if i % 2 else pairs_up))) for i in range(n)]

    for r in range(nbits):
        last = r == nbits - 1
        dim = 0 if last else nbits - 1 - r
        keep = lax.index_in_dim(held, 0, dim, keepdims=False)
        away = lax.index_in_dim(held, 1, dim, keepdims=False)
        if last:
            pairs = [(i, i ^ 1) for i in range(n)]
        else:
            pairs = swap(up[r], down[r])
        if 2 * bot == cols:
            flat_feats = feats.reshape(-1, 2 * bot)
            payload = jnp.concatenate([flat_feats, away.reshape(-1, cols)], axis=0)
            got = lax.ppermute(payload, "dp", pairs)
            got_feats = got[: flat_feats.shape[0]].reshape(feats.shape)
            got_held = got[flat_feats.shape[0]:].reshape(away.shape)
        else:
            got_feats, got_held = lax.ppermute((feats, away), "dp", pairs)
        if last:
            got_feats = jnp.transpose(got_feats, cross_rev + [nbits - 1, nbits])
            got_held = jnp.transpose(got_held, cross_rev + [nbits - 1, nbits])
        feats = jnp.stack([feats, got_feats])
        held = jnp.stack([keep, got_held], axis=dim)
    feats = feats.reshape(-1, 2 * bot)
    src = me ^ pos
    where = src & 1
    for d, bit in enumerate(dim_bits):
        where = (where << 1) | ((src >> bit) & 1)
    held = jnp.take(held.reshape(n, 2 * rows, cols), where, axis=0)
    sw = held[:, :rows].reshape(n * rows, cols)
    tw = held[:, rows:].reshape(n * rows, cols)
    zt, zs = feats[:, :bot], feats[:, bot:]
    c = lax.dynamic_slice_in_dim(center, me * cols, cols)
    t_norm = jnp.sqrt(jnp.sum(jnp.square(tw.astype(jnp.float32)), 0) + 1e-06)
    s_norm = jnp.sqrt(jnp.sum(jnp.square(sw.astype(jnp.float32)), 0) + 1e-06)
    t_cos = jnp.dot(zt, tw, preferred_element_type=jnp.float32) / t_norm
    s_cos = jnp.dot(zs, sw, preferred_element_type=jnp.float32) / s_norm
    t_exp = jnp.exp((t_cos - c) / 0.04)
    s_exp = jnp.exp(s_cos / 0.1)
    totals = jnp.stack([jnp.sum(t_exp, 1), jnp.sum(s_exp, 1)])
    shape = (2,) + (2,) * nbits + (images,)
    for r in range(nbits):
        if r == nbits - 1:
            got = lax.ppermute(totals, "dp", [(i, i ^ 1) for i in range(n)]).reshape(shape)
            got = jnp.flip(jnp.transpose(got, [0, 1] + [2 + d for d in cross_rev] + [nbits + 1]), 1)
        else:
            got = lax.ppermute(totals, "dp", swap(up[r], down[r])).reshape(shape)
            got = jnp.flip(got, nbits - r)
        totals = totals + got.reshape(totals.shape)
    totals = exchange_all(totals, "tensor", lax.axis_size("tensor"))
    t_total, s_total = totals[0][:, None], totals[1][:, None]
    part_center = 0.5 * c + 0.5 * (jnp.sum(t_cos, 0) / (images * n))
    dlog = ((s_exp / s_total - t_exp / t_total) / 0.1).astype(jnp.bfloat16)
    scaled = jnp.sum(dlog.astype(jnp.float32) * s_cos, 0) / s_norm
    product = lax.dot_general(
        zs, dlog, (((0,), (0,)), ((), ())), preferred_element_type=jnp.float32
    )
    grad = (product - sw.astype(jnp.float32) * scaled) / s_norm
    high = part_center.astype(jnp.bfloat16)
    low = (part_center - high.astype(jnp.float32)).astype(jnp.bfloat16)
    sent = jnp.concatenate(
        [
            grad.astype(jnp.bfloat16).reshape(n, rows, cols),
            jnp.broadcast_to(jnp.stack([high, low]), (n, 2, cols)),
        ],
        axis=1,
    )
    got = lax.all_to_all(sent, "dp", 0, 2, tiled=True)
    got = got.reshape(rows + 2, n * cols).astype(jnp.float32)
    return (master_new, got[:rows], got[rows] + got[rows + 1])


def solution(mesh):
    placed = (P("dp", "tensor"), P("dp", "tensor"), P("dp", None), P("dp", None), P("tensor"))
    return jax.shard_map(
        shards_for(mesh),
        mesh=mesh,
        in_specs=placed,
        out_specs=(P("dp", "tensor"), P("dp", "tensor"), P("tensor")),
        check_vma=False,
    )


def shards_for(mesh):
    ndp = mesh.shape["dp"]

    def shards(teacher_master, student_weight, teacher_feat, student_feat, center):
        images_all = teacher_feat.shape[0] * ndp
        cols = center.shape[0]
        if images_all < cols and cols % ndp == 0 and ndp > 1 and ndp & (ndp - 1) == 0:
            return feature_plan(teacher_master, student_weight, teacher_feat, student_feat, center)
        return weight_plan(teacher_master, student_weight, teacher_feat, student_feat, center)

    return shards
```

```python
import jax
import jax.numpy as jnp
from jax import lax
from jax.sharding import PartitionSpec as P


def unit_rows(feat):
    wide = feat.astype(jnp.float32)
    return (wide * lax.rsqrt(jnp.sum(wide * wide, 1, keepdims=True) + 1e-06)).astype(jnp.bfloat16)


def weight_plan(teacher_master, student_weight, teacher_feat, student_feat, center):
    zt = unit_rows(teacher_feat)
    zs = unit_rows(student_feat)
    images_all = teacher_feat.shape[0] * lax.axis_size("dp")
    student_full = lax.all_gather(student_weight, "dp", axis=0, tiled=True)
    master_new = 0.996 * teacher_master + 0.004 * student_weight.astype(jnp.float32)
    weight = lax.all_gather(master_new.astype(jnp.bfloat16), "dp", axis=0, tiled=True)
    raw = jnp.dot(zt, weight, preferred_element_type=jnp.float32)
    t_norm = jnp.sqrt(jnp.sum(jnp.square(weight.astype(jnp.float32)), 0) + 1e-06)
    t_cos = raw / t_norm
    s_norm = jnp.sqrt(jnp.sum(jnp.square(student_full.astype(jnp.float32)), 0) + 1e-06)
    s_cos = jnp.dot(zs, student_full, preferred_element_type=jnp.float32) / s_norm
    t_exp = jnp.exp((t_cos - center) / 0.04)
    s_exp = jnp.exp(s_cos / 0.1)
    t_total, s_total = lax.psum(
        (jnp.sum(t_exp, 1, keepdims=True), jnp.sum(s_exp, 1, keepdims=True)), "tensor"
    )
    cos_mean = lax.psum(jnp.sum(t_cos, 0), "dp") / images_all
    new_center = 0.5 * center + 0.5 * cos_mean
    dlog = ((s_exp / s_total - t_exp / t_total) / 0.1).astype(jnp.bfloat16)
    scaled = jnp.sum(dlog.astype(jnp.float32) * s_cos, 0) / s_norm
    product = lax.dot_general(
        zs, dlog, (((0,), (0,)), ((), ())), preferred_element_type=jnp.float32
    )
    student_grad = lax.psum_scatter(
        (product - student_full.astype(jnp.float32) * scaled) / s_norm,
        "dp",
        scatter_dimension=0,
        tiled=True,
    )
    return (master_new, student_grad, new_center)


def exchange_sum(x, axis, n):
    if n & (n - 1):
        return lax.psum(x, axis)
    step = 1
    while step < n:
        x = x + lax.ppermute(x, axis, [(i, i ^ step) for i in range(n)])
        step *= 2
    return x


def exchange_all(x, axis, n):
    total = x
    for k in range(1, n):
        total = total + lax.ppermute(x, axis, [(i, (i + k) % n) for i in range(n)])
    return total


def feature_plan(teacher_master, student_weight, teacher_feat, student_feat, center):
    n = lax.axis_size("dp")
    me = lax.axis_index("dp")
    rows, width = teacher_master.shape
    bot = teacher_feat.shape[1]
    images = teacher_feat.shape[0]
    cols = width // n
    nbits = n.bit_length() - 1
    odd = me % 2
    up = list(range(1, nbits))
    down = up[::-1]
    dim_bits = [jnp.where(odd == 1, down[r], up[r]) for r in range(nbits - 1)][::-1]
    master_new = 0.996 * teacher_master + 0.004 * student_weight.astype(jnp.float32)
    both = jnp.stack([student_weight, master_new.astype(jnp.bfloat16)])
    both = both.reshape(2, rows, n, cols).transpose(2, 0, 1, 3).reshape(n, 2 * rows, cols)
    pos = jnp.arange(n)
    rel = (pos >> (nbits - 1)) & 1
    for d, bit in enumerate(dim_bits):
        rel = rel | (((pos >> (nbits - 2 - d)) & 1) << bit)
    held = jnp.take(both, me ^ rel, axis=0).reshape((2,) * nbits + (2 * rows, cols))
    feats = jnp.concatenate([unit_rows(teacher_feat), unit_rows(student_feat)], axis=1)
    cross_rev = list(range(nbits - 2, -1, -1))

    def swap(pairs_up, pairs_down):
        return [(i, i ^ (1 << (pairs_down if i % 2 else pairs_up))) for i in range(n)]

    for r in range(nbits):
        last = r == nbits - 1
        dim = 0 if last else nbits - 1 - r
        keep = lax.index_in_dim(held, 0, dim, keepdims=False)
        away = lax.index_in_dim(held, 1, dim, keepdims=False)
        if last:
            pairs = [(i, i ^ 1) for i in range(n)]
        else:
            pairs = swap(up[r], down[r])
        if 2 * bot == cols:
            flat_feats = feats.reshape(-1, 2 * bot)
            payload = jnp.concatenate([flat_feats, away.reshape(-1, cols)], axis=0)
            got = lax.ppermute(payload, "dp", pairs)
            got_feats = got[: flat_feats.shape[0]].reshape(feats.shape)
            got_held = got[flat_feats.shape[0]:].reshape(away.shape)
        else:
            got_feats, got_held = lax.ppermute((feats, away), "dp", pairs)
        if last:
            got_feats = jnp.transpose(got_feats, cross_rev + [nbits - 1, nbits])
            got_held = jnp.transpose(got_held, cross_rev + [nbits - 1, nbits])
        feats = jnp.stack([feats, got_feats])
        held = jnp.stack([keep, got_held], axis=dim)
    feats = feats.reshape(-1, 2 * bot)
    src = me ^ pos
    where = src & 1
    for d, bit in enumerate(dim_bits):
        where = (where << 1) | ((src >> bit) & 1)
    held = jnp.take(held.reshape(n, 2 * rows, cols), where, axis=0)
    sw = held[:, :rows].reshape(n * rows, cols)
    tw = held[:, rows:].reshape(n * rows, cols)
    zt, zs = feats[:, :bot], feats[:, bot:]
    c = lax.dynamic_slice_in_dim(center, me * cols, cols)
    t_norm = jnp.sqrt(jnp.sum(jnp.square(tw.astype(jnp.float32)), 0) + 1e-06)
    s_norm = jnp.sqrt(jnp.sum(jnp.square(sw.astype(jnp.float32)), 0) + 1e-06)
    t_cos = jnp.dot(zt, tw, preferred_element_type=jnp.float32) / t_norm
    s_cos = jnp.dot(zs, sw, preferred_element_type=jnp.float32) / s_norm
    t_exp = jnp.exp((t_cos - c) / 0.04)
    s_exp = jnp.exp(s_cos / 0.1)
    totals = jnp.stack([jnp.sum(t_exp, 1), jnp.sum(s_exp, 1)])
    shape = (2,) + (2,) * nbits + (images,)
    for r in range(nbits):
        if r == nbits - 1:
            got = lax.ppermute(totals, "dp", [(i, i ^ 1) for i in range(n)]).reshape(shape)
            got = jnp.flip(jnp.transpose(got, [0, 1] + [2 + d for d in cross_rev] + [nbits + 1]), 1)
        else:
            got = lax.ppermute(totals, "dp", swap(up[r], down[r])).reshape(shape)
            got = jnp.flip(got, nbits - r)
        totals = totals + got.reshape(totals.shape)
    totals = exchange_all(totals, "tensor", lax.axis_size("tensor"))
    t_total, s_total = totals[0][:, None], totals[1][:, None]
    part_center = 0.5 * c + 0.5 * (jnp.sum(t_cos, 0) / (images * n))
    dlog = ((s_exp / s_total - t_exp / t_total) / 0.1).astype(jnp.bfloat16)
    product = lax.dot_general(
        zs, dlog, (((0,), (0,)), ((), ())), preferred_element_type=jnp.float32
    )
    wide = sw.astype(jnp.float32)
    scaled = jnp.sum(wide * product, 0) / s_norm / s_norm
    grad = (product - wide * scaled) / s_norm
    high = part_center.astype(jnp.bfloat16)
    low = (part_center - high.astype(jnp.float32)).astype(jnp.bfloat16)
    sent = jnp.concatenate(
        [
            grad.astype(jnp.bfloat16).reshape(n, rows, cols),
            jnp.broadcast_to(jnp.stack([high, low]), (n, 2, cols)),
        ],
        axis=1,
    )
    got = lax.all_to_all(sent, "dp", 0, 2, tiled=True)
    got = got.reshape(rows + 2, n * cols).astype(jnp.float32)
    return (master_new, got[:rows], got[rows] + got[rows + 1])


def solution(mesh):
    placed = (P("dp", "tensor"), P("dp", "tensor"), P("dp", None), P("dp", None), P("tensor"))
    return jax.shard_map(
        shards_for(mesh),
        mesh=mesh,
        in_specs=placed,
        out_specs=(P("dp", "tensor"), P("dp", "tensor"), P("tensor")),
        check_vma=False,
    )


def shards_for(mesh):
    ndp = mesh.shape["dp"]

    def shards(teacher_master, student_weight, teacher_feat, student_feat, center):
        images_all = teacher_feat.shape[0] * ndp
        cols = center.shape[0]
        if images_all < cols and cols % ndp == 0 and ndp > 1 and ndp & (ndp - 1) == 0:
            return feature_plan(teacher_master, student_weight, teacher_feat, student_feat, center)
        return weight_plan(teacher_master, student_weight, teacher_feat, student_feat, center)

    return shards
```

```python
import jax
import jax.numpy as jnp
from jax import lax
from jax.sharding import PartitionSpec as P


def unit_rows(feat):
    wide = feat.astype(jnp.float32)
    return (wide * lax.rsqrt(jnp.sum(wide * wide, 1, keepdims=True) + 1e-06)).astype(jnp.bfloat16)


def weight_plan(teacher_master, student_weight, teacher_feat, student_feat, center):
    zt = unit_rows(teacher_feat)
    zs = unit_rows(student_feat)
    images_all = teacher_feat.shape[0] * lax.axis_size("dp")
    student_full = lax.all_gather(student_weight, "dp", axis=0, tiled=True)
    master_new = 0.996 * teacher_master + 0.004 * student_weight.astype(jnp.float32)
    weight = lax.all_gather(master_new.astype(jnp.bfloat16), "dp", axis=0, tiled=True)
    raw = jnp.dot(zt, weight, preferred_element_type=jnp.float32)
    t_norm = jnp.sqrt(jnp.sum(jnp.square(weight.astype(jnp.float32)), 0) + 1e-06)
    t_cos = raw / t_norm
    s_norm = jnp.sqrt(jnp.sum(jnp.square(student_full.astype(jnp.float32)), 0) + 1e-06)
    s_cos = jnp.dot(zs, student_full, preferred_element_type=jnp.float32) / s_norm
    t_exp = jnp.exp((t_cos - center) / 0.04)
    s_exp = jnp.exp(s_cos / 0.1)
    t_total, s_total = lax.psum(
        (jnp.sum(t_exp, 1, keepdims=True), jnp.sum(s_exp, 1, keepdims=True)), "tensor"
    )
    cos_mean = lax.psum(jnp.sum(t_cos, 0), "dp") / images_all
    new_center = 0.5 * center + 0.5 * cos_mean
    dlog = ((s_exp / s_total - t_exp / t_total) / 0.1).astype(jnp.bfloat16)
    scaled = jnp.sum(dlog.astype(jnp.float32) * s_cos, 0) / s_norm
    product = lax.dot_general(
        zs, dlog, (((0,), (0,)), ((), ())), preferred_element_type=jnp.float32
    )
    student_grad = lax.psum_scatter(
        (product - student_full.astype(jnp.float32) * scaled) / s_norm,
        "dp",
        scatter_dimension=0,
        tiled=True,
    )
    return (master_new, student_grad, new_center)


def exchange_sum(x, axis, n):
    if n & (n - 1):
        return lax.psum(x, axis)
    step = 1
    while step < n:
        x = x + lax.ppermute(x, axis, [(i, i ^ step) for i in range(n)])
        step *= 2
    return x


def exchange_all(x, axis, n):
    total = x
    for k in range(1, n):
        total = total + lax.ppermute(x, axis, [(i, (i + k) % n) for i in range(n)])
    return total


def feature_plan(teacher_master, student_weight, teacher_feat, student_feat, center):
    n = lax.axis_size("dp")
    me = lax.axis_index("dp")
    rows, width = teacher_master.shape
    bot = teacher_feat.shape[1]
    images = teacher_feat.shape[0]
    cols = width // n
    nbits = n.bit_length() - 1
    odd = me % 2
    up = list(range(1, nbits))
    down = up[::-1]
    dim_bits = [jnp.where(odd == 1, down[r], up[r]) for r in range(nbits - 1)][::-1]
    master_new = 0.996 * teacher_master + 0.004 * student_weight.astype(jnp.float32)
    both = jnp.stack([student_weight, master_new.astype(jnp.bfloat16)])
    both = both.reshape(2, rows, n, cols).transpose(2, 0, 1, 3).reshape(n, 2 * rows, cols)
    pos = jnp.arange(n)
    rel = (pos >> (nbits - 1)) & 1
    for d, bit in enumerate(dim_bits):
        rel = rel | (((pos >> (nbits - 2 - d)) & 1) << bit)
    held = jnp.take(both, me ^ rel, axis=0).reshape((2,) * nbits + (2 * rows, cols))
    feats = jnp.concatenate([unit_rows(teacher_feat), unit_rows(student_feat)], axis=1)
    cross_rev = list(range(nbits - 2, -1, -1))

    def swap(pairs_up, pairs_down):
        return [(i, i ^ (1 << (pairs_down if i % 2 else pairs_up))) for i in range(n)]

    for r in range(nbits):
        last = r == nbits - 1
        dim = 0 if last else nbits - 1 - r
        keep = lax.index_in_dim(held, 0, dim, keepdims=False)
        away = lax.index_in_dim(held, 1, dim, keepdims=False)
        if last:
            pairs = [(i, i ^ 1) for i in range(n)]
        else:
            pairs = swap(up[r], down[r])
        if 2 * bot == cols:
            flat_feats = feats.reshape(-1, 2 * bot)
            payload = jnp.concatenate([flat_feats, away.reshape(-1, cols)], axis=0)
            if last:
                got = lax.ppermute(payload, "dp", pairs)
            else:
                cut = payload.shape[0] // 2
                got = jnp.concatenate(
                    [lax.ppermute(payload[:cut], "dp", pairs), lax.ppermute(payload[cut:], "dp", pairs)]
                )
            got_feats = got[: flat_feats.shape[0]].reshape(feats.shape)
            got_held = got[flat_feats.shape[0]:].reshape(away.shape)
        else:
            got_feats, got_held = lax.ppermute((feats, away), "dp", pairs)
        if last:
            got_feats = jnp.transpose(got_feats, cross_rev + [nbits - 1, nbits])
            got_held = jnp.transpose(got_held, cross_rev + [nbits - 1, nbits])
        feats = jnp.stack([feats, got_feats])
        held = jnp.stack([keep, got_held], axis=dim)
    feats = feats.reshape(-1, 2 * bot)
    src = me ^ pos
    where = src & 1
    for d, bit in enumerate(dim_bits):
        where = (where << 1) | ((src >> bit) & 1)
    held = jnp.take(held.reshape(n, 2 * rows, cols), where, axis=0)
    sw = held[:, :rows].reshape(n * rows, cols)
    tw = held[:, rows:].reshape(n * rows, cols)
    zt, zs = feats[:, :bot], feats[:, bot:]
    c = lax.dynamic_slice_in_dim(center, me * cols, cols)
    t_norm = jnp.sqrt(jnp.sum(jnp.square(tw.astype(jnp.float32)), 0) + 1e-06)
    s_norm = jnp.sqrt(jnp.sum(jnp.square(sw.astype(jnp.float32)), 0) + 1e-06)
    t_cos = jnp.dot(zt, tw, preferred_element_type=jnp.float32) / t_norm
    s_cos = jnp.dot(zs, sw, preferred_element_type=jnp.float32) / s_norm
    t_exp = jnp.exp((t_cos - c) / 0.04)
    s_exp = jnp.exp(s_cos / 0.1)
    totals = jnp.stack([jnp.sum(t_exp, 1), jnp.sum(s_exp, 1)])
    shape = (2,) + (2,) * nbits + (images,)
    for r in range(nbits):
        if r == nbits - 1:
            got = lax.ppermute(totals, "dp", [(i, i ^ 1) for i in range(n)]).reshape(shape)
            got = jnp.flip(jnp.transpose(got, [0, 1] + [2 + d for d in cross_rev] + [nbits + 1]), 1)
        else:
            got = lax.ppermute(totals, "dp", swap(up[r], down[r])).reshape(shape)
            got = jnp.flip(got, nbits - r)
        totals = totals + got.reshape(totals.shape)
    totals = exchange_all(totals, "tensor", lax.axis_size("tensor"))
    t_total, s_total = totals[0][:, None], totals[1][:, None]
    part_center = 0.5 * c + 0.5 * (jnp.sum(t_cos, 0) / (images * n))
    dlog = ((s_exp / s_total - t_exp / t_total) / 0.1).astype(jnp.bfloat16)
    product = lax.dot_general(
        zs, dlog, (((0,), (0,)), ((), ())), preferred_element_type=jnp.float32
    )
    wide = sw.astype(jnp.float32)
    scaled = jnp.sum(wide * product, 0) / s_norm / s_norm
    grad = (product - wide * scaled) / s_norm
    high = part_center.astype(jnp.bfloat16)
    low = (part_center - high.astype(jnp.float32)).astype(jnp.bfloat16)
    sent = jnp.concatenate(
        [
            grad.astype(jnp.bfloat16).reshape(n, rows, cols),
            jnp.broadcast_to(jnp.stack([high, low]), (n, 2, cols)),
        ],
        axis=1,
    )
    got = lax.all_to_all(sent, "dp", 0, 2, tiled=True)
    got = got.reshape(rows + 2, n * cols).astype(jnp.float32)
    return (master_new, got[:rows], got[rows] + got[rows + 1])


def solution(mesh):
    placed = (P("dp", "tensor"), P("dp", "tensor"), P("dp", None), P("dp", None), P("tensor"))
    return jax.shard_map(
        shards_for(mesh),
        mesh=mesh,
        in_specs=placed,
        out_specs=(P("dp", "tensor"), P("dp", "tensor"), P("tensor")),
        check_vma=False,
    )


def shards_for(mesh):
    ndp = mesh.shape["dp"]

    def shards(teacher_master, student_weight, teacher_feat, student_feat, center):
        images_all = teacher_feat.shape[0] * ndp
        cols = center.shape[0]
        if images_all < cols and cols % ndp == 0 and ndp > 1 and ndp & (ndp - 1) == 0:
            return feature_plan(teacher_master, student_weight, teacher_feat, student_feat, center)
        return weight_plan(teacher_master, student_weight, teacher_feat, student_feat, center)

    return shards
```

```python
import jax
import jax.numpy as jnp
from jax import lax
from jax.sharding import PartitionSpec as P


def unit_rows(feat):
    wide = feat.astype(jnp.float32)
    return (wide * lax.rsqrt(jnp.sum(wide * wide, 1, keepdims=True) + 1e-06)).astype(jnp.bfloat16)


def weight_plan(teacher_master, student_weight, teacher_feat, student_feat, center):
    zt = unit_rows(teacher_feat)
    zs = unit_rows(student_feat)
    images_all = teacher_feat.shape[0] * lax.axis_size("dp")
    student_full = lax.all_gather(student_weight, "dp", axis=0, tiled=True)
    master_new = 0.996 * teacher_master + 0.004 * student_weight.astype(jnp.float32)
    weight = lax.all_gather(master_new.astype(jnp.bfloat16), "dp", axis=0, tiled=True)
    raw = jnp.dot(zt, weight, preferred_element_type=jnp.float32)
    t_norm = jnp.sqrt(jnp.sum(jnp.square(weight.astype(jnp.float32)), 0) + 1e-06)
    t_cos = raw / t_norm
    s_norm = jnp.sqrt(jnp.sum(jnp.square(student_full.astype(jnp.float32)), 0) + 1e-06)
    s_cos = jnp.dot(zs, student_full, preferred_element_type=jnp.float32) / s_norm
    t_exp = jnp.exp((t_cos - center) / 0.04)
    s_exp = jnp.exp(s_cos / 0.1)
    t_total, s_total = lax.psum(
        (jnp.sum(t_exp, 1, keepdims=True), jnp.sum(s_exp, 1, keepdims=True)), "tensor"
    )
    cos_mean = lax.psum(jnp.sum(t_cos, 0), "dp") / images_all
    new_center = 0.5 * center + 0.5 * cos_mean
    dlog = ((s_exp / s_total - t_exp / t_total) / 0.1).astype(jnp.bfloat16)
    scaled = jnp.sum(dlog.astype(jnp.float32) * s_cos, 0) / s_norm
    product = lax.dot_general(
        zs, dlog, (((0,), (0,)), ((), ())), preferred_element_type=jnp.float32
    )
    student_grad = lax.psum_scatter(
        (product - student_full.astype(jnp.float32) * scaled) / s_norm,
        "dp",
        scatter_dimension=0,
        tiled=True,
    )
    return (master_new, student_grad, new_center)


def exchange_sum(x, axis, n):
    if n & (n - 1):
        return lax.psum(x, axis)
    step = 1
    while step < n:
        x = x + lax.ppermute(x, axis, [(i, i ^ step) for i in range(n)])
        step *= 2
    return x


def exchange_all(x, axis, n):
    total = x
    for k in range(1, n):
        total = total + lax.ppermute(x, axis, [(i, (i + k) % n) for i in range(n)])
    return total


def feature_plan(teacher_master, student_weight, teacher_feat, student_feat, center):
    n = lax.axis_size("dp")
    me = lax.axis_index("dp")
    rows, width = teacher_master.shape
    bot = teacher_feat.shape[1]
    images = teacher_feat.shape[0]
    cols = width // n
    nbits = n.bit_length() - 1
    odd = me % 2
    up = list(range(1, nbits))
    down = up[::-1]
    dim_bits = [jnp.where(odd == 1, down[r], up[r]) for r in range(nbits - 1)][::-1]
    master_new = 0.996 * teacher_master + 0.004 * student_weight.astype(jnp.float32)
    both = jnp.stack([student_weight, master_new.astype(jnp.bfloat16)])
    both = both.reshape(2, rows, n, cols).transpose(2, 0, 1, 3).reshape(n, 2 * rows, cols)
    pos = jnp.arange(n)
    rel = (pos >> (nbits - 1)) & 1
    for d, bit in enumerate(dim_bits):
        rel = rel | (((pos >> (nbits - 2 - d)) & 1) << bit)
    held = jnp.take(both, me ^ rel, axis=0).reshape((2,) * nbits + (2 * rows, cols))
    feats = jnp.concatenate([unit_rows(teacher_feat), unit_rows(student_feat)], axis=1)
    cross_rev = list(range(nbits - 2, -1, -1))

    def swap(pairs_up, pairs_down):
        return [(i, i ^ (1 << (pairs_down if i % 2 else pairs_up))) for i in range(n)]

    for r in range(nbits):
        last = r == nbits - 1
        dim = 0 if last else nbits - 1 - r
        keep = lax.index_in_dim(held, 0, dim, keepdims=False)
        away = lax.index_in_dim(held, 1, dim, keepdims=False)
        if last:
            pairs = [(i, i ^ 1) for i in range(n)]
        else:
            pairs = swap(up[r], down[r])
        if 2 * bot == cols:
            flat_feats = feats.reshape(-1, 2 * bot)
            payload = jnp.concatenate([flat_feats, away.reshape(-1, cols)], axis=0)
            got = lax.ppermute(payload, "dp", pairs)
            got_feats = got[: flat_feats.shape[0]].reshape(feats.shape)
            got_held = got[flat_feats.shape[0]:].reshape(away.shape)
        else:
            got_feats, got_held = lax.ppermute((feats, away), "dp", pairs)
        if last:
            got_feats = jnp.transpose(got_feats, cross_rev + [nbits - 1, nbits])
            got_held = jnp.transpose(got_held, cross_rev + [nbits - 1, nbits])
        feats = jnp.stack([feats, got_feats])
        held = jnp.stack([keep, got_held], axis=dim)
    feats = feats.reshape(-1, 2 * bot)
    src = me ^ pos
    where = src & 1
    for d, bit in enumerate(dim_bits):
        where = (where << 1) | ((src >> bit) & 1)
    held = jnp.take(held.reshape(n, 2 * rows, cols), where, axis=0)
    sw = held[:, :rows].reshape(n * rows, cols)
    tw = held[:, rows:].reshape(n * rows, cols)
    zt, zs = feats[:, :bot], feats[:, bot:]
    c = lax.dynamic_slice_in_dim(center, me * cols, cols)
    t_norm = jnp.sqrt(jnp.sum(jnp.square(tw.astype(jnp.float32)), 0) + 1e-06)
    s_norm = jnp.sqrt(jnp.sum(jnp.square(sw.astype(jnp.float32)), 0) + 1e-06)
    t_cos = jnp.dot(zt, tw, preferred_element_type=jnp.float32) / t_norm
    s_cos = jnp.dot(zs, sw, preferred_element_type=jnp.float32) / s_norm
    t_exp = jnp.exp((t_cos - c) / 0.04)
    s_exp = jnp.exp(s_cos / 0.1)
    totals = jnp.stack([jnp.sum(t_exp, 1), jnp.sum(s_exp, 1)])
    shape = (2,) + (2,) * nbits + (images,)
    for r in range(nbits):
        if r == nbits - 1:
            got = lax.ppermute(totals, "dp", [(i, i ^ 1) for i in range(n)]).reshape(shape)
            got = jnp.flip(jnp.transpose(got, [0, 1] + [2 + d for d in cross_rev] + [nbits + 1]), 1)
        else:
            got = lax.ppermute(totals, "dp", swap(up[r], down[r])).reshape(shape)
            got = jnp.flip(got, nbits - r)
        totals = totals + got.reshape(totals.shape)
    totals = exchange_sum(totals, "tensor", lax.axis_size("tensor"))
    t_total, s_total = totals[0][:, None], totals[1][:, None]
    part_center = 0.5 * c + 0.5 * (jnp.sum(t_cos, 0) / (images * n))
    dlog = ((s_exp / s_total - t_exp / t_total) / 0.1).astype(jnp.bfloat16)
    product = lax.dot_general(
        zs, dlog, (((0,), (0,)), ((), ())), preferred_element_type=jnp.float32
    )
    wide = sw.astype(jnp.float32)
    scaled = jnp.sum(wide * product, 0) / s_norm / s_norm
    grad = (product - wide * scaled) / s_norm
    high = part_center.astype(jnp.bfloat16)
    low = (part_center - high.astype(jnp.float32)).astype(jnp.bfloat16)
    sent = jnp.concatenate(
        [
            grad.astype(jnp.bfloat16).reshape(n, rows, cols),
            jnp.broadcast_to(jnp.stack([high, low]), (n, 2, cols)),
        ],
        axis=1,
    )
    got = lax.all_to_all(sent, "dp", 0, 2, tiled=True)
    got = got.reshape(rows + 2, n * cols).astype(jnp.float32)
    return (master_new, got[:rows], got[rows] + got[rows + 1])


def solution(mesh):
    placed = (P("dp", "tensor"), P("dp", "tensor"), P("dp", None), P("dp", None), P("tensor"))
    return jax.shard_map(
        shards_for(mesh),
        mesh=mesh,
        in_specs=placed,
        out_specs=(P("dp", "tensor"), P("dp", "tensor"), P("tensor")),
        check_vma=False,
    )


def shards_for(mesh):
    ndp = mesh.shape["dp"]

    def shards(teacher_master, student_weight, teacher_feat, student_feat, center):
        images_all = teacher_feat.shape[0] * ndp
        cols = center.shape[0]
        if images_all < cols and cols % ndp == 0 and ndp > 1 and ndp & (ndp - 1) == 0:
            return feature_plan(teacher_master, student_weight, teacher_feat, student_feat, center)
        return weight_plan(teacher_master, student_weight, teacher_feat, student_feat, center)

    return shards
```

```python
import jax
import jax.numpy as jnp
from jax import lax
from jax.sharding import PartitionSpec as P


def unit_rows(feat):
    wide = feat.astype(jnp.float32)
    return (wide * lax.rsqrt(jnp.sum(wide * wide, 1, keepdims=True) + 1e-06)).astype(jnp.bfloat16)


def weight_plan(teacher_master, student_weight, teacher_feat, student_feat, center):
    zt = unit_rows(teacher_feat)
    zs = unit_rows(student_feat)
    images_all = teacher_feat.shape[0] * lax.axis_size("dp")
    student_full = lax.all_gather(student_weight, "dp", axis=0, tiled=True)
    master_new = 0.996 * teacher_master + 0.004 * student_weight.astype(jnp.float32)
    weight = lax.all_gather(master_new.astype(jnp.bfloat16), "dp", axis=0, tiled=True)
    raw = jnp.dot(zt, weight, preferred_element_type=jnp.float32)
    t_norm = jnp.sqrt(jnp.sum(jnp.square(weight.astype(jnp.float32)), 0) + 1e-06)
    t_cos = raw / t_norm
    s_norm = jnp.sqrt(jnp.sum(jnp.square(student_full.astype(jnp.float32)), 0) + 1e-06)
    s_cos = jnp.dot(zs, student_full, preferred_element_type=jnp.float32) / s_norm
    t_exp = jnp.exp((t_cos - center) / 0.04)
    s_exp = jnp.exp(s_cos / 0.1)
    t_total, s_total = lax.psum(
        (jnp.sum(t_exp, 1, keepdims=True), jnp.sum(s_exp, 1, keepdims=True)), "tensor"
    )
    cos_mean = lax.psum(jnp.sum(t_cos, 0), "dp") / images_all
    new_center = 0.5 * center + 0.5 * cos_mean
    dlog = ((s_exp / s_total - t_exp / t_total) / 0.1).astype(jnp.bfloat16)
    scaled = jnp.sum(dlog.astype(jnp.float32) * s_cos, 0) / s_norm
    product = lax.dot_general(
        zs, dlog, (((0,), (0,)), ((), ())), preferred_element_type=jnp.float32
    )
    student_grad = lax.psum_scatter(
        (product - student_full.astype(jnp.float32) * scaled) / s_norm,
        "dp",
        scatter_dimension=0,
        tiled=True,
    )
    return (master_new, student_grad, new_center)


def exchange_sum(x, axis, n):
    if n & (n - 1):
        return lax.psum(x, axis)
    step = 1
    while step < n:
        x = x + lax.ppermute(x, axis, [(i, i ^ step) for i in range(n)])
        step *= 2
    return x


def exchange_all(x, axis, n):
    total = x
    for k in range(1, n):
        total = total + lax.ppermute(x, axis, [(i, (i + k) % n) for i in range(n)])
    return total


def feature_plan(teacher_master, student_weight, teacher_feat, student_feat, center):
    n = lax.axis_size("dp")
    me = lax.axis_index("dp")
    rows, width = teacher_master.shape
    bot = teacher_feat.shape[1]
    images = teacher_feat.shape[0]
    cols = width // n
    nbits = n.bit_length() - 1
    odd = me % 2
    up = list(range(1, nbits))
    down = up[::-1]
    dim_bits = [jnp.where(odd == 1, down[r], up[r]) for r in range(nbits - 1)][::-1]
    master_new = 0.996 * teacher_master + 0.004 * student_weight.astype(jnp.float32)

    def by_destination(weight):
        return weight.reshape(rows, n, cols).transpose(1, 0, 2)

    pos = jnp.arange(n)
    rel = (pos >> (nbits - 1)) & 1
    for d, bit in enumerate(dim_bits):
        rel = rel | (((pos >> (nbits - 2 - d)) & 1) << bit)
    held = [
        jnp.take(by_destination(w), me ^ rel, axis=0).reshape((2,) * nbits + (rows, cols))
        for w in (student_weight, master_new.astype(jnp.bfloat16))
    ]
    feats = jnp.concatenate([unit_rows(teacher_feat), unit_rows(student_feat)], axis=1)
    cross_rev = list(range(nbits - 2, -1, -1))

    def swap(pairs_up, pairs_down):
        return [(i, i ^ (1 << (pairs_down if i % 2 else pairs_up))) for i in range(n)]

    for r in range(nbits):
        last = r == nbits - 1
        dim = 0 if last else nbits - 1 - r
        keep = [lax.index_in_dim(h, 0, dim, keepdims=False) for h in held]
        away = [lax.index_in_dim(h, 1, dim, keepdims=False) for h in held]
        if last:
            pairs = [(i, i ^ 1) for i in range(n)]
        else:
            pairs = swap(up[r], down[r])
        flat = [feats.reshape(-1, 2 * bot)] + [a.reshape(-1, cols) for a in away]
        if 2 * bot == cols and r == 0:
            got = lax.ppermute(jnp.concatenate(flat[:2], axis=0), "dp", pairs)
            got = [got[: flat[0].shape[0]], got[flat[0].shape[0]:]]
            got = got + [lax.ppermute(flat[2], "dp", pairs)]
        elif 2 * bot == cols:
            got = lax.ppermute(jnp.concatenate(flat, axis=0), "dp", pairs)
            cut = [flat[0].shape[0], flat[0].shape[0] + flat[1].shape[0]]
            got = [got[: cut[0]], got[cut[0]: cut[1]], got[cut[1]:]]
        else:
            got = list(lax.ppermute(tuple(flat), "dp", pairs))
        got_feats = got[0].reshape(feats.shape)
        got_held = [g.reshape(a.shape) for g, a in zip(got[1:], away)]
        if last:
            got_feats = jnp.transpose(got_feats, cross_rev + [nbits - 1, nbits])
            got_held = [jnp.transpose(g, cross_rev + [nbits - 1, nbits]) for g in got_held]
        feats = jnp.stack([feats, got_feats])
        held = [jnp.stack([k, g], axis=dim) for k, g in zip(keep, got_held)]
    feats = feats.reshape(-1, 2 * bot)
    src = me ^ pos
    where = src & 1
    for d, bit in enumerate(dim_bits):
        where = (where << 1) | ((src >> bit) & 1)
    sw, tw = [jnp.take(h.reshape(n, rows, cols), where, axis=0).reshape(n * rows, cols) for h in held]
    zt, zs = feats[:, :bot], feats[:, bot:]
    c = lax.dynamic_slice_in_dim(center, me * cols, cols)
    t_norm = jnp.sqrt(jnp.sum(jnp.square(tw.astype(jnp.float32)), 0) + 1e-06)
    s_norm = jnp.sqrt(jnp.sum(jnp.square(sw.astype(jnp.float32)), 0) + 1e-06)
    t_cos = jnp.dot(zt, tw, preferred_element_type=jnp.float32) / t_norm
    s_cos = jnp.dot(zs, sw, preferred_element_type=jnp.float32) / s_norm
    t_exp = jnp.exp((t_cos - c) / 0.04)
    s_exp = jnp.exp(s_cos / 0.1)
    totals = jnp.stack([jnp.sum(t_exp, 1), jnp.sum(s_exp, 1)])
    shape = (2,) + (2,) * nbits + (images,)
    for r in range(nbits):
        if r == nbits - 1:
            got = lax.ppermute(totals, "dp", [(i, i ^ 1) for i in range(n)]).reshape(shape)
            got = jnp.flip(jnp.transpose(got, [0, 1] + [2 + d for d in cross_rev] + [nbits + 1]), 1)
        else:
            got = lax.ppermute(totals, "dp", swap(up[r], down[r])).reshape(shape)
            got = jnp.flip(got, nbits - r)
        totals = totals + got.reshape(totals.shape)
    totals = exchange_all(totals, "tensor", lax.axis_size("tensor"))
    t_total, s_total = totals[0][:, None], totals[1][:, None]
    part_center = 0.5 * c + 0.5 * (jnp.sum(t_cos, 0) / (images * n))
    dlog = ((s_exp / s_total - t_exp / t_total) / 0.1).astype(jnp.bfloat16)
    product = lax.dot_general(
        zs, dlog, (((0,), (0,)), ((), ())), preferred_element_type=jnp.float32
    )
    wide = sw.astype(jnp.float32)
    scaled = jnp.sum(wide * product, 0) / s_norm / s_norm
    grad = (product - wide * scaled) / s_norm
    high = part_center.astype(jnp.bfloat16)
    low = (part_center - high.astype(jnp.float32)).astype(jnp.bfloat16)
    sent = jnp.concatenate(
        [
            grad.astype(jnp.bfloat16).reshape(n, rows, cols),
            jnp.broadcast_to(jnp.stack([high, low]), (n, 2, cols)),
        ],
        axis=1,
    )
    got = lax.all_to_all(sent, "dp", 0, 2, tiled=True)
    got = got.reshape(rows + 2, n * cols).astype(jnp.float32)
    return (master_new, got[:rows], got[rows] + got[rows + 1])


def solution(mesh):
    placed = (P("dp", "tensor"), P("dp", "tensor"), P("dp", None), P("dp", None), P("tensor"))
    return jax.shard_map(
        shards_for(mesh),
        mesh=mesh,
        in_specs=placed,
        out_specs=(P("dp", "tensor"), P("dp", "tensor"), P("tensor")),
        check_vma=False,
    )


def shards_for(mesh):
    ndp = mesh.shape["dp"]

    def shards(teacher_master, student_weight, teacher_feat, student_feat, center):
        images_all = teacher_feat.shape[0] * ndp
        cols = center.shape[0]
        if images_all < cols and cols % ndp == 0 and ndp > 1 and ndp & (ndp - 1) == 0:
            return feature_plan(teacher_master, student_weight, teacher_feat, student_feat, center)
        return weight_plan(teacher_master, student_weight, teacher_feat, student_feat, center)

    return shards
```

```python
import jax
import jax.numpy as jnp
from jax import lax
from jax.sharding import PartitionSpec as P


def unit_rows(feat):
    wide = feat.astype(jnp.float32)
    return (wide * lax.rsqrt(jnp.sum(wide * wide, 1, keepdims=True) + 1e-06)).astype(jnp.bfloat16)


def weight_plan(teacher_master, student_weight, teacher_feat, student_feat, center):
    zt = unit_rows(teacher_feat)
    zs = unit_rows(student_feat)
    images_all = teacher_feat.shape[0] * lax.axis_size("dp")
    student_full = lax.all_gather(student_weight, "dp", axis=0, tiled=True)
    master_new = 0.996 * teacher_master + 0.004 * student_weight.astype(jnp.float32)
    weight = lax.all_gather(master_new.astype(jnp.bfloat16), "dp", axis=0, tiled=True)
    raw = jnp.dot(zt, weight, preferred_element_type=jnp.float32)
    t_norm = jnp.sqrt(jnp.sum(jnp.square(weight.astype(jnp.float32)), 0) + 1e-06)
    t_cos = raw / t_norm
    s_norm = jnp.sqrt(jnp.sum(jnp.square(student_full.astype(jnp.float32)), 0) + 1e-06)
    s_cos = jnp.dot(zs, student_full, preferred_element_type=jnp.float32) / s_norm
    t_exp = jnp.exp((t_cos - center) / 0.04)
    s_exp = jnp.exp(s_cos / 0.1)
    t_total, s_total = lax.psum(
        (jnp.sum(t_exp, 1, keepdims=True), jnp.sum(s_exp, 1, keepdims=True)), "tensor"
    )
    cos_mean = lax.psum(jnp.sum(t_cos, 0), "dp") / images_all
    new_center = 0.5 * center + 0.5 * cos_mean
    dlog = ((s_exp / s_total - t_exp / t_total) / 0.1).astype(jnp.bfloat16)
    scaled = jnp.sum(dlog.astype(jnp.float32) * s_cos, 0) / s_norm
    product = lax.dot_general(
        zs, dlog, (((0,), (0,)), ((), ())), preferred_element_type=jnp.float32
    )
    student_grad = lax.psum_scatter(
        (product - student_full.astype(jnp.float32) * scaled) / s_norm,
        "dp",
        scatter_dimension=0,
        tiled=True,
    )
    return (master_new, student_grad, new_center)


def exchange_sum(x, axis, n):
    if n & (n - 1):
        return lax.psum(x, axis)
    step = 1
    while step < n:
        x = x + lax.ppermute(x, axis, [(i, i ^ step) for i in range(n)])
        step *= 2
    return x


def exchange_all(x, axis, n):
    total = x
    for k in range(1, n):
        total = total + lax.ppermute(x, axis, [(i, (i + k) % n) for i in range(n)])
    return total


def feature_plan(teacher_master, student_weight, teacher_feat, student_feat, center):
    n = lax.axis_size("dp")
    me = lax.axis_index("dp")
    rows, width = teacher_master.shape
    bot = teacher_feat.shape[1]
    images = teacher_feat.shape[0]
    cols = width // n
    nbits = n.bit_length() - 1
    odd = me % 2
    up = list(range(1, nbits))
    down = up[::-1]
    dim_bits = [jnp.where(odd == 1, down[r], up[r]) for r in range(nbits - 1)][::-1]
    master_new = 0.996 * teacher_master + 0.004 * student_weight.astype(jnp.float32)
    both = jnp.stack([student_weight, master_new.astype(jnp.bfloat16)])
    both = both.reshape(2, rows, n, cols).transpose(2, 0, 1, 3).reshape(n, 2 * rows, cols)
    pos = jnp.arange(n)
    rel = (pos >> (nbits - 1)) & 1
    for d, bit in enumerate(dim_bits):
        rel = rel | (((pos >> (nbits - 2 - d)) & 1) << bit)
    held = jnp.take(both, me ^ rel, axis=0).reshape((2,) * nbits + (2 * rows, cols))
    feats = jnp.concatenate([unit_rows(teacher_feat), unit_rows(student_feat)], axis=1)
    cross_rev = list(range(nbits - 2, -1, -1))

    def swap(pairs_up, pairs_down):
        return [(i, i ^ (1 << (pairs_down if i % 2 else pairs_up))) for i in range(n)]

    for r in range(nbits):
        last = r == nbits - 1
        dim = 0 if last else nbits - 1 - r
        keep = lax.index_in_dim(held, 0, dim, keepdims=False)
        away = lax.index_in_dim(held, 1, dim, keepdims=False)
        if last:
            pairs = [(i, i ^ 1) for i in range(n)]
        else:
            pairs = swap(up[r], down[r])
        if 2 * bot == cols:
            flat_feats = feats.reshape(-1, 2 * bot)
            payload = jnp.concatenate([flat_feats, away.reshape(-1, cols)], axis=0)
            got = lax.ppermute(payload, "dp", pairs)
            got_feats = got[: flat_feats.shape[0]].reshape(feats.shape)
            got_held = got[flat_feats.shape[0]:].reshape(away.shape)
        else:
            got_feats, got_held = lax.ppermute((feats, away), "dp", pairs)
        if last:
            got_feats = jnp.transpose(got_feats, cross_rev + [nbits - 1, nbits])
            got_held = jnp.transpose(got_held, cross_rev + [nbits - 1, nbits])
        feats = jnp.stack([feats, got_feats])
        held = jnp.stack([keep, got_held], axis=dim)
    feats = feats.reshape(-1, 2 * bot)
    src = me ^ pos
    where = src & 1
    for d, bit in enumerate(dim_bits):
        where = (where << 1) | ((src >> bit) & 1)
    held = jnp.take(held.reshape(n, 2 * rows, cols), where, axis=0)
    sw = held[:, :rows].reshape(n * rows, cols)
    tw = held[:, rows:].reshape(n * rows, cols)
    zt, zs = feats[:, :bot], feats[:, bot:]
    c = lax.dynamic_slice_in_dim(center, me * cols, cols)
    t_norm = jnp.sqrt(jnp.sum(jnp.square(tw.astype(jnp.float32)), 0) + 1e-06)
    s_norm = jnp.sqrt(jnp.sum(jnp.square(sw.astype(jnp.float32)), 0) + 1e-06)
    t_cos = jnp.dot(zt, tw, preferred_element_type=jnp.float32) / t_norm
    s_cos = jnp.dot(zs, sw, preferred_element_type=jnp.float32) / s_norm
    t_exp = jnp.exp((t_cos - c) / 0.04)
    s_exp = jnp.exp(s_cos / 0.1)
    totals = jnp.stack([jnp.sum(t_exp, 1), jnp.sum(s_exp, 1)])
    t_exp = t_exp.astype(jnp.bfloat16).astype(jnp.float32)
    s_exp = s_exp.astype(jnp.bfloat16).astype(jnp.float32)
    shape = (2,) + (2,) * nbits + (images,)
    for r in range(nbits):
        if r == nbits - 1:
            got = lax.ppermute(totals, "dp", [(i, i ^ 1) for i in range(n)]).reshape(shape)
            got = jnp.flip(jnp.transpose(got, [0, 1] + [2 + d for d in cross_rev] + [nbits + 1]), 1)
        else:
            got = lax.ppermute(totals, "dp", swap(up[r], down[r])).reshape(shape)
            got = jnp.flip(got, nbits - r)
        totals = totals + got.reshape(totals.shape)
    totals = exchange_all(totals, "tensor", lax.axis_size("tensor"))
    t_total, s_total = totals[0][:, None], totals[1][:, None]
    part_center = 0.5 * c + 0.5 * (jnp.sum(t_cos, 0) / (images * n))
    dlog = ((s_exp / s_total - t_exp / t_total) / 0.1).astype(jnp.bfloat16)
    product = lax.dot_general(
        zs, dlog, (((0,), (0,)), ((), ())), preferred_element_type=jnp.float32
    )
    wide = sw.astype(jnp.float32)
    scaled = jnp.sum(wide * product, 0) / s_norm / s_norm
    grad = (product - wide * scaled) / s_norm
    high = part_center.astype(jnp.bfloat16)
    low = (part_center - high.astype(jnp.float32)).astype(jnp.bfloat16)
    sent = jnp.concatenate(
        [
            grad.astype(jnp.bfloat16).reshape(n, rows, cols),
            jnp.broadcast_to(jnp.stack([high, low]), (n, 2, cols)),
        ],
        axis=1,
    )
    got = lax.all_to_all(sent, "dp", 0, 2, tiled=True)
    got = got.reshape(rows + 2, n * cols).astype(jnp.float32)
    return (master_new, got[:rows], got[rows] + got[rows + 1])


def solution(mesh):
    placed = (P("dp", "tensor"), P("dp", "tensor"), P("dp", None), P("dp", None), P("tensor"))
    return jax.shard_map(
        shards_for(mesh),
        mesh=mesh,
        in_specs=placed,
        out_specs=(P("dp", "tensor"), P("dp", "tensor"), P("tensor")),
        check_vma=False,
    )


def shards_for(mesh):
    ndp = mesh.shape["dp"]

    def shards(teacher_master, student_weight, teacher_feat, student_feat, center):
        images_all = teacher_feat.shape[0] * ndp
        cols = center.shape[0]
        if images_all < cols and cols % ndp == 0 and ndp > 1 and ndp & (ndp - 1) == 0:
            return feature_plan(teacher_master, student_weight, teacher_feat, student_feat, center)
        return weight_plan(teacher_master, student_weight, teacher_feat, student_feat, center)

    return shards
```

```python
import jax
import jax.numpy as jnp
from jax import lax
from jax.sharding import PartitionSpec as P


def unit_rows(feat):
    wide = feat.astype(jnp.float32)
    return (wide * lax.rsqrt(jnp.sum(wide * wide, 1, keepdims=True) + 1e-06)).astype(jnp.bfloat16)


def weight_plan(teacher_master, student_weight, teacher_feat, student_feat, center):
    zt = unit_rows(teacher_feat)
    zs = unit_rows(student_feat)
    images_all = teacher_feat.shape[0] * lax.axis_size("dp")
    student_full = lax.all_gather(student_weight, "dp", axis=0, tiled=True)
    master_new = 0.996 * teacher_master + 0.004 * student_weight.astype(jnp.float32)
    weight = lax.all_gather(master_new.astype(jnp.bfloat16), "dp", axis=0, tiled=True)
    raw = jnp.dot(zt, weight, preferred_element_type=jnp.float32)
    t_norm = jnp.sqrt(jnp.sum(jnp.square(weight.astype(jnp.float32)), 0) + 1e-06)
    t_cos = raw / t_norm
    s_norm = jnp.sqrt(jnp.sum(jnp.square(student_full.astype(jnp.float32)), 0) + 1e-06)
    s_cos = jnp.dot(zs, student_full, preferred_element_type=jnp.float32) / s_norm
    t_exp = jnp.exp((t_cos - center) / 0.04)
    s_exp = jnp.exp(s_cos / 0.1)
    t_total, s_total = lax.psum(
        (jnp.sum(t_exp, 1, keepdims=True), jnp.sum(s_exp, 1, keepdims=True)), "tensor"
    )
    cos_mean = lax.psum(jnp.sum(t_cos, 0), "dp") / images_all
    new_center = 0.5 * center + 0.5 * cos_mean
    dlog = ((s_exp / s_total - t_exp / t_total) / 0.1).astype(jnp.bfloat16)
    scaled = jnp.sum(dlog.astype(jnp.float32) * s_cos, 0) / s_norm
    product = lax.dot_general(
        zs, dlog, (((0,), (0,)), ((), ())), preferred_element_type=jnp.float32
    )
    student_grad = lax.psum_scatter(
        (product - student_full.astype(jnp.float32) * scaled) / s_norm,
        "dp",
        scatter_dimension=0,
        tiled=True,
    )
    return (master_new, student_grad, new_center)


def exchange_sum(x, axis, n):
    if n & (n - 1):
        return lax.psum(x, axis)
    step = 1
    while step < n:
        x = x + lax.ppermute(x, axis, [(i, i ^ step) for i in range(n)])
        step *= 2
    return x


def exchange_all(x, axis, n):
    total = x
    for k in range(1, n):
        total = total + lax.ppermute(x, axis, [(i, (i + k) % n) for i in range(n)])
    return total


def feature_plan(teacher_master, student_weight, teacher_feat, student_feat, center):
    n = lax.axis_size("dp")
    me = lax.axis_index("dp")
    rows, width = teacher_master.shape
    bot = teacher_feat.shape[1]
    images = teacher_feat.shape[0]
    cols = width // n
    nbits = n.bit_length() - 1
    odd = me % 2
    up = list(range(1, nbits))
    down = up[::-1]
    dim_bits = [jnp.where(odd == 1, down[r], up[r]) for r in range(nbits - 1)][::-1]
    master_new = 0.996 * teacher_master + 0.004 * student_weight.astype(jnp.float32)
    both = jnp.stack([student_weight, master_new.astype(jnp.bfloat16)])
    both = both.reshape(2, rows, n, cols).transpose(2, 0, 1, 3).reshape(n, 2 * rows, cols)
    pos = jnp.arange(n)
    rel = (pos >> (nbits - 1)) & 1
    for d, bit in enumerate(dim_bits):
        rel = rel | (((pos >> (nbits - 2 - d)) & 1) << bit)
    held = jnp.take(both, me ^ rel, axis=0).reshape((2,) * nbits + (2 * rows, cols))
    feats = jnp.concatenate([unit_rows(teacher_feat), unit_rows(student_feat)], axis=1)
    cross_rev = list(range(nbits - 2, -1, -1))

    def swap(pairs_up, pairs_down):
        return [(i, i ^ (1 << (pairs_down if i % 2 else pairs_up))) for i in range(n)]

    for r in range(nbits):
        last = r == nbits - 1
        dim = 0 if last else nbits - 1 - r
        keep = lax.index_in_dim(held, 0, dim, keepdims=False)
        away = lax.index_in_dim(held, 1, dim, keepdims=False)
        if last:
            pairs = [(i, i ^ 1) for i in range(n)]
        else:
            pairs = swap(up[r], down[r])
        if 2 * bot == cols:
            flat_feats = feats.reshape(-1, 2 * bot)
            payload = jnp.concatenate([flat_feats, away.reshape(-1, cols)], axis=0)
            got = lax.ppermute(payload, "dp", pairs)
            got_feats = got[: flat_feats.shape[0]].reshape(feats.shape)
            got_held = got[flat_feats.shape[0]:].reshape(away.shape)
        else:
            got_feats, got_held = lax.ppermute((feats, away), "dp", pairs)
        if last:
            got_feats = jnp.transpose(got_feats, cross_rev + [nbits - 1, nbits])
            got_held = jnp.transpose(got_held, cross_rev + [nbits - 1, nbits])
        feats = jnp.stack([feats, got_feats])
        held = jnp.stack([keep, got_held], axis=dim)
    feats = feats.reshape(-1, 2 * bot)
    src = me ^ pos
    where = src & 1
    for d, bit in enumerate(dim_bits):
        where = (where << 1) | ((src >> bit) & 1)
    held = jnp.take(held.reshape(n, 2 * rows, cols), where, axis=0)
    sw = held[:, :rows].reshape(n * rows, cols)
    tw = held[:, rows:].reshape(n * rows, cols)
    zt, zs = feats[:, :bot], feats[:, bot:]
    c = lax.dynamic_slice_in_dim(center, me * cols, cols)
    t_norm = jnp.sqrt(jnp.sum(jnp.square(tw.astype(jnp.float32)), 0) + 1e-06)
    s_norm = jnp.sqrt(jnp.sum(jnp.square(sw.astype(jnp.float32)), 0) + 1e-06)
    t_cos = jnp.dot(zt, tw, preferred_element_type=jnp.float32) / t_norm
    s_cos = jnp.dot(zs, sw, preferred_element_type=jnp.float32) / s_norm
    t_exp = jnp.exp((t_cos - c) / 0.04)
    s_exp = jnp.exp(s_cos / 0.1)
    totals = jnp.stack([jnp.sum(t_exp, 1), jnp.sum(s_exp, 1)])
    t_exp, s_exp = lax.optimization_barrier((t_exp.astype(jnp.bfloat16), s_exp.astype(jnp.bfloat16)))
    t_exp, s_exp = t_exp.astype(jnp.float32), s_exp.astype(jnp.float32)
    shape = (2,) + (2,) * nbits + (images,)
    for r in range(nbits):
        if r == nbits - 1:
            got = lax.ppermute(totals, "dp", [(i, i ^ 1) for i in range(n)]).reshape(shape)
            got = jnp.flip(jnp.transpose(got, [0, 1] + [2 + d for d in cross_rev] + [nbits + 1]), 1)
        else:
            got = lax.ppermute(totals, "dp", swap(up[r], down[r])).reshape(shape)
            got = jnp.flip(got, nbits - r)
        totals = totals + got.reshape(totals.shape)
    totals = exchange_all(totals, "tensor", lax.axis_size("tensor"))
    t_total, s_total = totals[0][:, None], totals[1][:, None]
    part_center = 0.5 * c + 0.5 * (jnp.sum(t_cos, 0) / (images * n))
    dlog = ((s_exp / s_total - t_exp / t_total) / 0.1).astype(jnp.bfloat16)
    product = lax.dot_general(
        zs, dlog, (((0,), (0,)), ((), ())), preferred_element_type=jnp.float32
    )
    wide = sw.astype(jnp.float32)
    scaled = jnp.sum(wide * product, 0) / s_norm / s_norm
    grad = (product - wide * scaled) / s_norm
    high = part_center.astype(jnp.bfloat16)
    low = (part_center - high.astype(jnp.float32)).astype(jnp.bfloat16)
    sent = jnp.concatenate(
        [
            grad.astype(jnp.bfloat16).reshape(n, rows, cols),
            jnp.broadcast_to(jnp.stack([high, low]), (n, 2, cols)),
        ],
        axis=1,
    )
    got = lax.all_to_all(sent, "dp", 0, 2, tiled=True)
    got = got.reshape(rows + 2, n * cols).astype(jnp.float32)
    return (master_new, got[:rows], got[rows] + got[rows + 1])


def solution(mesh):
    placed = (P("dp", "tensor"), P("dp", "tensor"), P("dp", None), P("dp", None), P("tensor"))
    return jax.shard_map(
        shards_for(mesh),
        mesh=mesh,
        in_specs=placed,
        out_specs=(P("dp", "tensor"), P("dp", "tensor"), P("tensor")),
        check_vma=False,
    )


def shards_for(mesh):
    ndp = mesh.shape["dp"]

    def shards(teacher_master, student_weight, teacher_feat, student_feat, center):
        images_all = teacher_feat.shape[0] * ndp
        cols = center.shape[0]
        if images_all < cols and cols % ndp == 0 and ndp > 1 and ndp & (ndp - 1) == 0:
            return feature_plan(teacher_master, student_weight, teacher_feat, student_feat, center)
        return weight_plan(teacher_master, student_weight, teacher_feat, student_feat, center)

    return shards
```

```python
import jax
import jax.numpy as jnp
from jax import lax
from jax.sharding import PartitionSpec as P


def unit_rows(feat):
    wide = feat.astype(jnp.float32)
    return (wide * lax.rsqrt(jnp.sum(wide * wide, 1, keepdims=True) + 1e-06)).astype(jnp.bfloat16)


def weight_plan(teacher_master, student_weight, teacher_feat, student_feat, center):
    zt = unit_rows(teacher_feat)
    zs = unit_rows(student_feat)
    images_all = teacher_feat.shape[0] * lax.axis_size("dp")
    student_full = lax.all_gather(student_weight, "dp", axis=0, tiled=True)
    master_new = 0.996 * teacher_master + 0.004 * student_weight.astype(jnp.float32)
    weight = lax.all_gather(master_new.astype(jnp.bfloat16), "dp", axis=0, tiled=True)
    raw = jnp.dot(zt, weight, preferred_element_type=jnp.float32)
    t_norm = jnp.sqrt(jnp.sum(jnp.square(weight.astype(jnp.float32)), 0) + 1e-06)
    t_cos = raw / t_norm
    s_norm = jnp.sqrt(jnp.sum(jnp.square(student_full.astype(jnp.float32)), 0) + 1e-06)
    s_cos = jnp.dot(zs, student_full, preferred_element_type=jnp.float32) / s_norm
    t_exp = jnp.exp((t_cos - center) / 0.04)
    s_exp = jnp.exp(s_cos / 0.1)
    t_total, s_total = lax.psum(
        (jnp.sum(t_exp, 1, keepdims=True), jnp.sum(s_exp, 1, keepdims=True)), "tensor"
    )
    cos_mean = lax.psum(jnp.sum(t_cos, 0), "dp") / images_all
    new_center = 0.5 * center + 0.5 * cos_mean
    dlog = ((s_exp / s_total - t_exp / t_total) / 0.1).astype(jnp.bfloat16)
    scaled = jnp.sum(dlog.astype(jnp.float32) * s_cos, 0) / s_norm
    product = lax.dot_general(
        zs, dlog, (((0,), (0,)), ((), ())), preferred_element_type=jnp.float32
    )
    student_grad = lax.psum_scatter(
        (product - student_full.astype(jnp.float32) * scaled) / s_norm,
        "dp",
        scatter_dimension=0,
        tiled=True,
    )
    return (master_new, student_grad, new_center)


def exchange_sum(x, axis, n):
    if n & (n - 1):
        return lax.psum(x, axis)
    step = 1
    while step < n:
        x = x + lax.ppermute(x, axis, [(i, i ^ step) for i in range(n)])
        step *= 2
    return x


def exchange_all(x, axis, n):
    total = x
    for k in range(1, n):
        total = total + lax.ppermute(x, axis, [(i, (i + k) % n) for i in range(n)])
    return total


def teacher_rows(teacher_master, student_weight):
    master, student = lax.optimization_barrier((teacher_master, student_weight))
    return (0.996 * master + 0.004 * student.astype(jnp.float32)).astype(jnp.bfloat16)


def feature_plan(teacher_master, student_weight, teacher_feat, student_feat, center):
    n = lax.axis_size("dp")
    me = lax.axis_index("dp")
    rows, width = teacher_master.shape
    bot = teacher_feat.shape[1]
    images = teacher_feat.shape[0]
    cols = width // n
    nbits = n.bit_length() - 1
    odd = me % 2
    up = list(range(1, nbits))
    down = up[::-1]
    dim_bits = [jnp.where(odd == 1, down[r], up[r]) for r in range(nbits - 1)][::-1]
    master_new = 0.996 * teacher_master + 0.004 * student_weight.astype(jnp.float32)
    both = jnp.stack([student_weight, teacher_rows(teacher_master, student_weight)])
    both = both.reshape(2, rows, n, cols).transpose(2, 0, 1, 3).reshape(n, 2 * rows, cols)
    pos = jnp.arange(n)
    rel = (pos >> (nbits - 1)) & 1
    for d, bit in enumerate(dim_bits):
        rel = rel | (((pos >> (nbits - 2 - d)) & 1) << bit)
    held = jnp.take(both, me ^ rel, axis=0).reshape((2,) * nbits + (2 * rows, cols))
    feats = jnp.concatenate([unit_rows(teacher_feat), unit_rows(student_feat)], axis=1)
    cross_rev = list(range(nbits - 2, -1, -1))

    def swap(pairs_up, pairs_down):
        return [(i, i ^ (1 << (pairs_down if i % 2 else pairs_up))) for i in range(n)]

    for r in range(nbits):
        last = r == nbits - 1
        dim = 0 if last else nbits - 1 - r
        keep = lax.index_in_dim(held, 0, dim, keepdims=False)
        away = lax.index_in_dim(held, 1, dim, keepdims=False)
        if last:
            pairs = [(i, i ^ 1) for i in range(n)]
        else:
            pairs = swap(up[r], down[r])
        if 2 * bot == cols:
            flat_feats = feats.reshape(-1, 2 * bot)
            payload = jnp.concatenate([flat_feats, away.reshape(-1, cols)], axis=0)
            got = lax.ppermute(payload, "dp", pairs)
            got_feats = got[: flat_feats.shape[0]].reshape(feats.shape)
            got_held = got[flat_feats.shape[0]:].reshape(away.shape)
        else:
            got_feats, got_held = lax.ppermute((feats, away), "dp", pairs)
        if last:
            got_feats = jnp.transpose(got_feats, cross_rev + [nbits - 1, nbits])
            got_held = jnp.transpose(got_held, cross_rev + [nbits - 1, nbits])
        feats = jnp.stack([feats, got_feats])
        held = jnp.stack([keep, got_held], axis=dim)
    feats = feats.reshape(-1, 2 * bot)
    src = me ^ pos
    where = src & 1
    for d, bit in enumerate(dim_bits):
        where = (where << 1) | ((src >> bit) & 1)
    held = jnp.take(held.reshape(n, 2 * rows, cols), where, axis=0)
    sw = held[:, :rows].reshape(n * rows, cols)
    tw = held[:, rows:].reshape(n * rows, cols)
    zt, zs = feats[:, :bot], feats[:, bot:]
    c = lax.dynamic_slice_in_dim(center, me * cols, cols)
    t_norm = jnp.sqrt(jnp.sum(jnp.square(tw.astype(jnp.float32)), 0) + 1e-06)
    s_norm = jnp.sqrt(jnp.sum(jnp.square(sw.astype(jnp.float32)), 0) + 1e-06)
    t_cos = jnp.dot(zt, tw, preferred_element_type=jnp.float32) / t_norm
    s_cos = jnp.dot(zs, sw, preferred_element_type=jnp.float32) / s_norm
    t_exp = jnp.exp((t_cos - c) / 0.04)
    s_exp = jnp.exp(s_cos / 0.1)
    totals = jnp.stack([jnp.sum(t_exp, 1), jnp.sum(s_exp, 1)])
    t_exp, s_exp = lax.optimization_barrier((t_exp.astype(jnp.bfloat16), s_exp.astype(jnp.bfloat16)))
    t_exp, s_exp = t_exp.astype(jnp.float32), s_exp.astype(jnp.float32)
    shape = (2,) + (2,) * nbits + (images,)
    for r in range(nbits):
        if r == nbits - 1:
            got = lax.ppermute(totals, "dp", [(i, i ^ 1) for i in range(n)]).reshape(shape)
            got = jnp.flip(jnp.transpose(got, [0, 1] + [2 + d for d in cross_rev] + [nbits + 1]), 1)
        else:
            got = lax.ppermute(totals, "dp", swap(up[r], down[r])).reshape(shape)
            got = jnp.flip(got, nbits - r)
        totals = totals + got.reshape(totals.shape)
    totals = exchange_all(totals, "tensor", lax.axis_size("tensor"))
    t_total, s_total = totals[0][:, None], totals[1][:, None]
    part_center = 0.5 * c + 0.5 * (jnp.sum(t_cos, 0) / (images * n))
    dlog = ((s_exp / s_total - t_exp / t_total) / 0.1).astype(jnp.bfloat16)
    product = lax.dot_general(
        zs, dlog, (((0,), (0,)), ((), ())), preferred_element_type=jnp.float32
    )
    wide = sw.astype(jnp.float32)
    scaled = jnp.sum(wide * product, 0) / s_norm / s_norm
    grad = (product - wide * scaled) / s_norm
    high = part_center.astype(jnp.bfloat16)
    low = (part_center - high.astype(jnp.float32)).astype(jnp.bfloat16)
    sent = jnp.concatenate(
        [
            grad.astype(jnp.bfloat16).reshape(n, rows, cols),
            jnp.broadcast_to(jnp.stack([high, low]), (n, 2, cols)),
        ],
        axis=1,
    )
    got = lax.all_to_all(sent, "dp", 0, 2, tiled=True)
    got = got.reshape(rows + 2, n * cols).astype(jnp.float32)
    return (master_new, got[:rows], got[rows] + got[rows + 1])


def solution(mesh):
    placed = (P("dp", "tensor"), P("dp", "tensor"), P("dp", None), P("dp", None), P("tensor"))
    return jax.shard_map(
        shards_for(mesh),
        mesh=mesh,
        in_specs=placed,
        out_specs=(P("dp", "tensor"), P("dp", "tensor"), P("tensor")),
        check_vma=False,
    )


def shards_for(mesh):
    ndp = mesh.shape["dp"]

    def shards(teacher_master, student_weight, teacher_feat, student_feat, center):
        images_all = teacher_feat.shape[0] * ndp
        cols = center.shape[0]
        if images_all < cols and cols % ndp == 0 and ndp > 1 and ndp & (ndp - 1) == 0:
            return feature_plan(teacher_master, student_weight, teacher_feat, student_feat, center)
        return weight_plan(teacher_master, student_weight, teacher_feat, student_feat, center)

    return shards
```

```python
import jax
import jax.numpy as jnp
from jax import lax
from jax.sharding import PartitionSpec as P


def unit_rows(feat):
    wide = feat.astype(jnp.float32)
    return (wide * lax.rsqrt(jnp.sum(wide * wide, 1, keepdims=True) + 1e-06)).astype(jnp.bfloat16)


def weight_plan(teacher_master, student_weight, teacher_feat, student_feat, center):
    zt = unit_rows(teacher_feat)
    zs = unit_rows(student_feat)
    images_all = teacher_feat.shape[0] * lax.axis_size("dp")
    student_full = lax.all_gather(student_weight, "dp", axis=0, tiled=True)
    master_new = 0.996 * teacher_master + 0.004 * student_weight.astype(jnp.float32)
    weight = lax.all_gather(master_new.astype(jnp.bfloat16), "dp", axis=0, tiled=True)
    raw = jnp.dot(zt, weight, preferred_element_type=jnp.float32)
    t_norm = jnp.sqrt(jnp.sum(jnp.square(weight.astype(jnp.float32)), 0) + 1e-06)
    t_cos = raw / t_norm
    s_norm = jnp.sqrt(jnp.sum(jnp.square(student_full.astype(jnp.float32)), 0) + 1e-06)
    s_cos = jnp.dot(zs, student_full, preferred_element_type=jnp.float32) / s_norm
    t_exp = jnp.exp((t_cos - center) / 0.04)
    s_exp = jnp.exp(s_cos / 0.1)
    t_total, s_total = lax.psum(
        (jnp.sum(t_exp, 1, keepdims=True), jnp.sum(s_exp, 1, keepdims=True)), "tensor"
    )
    cos_mean = lax.psum(jnp.sum(t_cos, 0), "dp") / images_all
    new_center = 0.5 * center + 0.5 * cos_mean
    dlog = ((s_exp / s_total - t_exp / t_total) / 0.1).astype(jnp.bfloat16)
    scaled = jnp.sum(dlog.astype(jnp.float32) * s_cos, 0) / s_norm
    product = lax.dot_general(
        zs, dlog, (((0,), (0,)), ((), ())), preferred_element_type=jnp.float32
    )
    student_grad = lax.psum_scatter(
        (product - student_full.astype(jnp.float32) * scaled) / s_norm,
        "dp",
        scatter_dimension=0,
        tiled=True,
    )
    return (master_new, student_grad, new_center)


def exchange_sum(x, axis, n):
    if n & (n - 1):
        return lax.psum(x, axis)
    step = 1
    while step < n:
        x = x + lax.ppermute(x, axis, [(i, i ^ step) for i in range(n)])
        step *= 2
    return x


def exchange_all(x, axis, n):
    total = x
    for k in range(1, n):
        total = total + lax.ppermute(x, axis, [(i, (i + k) % n) for i in range(n)])
    return total


def feature_plan(teacher_master, student_weight, teacher_feat, student_feat, center):
    n = lax.axis_size("dp")
    me = lax.axis_index("dp")
    rows, width = teacher_master.shape
    bot = teacher_feat.shape[1]
    images = teacher_feat.shape[0]
    cols = width // n
    nbits = n.bit_length() - 1
    odd = me % 2
    up = list(range(1, nbits))
    down = up[::-1]
    dim_bits = [jnp.where(odd == 1, down[r], up[r]) for r in range(nbits - 1)][::-1]
    master_new = 0.996 * teacher_master + 0.004 * student_weight.astype(jnp.float32)
    both = jnp.stack([student_weight, master_new.astype(jnp.bfloat16)])
    both = both.reshape(2, rows, n, cols).transpose(2, 0, 1, 3).reshape(n, 2 * rows, cols)
    pos = jnp.arange(n)
    rel = (pos >> (nbits - 1)) & 1
    for d, bit in enumerate(dim_bits):
        rel = rel | (((pos >> (nbits - 2 - d)) & 1) << bit)
    held = jnp.take(both, me ^ rel, axis=0).reshape((2,) * nbits + (2 * rows, cols))
    feats = jnp.concatenate([unit_rows(teacher_feat), unit_rows(student_feat)], axis=1)
    cross_rev = list(range(nbits - 2, -1, -1))

    def swap(pairs_up, pairs_down):
        return [(i, i ^ (1 << (pairs_down if i % 2 else pairs_up))) for i in range(n)]

    for r in range(nbits):
        last = r == nbits - 1
        dim = 0 if last else nbits - 1 - r
        keep = lax.index_in_dim(held, 0, dim, keepdims=False)
        away = lax.index_in_dim(held, 1, dim, keepdims=False)
        if last:
            pairs = [(i, i ^ 1) for i in range(n)]
        else:
            pairs = swap(up[r], down[r])
        if 2 * bot == cols:
            flat_feats = feats.reshape(-1, 2 * bot)
            payload = jnp.concatenate([flat_feats, away.reshape(-1, cols)], axis=0)
            got = lax.ppermute(payload, "dp", pairs)
            got_feats = got[: flat_feats.shape[0]].reshape(feats.shape)
            got_held = got[flat_feats.shape[0]:].reshape(away.shape)
        else:
            got_feats, got_held = lax.ppermute((feats, away), "dp", pairs)
        if last:
            got_feats = jnp.transpose(got_feats, cross_rev + [nbits - 1, nbits])
            got_held = jnp.transpose(got_held, cross_rev + [nbits - 1, nbits])
        feats = jnp.stack([feats, got_feats])
        held = jnp.stack([keep, got_held], axis=dim)
    feats = feats.reshape(-1, 2 * bot)
    src = me ^ pos
    where = src & 1
    for d, bit in enumerate(dim_bits):
        where = (where << 1) | ((src >> bit) & 1)
    held = jnp.take(held.reshape(n, 2 * rows, cols), where, axis=0)
    sw = held[:, :rows].reshape(n * rows, cols)
    tw = held[:, rows:].reshape(n * rows, cols)
    zt, zs = feats[:, :bot], feats[:, bot:]
    c = lax.dynamic_slice_in_dim(center, me * cols, cols)
    t_norm = jnp.sqrt(jnp.sum(jnp.square(tw.astype(jnp.float32)), 0) + 1e-06)
    s_norm = jnp.sqrt(jnp.sum(jnp.square(sw.astype(jnp.float32)), 0) + 1e-06)
    t_cos = jnp.dot(zt, tw, preferred_element_type=jnp.float32) / t_norm
    s_cos = jnp.dot(zs, sw, preferred_element_type=jnp.float32) / s_norm
    t_exp = jnp.exp((t_cos - c) / 0.04)
    s_exp = jnp.exp(s_cos / 0.1)
    totals = jnp.stack([jnp.sum(t_exp, 1), jnp.sum(s_exp, 1)])
    t_exp, s_exp = lax.optimization_barrier((t_exp.astype(jnp.bfloat16), s_exp.astype(jnp.bfloat16)))
    t_exp, s_exp = t_exp.astype(jnp.float32), s_exp.astype(jnp.float32)
    shape = (2,) + (2,) * nbits + (images,)
    for r in range(nbits):
        if r == nbits - 1:
            got = lax.ppermute(totals, "dp", [(i, i ^ 1) for i in range(n)]).reshape(shape)
            got = jnp.flip(jnp.transpose(got, [0, 1] + [2 + d for d in cross_rev] + [nbits + 1]), 1)
        else:
            got = lax.ppermute(totals, "dp", swap(up[r], down[r])).reshape(shape)
            got = jnp.flip(got, nbits - r)
        totals = totals + got.reshape(totals.shape)
    totals = exchange_all(totals, "tensor", lax.axis_size("tensor"))
    t_total, s_total = totals[0][:, None], totals[1][:, None]
    part_center = 0.5 * c + 0.5 * (jnp.sum(t_cos, 0) / (images * n))
    dlog = ((s_exp / s_total - t_exp / t_total) / 0.1).astype(jnp.bfloat16)
    product = lax.dot_general(
        zs, dlog, (((0,), (0,)), ((), ())), preferred_element_type=jnp.float32
    )
    wide = sw.astype(jnp.float32)
    scaled = jnp.sum(wide * product, 0) / s_norm / s_norm
    grad = (product - wide * scaled) / s_norm
    high = part_center.astype(jnp.bfloat16)
    low = (part_center - high.astype(jnp.float32)).astype(jnp.bfloat16)
    lanes = 128 if (rows * cols) % 128 == 0 and (2 * cols) % 128 == 0 else cols
    grad_rows = rows * cols // lanes
    sent = jnp.concatenate(
        [
            grad.astype(jnp.bfloat16).reshape(n, grad_rows, lanes),
            jnp.broadcast_to(jnp.stack([high, low]), (n, 2, cols)).reshape(n, -1, lanes),
        ],
        axis=1,
    )
    got = lax.all_to_all(sent, "dp", 0, 0, tiled=True)
    student_grad = got[:, :grad_rows].reshape(n, rows, cols).transpose(1, 0, 2)
    student_grad = student_grad.reshape(rows, n * cols).astype(jnp.float32)
    parts = got[:, grad_rows:].reshape(n, 2, cols).astype(jnp.float32)
    return (master_new, student_grad, (parts[:, 0] + parts[:, 1]).reshape(n * cols))


def solution(mesh):
    placed = (P("dp", "tensor"), P("dp", "tensor"), P("dp", None), P("dp", None), P("tensor"))
    return jax.shard_map(
        shards_for(mesh),
        mesh=mesh,
        in_specs=placed,
        out_specs=(P("dp", "tensor"), P("dp", "tensor"), P("tensor")),
        check_vma=False,
    )


def shards_for(mesh):
    ndp = mesh.shape["dp"]

    def shards(teacher_master, student_weight, teacher_feat, student_feat, center):
        images_all = teacher_feat.shape[0] * ndp
        cols = center.shape[0]
        if images_all < cols and cols % ndp == 0 and ndp > 1 and ndp & (ndp - 1) == 0:
            return feature_plan(teacher_master, student_weight, teacher_feat, student_feat, center)
        return weight_plan(teacher_master, student_weight, teacher_feat, student_feat, center)

    return shards
```

```python
import jax
import jax.numpy as jnp
from jax import lax
from jax.sharding import PartitionSpec as P


def unit_rows(feat):
    wide = feat.astype(jnp.float32)
    return (wide * lax.rsqrt(jnp.sum(wide * wide, 1, keepdims=True) + 1e-06)).astype(jnp.bfloat16)


def weight_plan(teacher_master, student_weight, teacher_feat, student_feat, center):
    zt = unit_rows(teacher_feat)
    zs = unit_rows(student_feat)
    images_all = teacher_feat.shape[0] * lax.axis_size("dp")
    student_full = lax.all_gather(student_weight, "dp", axis=0, tiled=True)
    master_new = 0.996 * teacher_master + 0.004 * student_weight.astype(jnp.float32)
    weight = lax.all_gather(master_new.astype(jnp.bfloat16), "dp", axis=0, tiled=True)
    raw = jnp.dot(zt, weight, preferred_element_type=jnp.float32)
    t_norm = jnp.sqrt(jnp.sum(jnp.square(weight.astype(jnp.float32)), 0) + 1e-06)
    t_cos = raw / t_norm
    s_norm = jnp.sqrt(jnp.sum(jnp.square(student_full.astype(jnp.float32)), 0) + 1e-06)
    s_cos = jnp.dot(zs, student_full, preferred_element_type=jnp.float32) / s_norm
    t_exp = jnp.exp((t_cos - center) / 0.04)
    s_exp = jnp.exp(s_cos / 0.1)
    t_total, s_total = lax.psum(
        (jnp.sum(t_exp, 1, keepdims=True), jnp.sum(s_exp, 1, keepdims=True)), "tensor"
    )
    cos_mean = lax.psum(jnp.sum(t_cos, 0), "dp") / images_all
    new_center = 0.5 * center + 0.5 * cos_mean
    dlog = ((s_exp / s_total - t_exp / t_total) / 0.1).astype(jnp.bfloat16)
    scaled = jnp.sum(dlog.astype(jnp.float32) * s_cos, 0) / s_norm
    product = lax.dot_general(
        zs, dlog, (((0,), (0,)), ((), ())), preferred_element_type=jnp.float32
    )
    student_grad = lax.psum_scatter(
        (product - student_full.astype(jnp.float32) * scaled) / s_norm,
        "dp",
        scatter_dimension=0,
        tiled=True,
    )
    return (master_new, student_grad, new_center)


def exchange_sum(x, axis, n):
    if n & (n - 1):
        return lax.psum(x, axis)
    step = 1
    while step < n:
        x = x + lax.ppermute(x, axis, [(i, i ^ step) for i in range(n)])
        step *= 2
    return x


def exchange_all(x, axis, n):
    total = x
    for k in range(1, n):
        total = total + lax.ppermute(x, axis, [(i, (i + k) % n) for i in range(n)])
    return total


def feature_plan(teacher_master, student_weight, teacher_feat, student_feat, center):
    n = lax.axis_size("dp")
    me = lax.axis_index("dp")
    rows, width = teacher_master.shape
    bot = teacher_feat.shape[1]
    images = teacher_feat.shape[0]
    cols = width // n
    nbits = n.bit_length() - 1
    odd = me % 2
    up = list(range(1, nbits))
    down = up[::-1]
    dim_bits = [jnp.where(odd == 1, down[r], up[r]) for r in range(nbits - 1)][::-1]
    master_new = 0.996 * teacher_master + 0.004 * student_weight.astype(jnp.float32)
    both = jnp.stack([student_weight, master_new.astype(jnp.bfloat16)])
    both = both.reshape(2, rows, n, cols).transpose(2, 0, 1, 3).reshape(n, 2 * rows, cols)
    pos = jnp.arange(n)
    rel = (pos >> (nbits - 1)) & 1
    for d, bit in enumerate(dim_bits):
        rel = rel | (((pos >> (nbits - 2 - d)) & 1) << bit)
    held = jnp.take(both, me ^ rel, axis=0).reshape((2,) * nbits + (2 * rows, cols))
    feats = jnp.concatenate([unit_rows(teacher_feat), unit_rows(student_feat)], axis=1)
    cross_rev = list(range(nbits - 2, -1, -1))

    def swap(pairs_up, pairs_down):
        return [(i, i ^ (1 << (pairs_down if i % 2 else pairs_up))) for i in range(n)]

    for r in range(nbits):
        last = r == nbits - 1
        dim = 0 if last else nbits - 1 - r
        keep = lax.index_in_dim(held, 0, dim, keepdims=False)
        away = lax.index_in_dim(held, 1, dim, keepdims=False)
        if last:
            pairs = [(i, i ^ 1) for i in range(n)]
        else:
            pairs = swap(up[r], down[r])
        if 2 * bot == cols:
            flat_feats = feats.reshape(-1, 2 * bot)
            payload = jnp.concatenate([flat_feats, away.reshape(-1, cols)], axis=0)
            got = lax.ppermute(payload, "dp", pairs)
            got_feats = got[: flat_feats.shape[0]].reshape(feats.shape)
            got_held = got[flat_feats.shape[0]:].reshape(away.shape)
        else:
            got_feats, got_held = lax.ppermute((feats, away), "dp", pairs)
        if last:
            got_feats = jnp.transpose(got_feats, cross_rev + [nbits - 1, nbits])
            got_held = jnp.transpose(got_held, cross_rev + [nbits - 1, nbits])
        feats = jnp.stack([feats, got_feats])
        held = jnp.stack([keep, got_held], axis=dim)
    feats = feats.reshape(-1, 2 * bot)
    src = me ^ pos
    where = src & 1
    for d, bit in enumerate(dim_bits):
        where = (where << 1) | ((src >> bit) & 1)
    held = jnp.take(held.reshape(n, 2 * rows, cols), where, axis=0)
    sw = held[:, :rows].reshape(n * rows, cols)
    tw = held[:, rows:].reshape(n * rows, cols)
    zt, zs = feats[:, :bot], feats[:, bot:]
    c = lax.dynamic_slice_in_dim(center, me * cols, cols)
    t_norm = jnp.sqrt(jnp.sum(jnp.square(tw.astype(jnp.float32)), 0) + 1e-06)
    s_norm = jnp.sqrt(jnp.sum(jnp.square(sw.astype(jnp.float32)), 0) + 1e-06)
    t_cos = jnp.dot(zt, tw, preferred_element_type=jnp.float32) / t_norm
    s_cos = jnp.dot(zs, sw, preferred_element_type=jnp.float32) / s_norm
    t_exp = jnp.exp((t_cos - c) / 0.04)
    s_exp = jnp.exp(s_cos / 0.1)
    totals = jnp.stack([jnp.sum(t_exp, 1), jnp.sum(s_exp, 1)])
    t_exp, s_exp = lax.optimization_barrier((t_exp.astype(jnp.bfloat16), s_exp.astype(jnp.bfloat16)))
    t_exp, s_exp = t_exp.astype(jnp.float32), s_exp.astype(jnp.float32)
    shape = (2,) + (2,) * nbits + (images,)
    for r in range(nbits):
        if r == nbits - 1:
            got = lax.ppermute(totals, "dp", [(i, i ^ 1) for i in range(n)]).reshape(shape)
            got = jnp.flip(jnp.transpose(got, [0, 1] + [2 + d for d in cross_rev] + [nbits + 1]), 1)
        else:
            got = lax.ppermute(totals, "dp", swap(up[r], down[r])).reshape(shape)
            got = jnp.flip(got, nbits - r)
        totals = totals + got.reshape(totals.shape)
    totals = exchange_all(totals, "tensor", lax.axis_size("tensor"))
    t_total, s_total = totals[0][:, None], totals[1][:, None]
    part_center = 0.5 * c + 0.5 * (jnp.sum(t_cos, 0) / (images * n))
    dlog = ((s_exp / s_total - t_exp / t_total) / 0.1).astype(jnp.bfloat16)
    product = lax.dot_general(
        zs, dlog, (((0,), (0,)), ((), ())), preferred_element_type=jnp.float32
    )
    wide = sw.astype(jnp.float32)
    scaled = jnp.sum(wide * product, 0) / s_norm / s_norm
    grad = (product - wide * scaled) / s_norm
    high = part_center.astype(jnp.bfloat16)
    low = (part_center - high.astype(jnp.float32)).astype(jnp.bfloat16)
    lanes = 128 if (rows * cols) % 128 == 0 and (2 * cols) % 128 == 0 else cols
    grad_rows = rows * cols // lanes
    sent = jnp.concatenate(
        [
            grad.astype(jnp.bfloat16).reshape(n, grad_rows, lanes),
            jnp.broadcast_to(jnp.stack([high, low]), (n, 2, cols)).reshape(n, -1, lanes),
        ],
        axis=1,
    )
    got = lax.all_to_all(sent, "dp", 0, 0, tiled=True)
    student_grad = got[:, :grad_rows].reshape(n, rows, cols).transpose(1, 0, 2)
    student_grad = student_grad.reshape(rows, n * cols).astype(jnp.float32)
    half = cols // lanes
    high = got[:, grad_rows: grad_rows + half].astype(jnp.float32)
    low = got[:, grad_rows + half:].astype(jnp.float32)
    return (master_new, student_grad, (high + low).reshape(n * cols))


def solution(mesh):
    placed = (P("dp", "tensor"), P("dp", "tensor"), P("dp", None), P("dp", None), P("tensor"))
    return jax.shard_map(
        shards_for(mesh),
        mesh=mesh,
        in_specs=placed,
        out_specs=(P("dp", "tensor"), P("dp", "tensor"), P("tensor")),
        check_vma=False,
    )


def shards_for(mesh):
    ndp = mesh.shape["dp"]

    def shards(teacher_master, student_weight, teacher_feat, student_feat, center):
        images_all = teacher_feat.shape[0] * ndp
        cols = center.shape[0]
        if images_all < cols and cols % ndp == 0 and ndp > 1 and ndp & (ndp - 1) == 0:
            return feature_plan(teacher_master, student_weight, teacher_feat, student_feat, center)
        return weight_plan(teacher_master, student_weight, teacher_feat, student_feat, center)

    return shards
```

```python
import jax
import jax.numpy as jnp
from jax import lax
from jax.sharding import PartitionSpec as P


def unit_rows(feat):
    wide = feat.astype(jnp.float32)
    return (wide * lax.rsqrt(jnp.sum(wide * wide, 1, keepdims=True) + 1e-06)).astype(jnp.bfloat16)


def weight_plan(teacher_master, student_weight, teacher_feat, student_feat, center):
    zt = unit_rows(teacher_feat)
    zs = unit_rows(student_feat)
    images_all = teacher_feat.shape[0] * lax.axis_size("dp")
    student_full = lax.all_gather(student_weight, "dp", axis=0, tiled=True)
    master_new = 0.996 * teacher_master + 0.004 * student_weight.astype(jnp.float32)
    weight = lax.all_gather(master_new.astype(jnp.bfloat16), "dp", axis=0, tiled=True)
    raw = jnp.dot(zt, weight, preferred_element_type=jnp.float32)
    t_norm = jnp.sqrt(jnp.sum(jnp.square(weight.astype(jnp.float32)), 0) + 1e-06)
    t_cos = raw / t_norm
    s_norm = jnp.sqrt(jnp.sum(jnp.square(student_full.astype(jnp.float32)), 0) + 1e-06)
    s_cos = jnp.dot(zs, student_full, preferred_element_type=jnp.float32) / s_norm
    t_exp = jnp.exp((t_cos - center) / 0.04)
    s_exp = jnp.exp(s_cos / 0.1)
    t_total, s_total = lax.psum(
        (jnp.sum(t_exp, 1, keepdims=True), jnp.sum(s_exp, 1, keepdims=True)), "tensor"
    )
    cos_mean = lax.psum(jnp.sum(t_cos, 0), "dp") / images_all
    new_center = 0.5 * center + 0.5 * cos_mean
    dlog = ((s_exp / s_total - t_exp / t_total) / 0.1).astype(jnp.bfloat16)
    scaled = jnp.sum(dlog.astype(jnp.float32) * s_cos, 0) / s_norm
    product = lax.dot_general(
        zs, dlog, (((0,), (0,)), ((), ())), preferred_element_type=jnp.float32
    )
    student_grad = lax.psum_scatter(
        (product - student_full.astype(jnp.float32) * scaled) / s_norm,
        "dp",
        scatter_dimension=0,
        tiled=True,
    )
    return (master_new, student_grad, new_center)


def exchange_sum(x, axis, n):
    if n & (n - 1):
        return lax.psum(x, axis)
    step = 1
    while step < n:
        x = x + lax.ppermute(x, axis, [(i, i ^ step) for i in range(n)])
        step *= 2
    return x


def exchange_all(x, axis, n):
    total = x
    for k in range(1, n):
        total = total + lax.ppermute(x, axis, [(i, (i + k) % n) for i in range(n)])
    return total


def feature_plan(teacher_master, student_weight, teacher_feat, student_feat, center):
    n = lax.axis_size("dp")
    me = lax.axis_index("dp")
    rows, width = teacher_master.shape
    bot = teacher_feat.shape[1]
    images = teacher_feat.shape[0]
    cols = width // n
    nbits = n.bit_length() - 1
    odd = me % 2
    up = list(range(1, nbits))
    down = up[::-1]
    dim_bits = [jnp.where(odd == 1, down[r], up[r]) for r in range(nbits - 1)][::-1]
    master_new = 0.996 * teacher_master + 0.004 * student_weight.astype(jnp.float32)
    both = jnp.stack([student_weight, master_new.astype(jnp.bfloat16)])
    both = both.reshape(2, rows, n, cols).transpose(2, 0, 1, 3).reshape(n, 2 * rows, cols)
    pos = jnp.arange(n)
    rel = (pos >> (nbits - 1)) & 1
    for d, bit in enumerate(dim_bits):
        rel = rel | (((pos >> (nbits - 2 - d)) & 1) << bit)
    held = jnp.take(both, me ^ rel, axis=0).reshape((2,) * nbits + (2 * rows, cols))
    feats = jnp.concatenate([unit_rows(teacher_feat), unit_rows(student_feat)], axis=1)
    cross_rev = list(range(nbits - 2, -1, -1))

    def swap(pairs_up, pairs_down):
        return [(i, i ^ (1 << (pairs_down if i % 2 else pairs_up))) for i in range(n)]

    for r in range(nbits):
        last = r == nbits - 1
        dim = 0 if last else nbits - 1 - r
        keep = lax.index_in_dim(held, 0, dim, keepdims=False)
        away = lax.index_in_dim(held, 1, dim, keepdims=False)
        if last:
            pairs = [(i, i ^ 1) for i in range(n)]
        else:
            pairs = swap(up[r], down[r])
        if 2 * bot == cols:
            flat_feats = feats.reshape(-1, 2 * bot)
            payload = jnp.concatenate([flat_feats, away.reshape(-1, cols)], axis=0)
            got = lax.ppermute(payload, "dp", pairs)
            got_feats = got[: flat_feats.shape[0]].reshape(feats.shape)
            got_held = got[flat_feats.shape[0]:].reshape(away.shape)
        else:
            got_feats, got_held = lax.ppermute((feats, away), "dp", pairs)
        if last:
            got_feats = jnp.transpose(got_feats, cross_rev + [nbits - 1, nbits])
            got_held = jnp.transpose(got_held, cross_rev + [nbits - 1, nbits])
        feats = jnp.stack([feats, got_feats])
        held = jnp.stack([keep, got_held], axis=dim)
    feats = feats.reshape(-1, 2 * bot)
    src = me ^ pos
    where = src & 1
    for d, bit in enumerate(dim_bits):
        where = (where << 1) | ((src >> bit) & 1)
    held = jnp.take(held.reshape(n, 2 * rows, cols), where, axis=0)
    sw = held[:, :rows].reshape(n * rows, cols)
    tw = held[:, rows:].reshape(n * rows, cols)
    zt, zs = feats[:, :bot], feats[:, bot:]
    c = lax.dynamic_slice_in_dim(center, me * cols, cols)
    t_norm = jnp.sqrt(jnp.sum(jnp.square(tw.astype(jnp.float32)), 0) + 1e-06)
    s_norm = jnp.sqrt(jnp.sum(jnp.square(sw.astype(jnp.float32)), 0) + 1e-06)
    t_cos = jnp.dot(zt, tw, preferred_element_type=jnp.float32) / t_norm
    s_cos = jnp.dot(zs, sw, preferred_element_type=jnp.float32) / s_norm
    t_exp = jnp.exp((t_cos - c) / 0.04)
    s_exp = jnp.exp(s_cos / 0.1)
    totals = jnp.stack([jnp.sum(t_exp, 1), jnp.sum(s_exp, 1)])
    t_exp, s_exp = lax.optimization_barrier((t_exp.astype(jnp.bfloat16), s_exp.astype(jnp.bfloat16)))
    t_exp, s_exp = t_exp.astype(jnp.float32), s_exp.astype(jnp.float32)
    shape = (2,) + (2,) * nbits + (images,)
    for r in range(nbits):
        if r == nbits - 1:
            got = lax.ppermute(totals, "dp", [(i, i ^ 1) for i in range(n)]).reshape(shape)
            got = jnp.flip(jnp.transpose(got, [0, 1] + [2 + d for d in cross_rev] + [nbits + 1]), 1)
        else:
            got = lax.ppermute(totals, "dp", swap(up[r], down[r])).reshape(shape)
            got = jnp.flip(got, nbits - r)
        totals = totals + got.reshape(totals.shape)
    width_t = lax.axis_size("tensor")
    spread = jnp.broadcast_to(totals[None], (width_t,) + totals.shape)
    totals = jnp.sum(lax.all_to_all(spread, "tensor", 0, 0, tiled=True), 0)
    t_total, s_total = totals[0][:, None], totals[1][:, None]
    part_center = 0.5 * c + 0.5 * (jnp.sum(t_cos, 0) / (images * n))
    dlog = ((s_exp / s_total - t_exp / t_total) / 0.1).astype(jnp.bfloat16)
    product = lax.dot_general(
        zs, dlog, (((0,), (0,)), ((), ())), preferred_element_type=jnp.float32
    )
    wide = sw.astype(jnp.float32)
    scaled = jnp.sum(wide * product, 0) / s_norm / s_norm
    grad = (product - wide * scaled) / s_norm
    high = part_center.astype(jnp.bfloat16)
    low = (part_center - high.astype(jnp.float32)).astype(jnp.bfloat16)
    lanes = 128 if (rows * cols) % 128 == 0 and (2 * cols) % 128 == 0 else cols
    grad_rows = rows * cols // lanes
    sent = jnp.concatenate(
        [
            grad.astype(jnp.bfloat16).reshape(n, grad_rows, lanes),
            jnp.broadcast_to(jnp.stack([high, low]), (n, 2, cols)).reshape(n, -1, lanes),
        ],
        axis=1,
    )
    got = lax.all_to_all(sent, "dp", 0, 0, tiled=True)
    student_grad = got[:, :grad_rows].reshape(n, rows, cols).transpose(1, 0, 2)
    student_grad = student_grad.reshape(rows, n * cols).astype(jnp.float32)
    half = cols // lanes
    high = got[:, grad_rows: grad_rows + half].astype(jnp.float32)
    low = got[:, grad_rows + half:].astype(jnp.float32)
    return (master_new, student_grad, (high + low).reshape(n * cols))


def solution(mesh):
    placed = (P("dp", "tensor"), P("dp", "tensor"), P("dp", None), P("dp", None), P("tensor"))
    return jax.shard_map(
        shards_for(mesh),
        mesh=mesh,
        in_specs=placed,
        out_specs=(P("dp", "tensor"), P("dp", "tensor"), P("tensor")),
        check_vma=False,
    )


def shards_for(mesh):
    ndp = mesh.shape["dp"]

    def shards(teacher_master, student_weight, teacher_feat, student_feat, center):
        images_all = teacher_feat.shape[0] * ndp
        cols = center.shape[0]
        if images_all < cols and cols % ndp == 0 and ndp > 1 and ndp & (ndp - 1) == 0:
            return feature_plan(teacher_master, student_weight, teacher_feat, student_feat, center)
        return weight_plan(teacher_master, student_weight, teacher_feat, student_feat, center)

    return shards
```

```python
import jax
import jax.numpy as jnp
from jax import lax
from jax.sharding import PartitionSpec as P


def unit_rows(feat):
    wide = feat.astype(jnp.float32)
    return (wide * lax.rsqrt(jnp.sum(wide * wide, 1, keepdims=True) + 1e-06)).astype(jnp.bfloat16)


def weight_plan(teacher_master, student_weight, teacher_feat, student_feat, center):
    zt = unit_rows(teacher_feat)
    zs = unit_rows(student_feat)
    images_all = teacher_feat.shape[0] * lax.axis_size("dp")
    student_full = lax.all_gather(student_weight, "dp", axis=0, tiled=True)
    master_new = 0.996 * teacher_master + 0.004 * student_weight.astype(jnp.float32)
    weight = lax.all_gather(master_new.astype(jnp.bfloat16), "dp", axis=0, tiled=True)
    raw = jnp.dot(zt, weight, preferred_element_type=jnp.float32)
    t_norm = jnp.sqrt(jnp.sum(jnp.square(weight.astype(jnp.float32)), 0) + 1e-06)
    t_cos = raw / t_norm
    s_norm = jnp.sqrt(jnp.sum(jnp.square(student_full.astype(jnp.float32)), 0) + 1e-06)
    s_cos = jnp.dot(zs, student_full, preferred_element_type=jnp.float32) / s_norm
    t_exp = jnp.exp((t_cos - center) / 0.04)
    s_exp = jnp.exp(s_cos / 0.1)
    t_total, s_total = lax.psum(
        (jnp.sum(t_exp, 1, keepdims=True), jnp.sum(s_exp, 1, keepdims=True)), "tensor"
    )
    cos_mean = lax.psum(jnp.sum(t_cos, 0), "dp") / images_all
    new_center = 0.5 * center + 0.5 * cos_mean
    dlog = ((s_exp / s_total - t_exp / t_total) / 0.1).astype(jnp.bfloat16)
    scaled = jnp.sum(dlog.astype(jnp.float32) * s_cos, 0) / s_norm
    product = lax.dot_general(
        zs, dlog, (((0,), (0,)), ((), ())), preferred_element_type=jnp.float32
    )
    student_grad = lax.psum_scatter(
        (product - student_full.astype(jnp.float32) * scaled) / s_norm,
        "dp",
        scatter_dimension=0,
        tiled=True,
    )
    return (master_new, student_grad, new_center)


def exchange_sum(x, axis, n):
    if n & (n - 1):
        return lax.psum(x, axis)
    step = 1
    while step < n:
        x = x + lax.ppermute(x, axis, [(i, i ^ step) for i in range(n)])
        step *= 2
    return x


def exchange_all(x, axis, n):
    total = x
    for k in range(1, n):
        total = total + lax.ppermute(x, axis, [(i, (i + k) % n) for i in range(n)])
    return total


def feature_plan(teacher_master, student_weight, teacher_feat, student_feat, center):
    n = lax.axis_size("dp")
    me = lax.axis_index("dp")
    rows, width = teacher_master.shape
    bot = teacher_feat.shape[1]
    images = teacher_feat.shape[0]
    cols = width // n
    nbits = n.bit_length() - 1
    odd = me % 2
    up = list(range(1, nbits))
    down = up[::-1]
    dim_bits = [jnp.where(odd == 1, down[r], up[r]) for r in range(nbits - 1)][::-1]
    rebuilt = 0.996 * teacher_master + 0.004 * student_weight.astype(jnp.float32)
    both = jnp.stack([student_weight, rebuilt.astype(jnp.bfloat16)])
    both = both.reshape(2, rows, n, cols).transpose(2, 0, 1, 3).reshape(n, 2 * rows, cols)
    pos = jnp.arange(n)
    rel = (pos >> (nbits - 1)) & 1
    for d, bit in enumerate(dim_bits):
        rel = rel | (((pos >> (nbits - 2 - d)) & 1) << bit)
    held = jnp.take(both, me ^ rel, axis=0).reshape((2,) * nbits + (2 * rows, cols))
    feats = jnp.concatenate([unit_rows(teacher_feat), unit_rows(student_feat)], axis=1)
    cross_rev = list(range(nbits - 2, -1, -1))

    def swap(pairs_up, pairs_down):
        return [(i, i ^ (1 << (pairs_down if i % 2 else pairs_up))) for i in range(n)]

    for r in range(nbits):
        last = r == nbits - 1
        dim = 0 if last else nbits - 1 - r
        keep = lax.index_in_dim(held, 0, dim, keepdims=False)
        away = lax.index_in_dim(held, 1, dim, keepdims=False)
        if last:
            pairs = [(i, i ^ 1) for i in range(n)]
        else:
            pairs = swap(up[r], down[r])
        if 2 * bot == cols:
            flat_feats = feats.reshape(-1, 2 * bot)
            payload = jnp.concatenate([flat_feats, away.reshape(-1, cols)], axis=0)
            if r == min(1, nbits - 1):
                master, student, payload = lax.optimization_barrier(
                    (teacher_master, student_weight, payload)
                )
                master_new = 0.996 * master + 0.004 * student.astype(jnp.float32)
            got = lax.ppermute(payload, "dp", pairs)
            got_feats = got[: flat_feats.shape[0]].reshape(feats.shape)
            got_held = got[flat_feats.shape[0]:].reshape(away.shape)
        else:
            if r == min(1, nbits - 1):
                master_new = rebuilt
            got_feats, got_held = lax.ppermute((feats, away), "dp", pairs)
        if last:
            got_feats = jnp.transpose(got_feats, cross_rev + [nbits - 1, nbits])
            got_held = jnp.transpose(got_held, cross_rev + [nbits - 1, nbits])
        feats = jnp.stack([feats, got_feats])
        held = jnp.stack([keep, got_held], axis=dim)
    feats = feats.reshape(-1, 2 * bot)
    src = me ^ pos
    where = src & 1
    for d, bit in enumerate(dim_bits):
        where = (where << 1) | ((src >> bit) & 1)
    held = jnp.take(held.reshape(n, 2 * rows, cols), where, axis=0)
    sw = held[:, :rows].reshape(n * rows, cols)
    tw = held[:, rows:].reshape(n * rows, cols)
    zt, zs = feats[:, :bot], feats[:, bot:]
    c = lax.dynamic_slice_in_dim(center, me * cols, cols)
    t_norm = jnp.sqrt(jnp.sum(jnp.square(tw.astype(jnp.float32)), 0) + 1e-06)
    s_norm = jnp.sqrt(jnp.sum(jnp.square(sw.astype(jnp.float32)), 0) + 1e-06)
    t_cos = jnp.dot(zt, tw, preferred_element_type=jnp.float32) / t_norm
    s_cos = jnp.dot(zs, sw, preferred_element_type=jnp.float32) / s_norm
    t_exp = jnp.exp((t_cos - c) / 0.04)
    s_exp = jnp.exp(s_cos / 0.1)
    totals = jnp.stack([jnp.sum(t_exp, 1), jnp.sum(s_exp, 1)])
    t_exp, s_exp = lax.optimization_barrier((t_exp.astype(jnp.bfloat16), s_exp.astype(jnp.bfloat16)))
    t_exp, s_exp = t_exp.astype(jnp.float32), s_exp.astype(jnp.float32)
    totals, master_new = lax.optimization_barrier((totals, master_new))
    shape = (2,) + (2,) * nbits + (images,)
    for r in range(nbits):
        if r == nbits - 1:
            got = lax.ppermute(totals, "dp", [(i, i ^ 1) for i in range(n)]).reshape(shape)
            got = jnp.flip(jnp.transpose(got, [0, 1] + [2 + d for d in cross_rev] + [nbits + 1]), 1)
        else:
            got = lax.ppermute(totals, "dp", swap(up[r], down[r])).reshape(shape)
            got = jnp.flip(got, nbits - r)
        totals = totals + got.reshape(totals.shape)
    totals = exchange_all(totals, "tensor", lax.axis_size("tensor"))
    t_total, s_total = totals[0][:, None], totals[1][:, None]
    part_center = 0.5 * c + 0.5 * (jnp.sum(t_cos, 0) / (images * n))
    dlog = ((s_exp / s_total - t_exp / t_total) / 0.1).astype(jnp.bfloat16)
    product = lax.dot_general(
        zs, dlog, (((0,), (0,)), ((), ())), preferred_element_type=jnp.float32
    )
    wide = sw.astype(jnp.float32)
    scaled = jnp.sum(wide * product, 0) / s_norm / s_norm
    grad = (product - wide * scaled) / s_norm
    high = part_center.astype(jnp.bfloat16)
    low = (part_center - high.astype(jnp.float32)).astype(jnp.bfloat16)
    lanes = 128 if (rows * cols) % 128 == 0 and (2 * cols) % 128 == 0 else cols
    grad_rows = rows * cols // lanes
    sent = jnp.concatenate(
        [
            grad.astype(jnp.bfloat16).reshape(n, grad_rows, lanes),
            jnp.broadcast_to(jnp.stack([high, low]), (n, 2, cols)).reshape(n, -1, lanes),
        ],
        axis=1,
    )
    got = lax.all_to_all(sent, "dp", 0, 0, tiled=True)
    student_grad = got[:, :grad_rows].reshape(n, rows, cols).transpose(1, 0, 2)
    student_grad = student_grad.reshape(rows, n * cols).astype(jnp.float32)
    half = cols // lanes
    high = got[:, grad_rows: grad_rows + half].astype(jnp.float32)
    low = got[:, grad_rows + half:].astype(jnp.float32)
    return (master_new, student_grad, (high + low).reshape(n * cols))


def solution(mesh):
    placed = (P("dp", "tensor"), P("dp", "tensor"), P("dp", None), P("dp", None), P("tensor"))
    return jax.shard_map(
        shards_for(mesh),
        mesh=mesh,
        in_specs=placed,
        out_specs=(P("dp", "tensor"), P("dp", "tensor"), P("tensor")),
        check_vma=False,
    )


def shards_for(mesh):
    ndp = mesh.shape["dp"]

    def shards(teacher_master, student_weight, teacher_feat, student_feat, center):
        images_all = teacher_feat.shape[0] * ndp
        cols = center.shape[0]
        if images_all < cols and cols % ndp == 0 and ndp > 1 and ndp & (ndp - 1) == 0:
            return feature_plan(teacher_master, student_weight, teacher_feat, student_feat, center)
        return weight_plan(teacher_master, student_weight, teacher_feat, student_feat, center)

    return shards
```

```python
import jax
import jax.numpy as jnp
from jax import lax
from jax.sharding import PartitionSpec as P


def unit_rows(feat):
    wide = feat.astype(jnp.float32)
    return (wide * lax.rsqrt(jnp.sum(wide * wide, 1, keepdims=True) + 1e-06)).astype(jnp.bfloat16)


def weight_plan(teacher_master, student_weight, teacher_feat, student_feat, center):
    zt = unit_rows(teacher_feat)
    zs = unit_rows(student_feat)
    images_all = teacher_feat.shape[0] * lax.axis_size("dp")
    student_full = lax.all_gather(student_weight, "dp", axis=0, tiled=True)
    master_new = 0.996 * teacher_master + 0.004 * student_weight.astype(jnp.float32)
    weight = lax.all_gather(master_new.astype(jnp.bfloat16), "dp", axis=0, tiled=True)
    raw = jnp.dot(zt, weight, preferred_element_type=jnp.float32)
    t_norm = jnp.sqrt(jnp.sum(jnp.square(weight.astype(jnp.float32)), 0) + 1e-06)
    t_cos = raw / t_norm
    s_norm = jnp.sqrt(jnp.sum(jnp.square(student_full.astype(jnp.float32)), 0) + 1e-06)
    s_cos = jnp.dot(zs, student_full, preferred_element_type=jnp.float32) / s_norm
    t_exp = jnp.exp((t_cos - center) / 0.04)
    s_exp = jnp.exp(s_cos / 0.1)
    t_total, s_total = lax.psum(
        (jnp.sum(t_exp, 1, keepdims=True), jnp.sum(s_exp, 1, keepdims=True)), "tensor"
    )
    cos_mean = lax.psum(jnp.sum(t_cos, 0), "dp") / images_all
    new_center = 0.5 * center + 0.5 * cos_mean
    dlog = ((s_exp / s_total - t_exp / t_total) / 0.1).astype(jnp.bfloat16)
    scaled = jnp.sum(dlog.astype(jnp.float32) * s_cos, 0) / s_norm
    product = lax.dot_general(
        zs, dlog, (((0,), (0,)), ((), ())), preferred_element_type=jnp.float32
    )
    student_grad = lax.psum_scatter(
        (product - student_full.astype(jnp.float32) * scaled) / s_norm,
        "dp",
        scatter_dimension=0,
        tiled=True,
    )
    return (master_new, student_grad, new_center)


def exchange_sum(x, axis, n):
    if n & (n - 1):
        return lax.psum(x, axis)
    step = 1
    while step < n:
        x = x + lax.ppermute(x, axis, [(i, i ^ step) for i in range(n)])
        step *= 2
    return x


def exchange_all(x, axis, n):
    total = x
    for k in range(1, n):
        total = total + lax.ppermute(x, axis, [(i, (i + k) % n) for i in range(n)])
    return total


def feature_plan(teacher_master, student_weight, teacher_feat, student_feat, center):
    n = lax.axis_size("dp")
    me = lax.axis_index("dp")
    rows, width = teacher_master.shape
    bot = teacher_feat.shape[1]
    images = teacher_feat.shape[0]
    cols = width // n
    nbits = n.bit_length() - 1
    odd = me % 2
    up = list(range(1, nbits))
    down = up[::-1]
    dim_bits = [jnp.where(odd == 1, down[r], up[r]) for r in range(nbits - 1)][::-1]
    rebuilt = 0.996 * teacher_master + 0.004 * student_weight.astype(jnp.float32)
    both = jnp.stack([student_weight, rebuilt.astype(jnp.bfloat16)])
    both = both.reshape(2, rows, n, cols).transpose(2, 0, 1, 3).reshape(n, 2 * rows, cols)
    pos = jnp.arange(n)
    rel = (pos >> (nbits - 1)) & 1
    for d, bit in enumerate(dim_bits):
        rel = rel | (((pos >> (nbits - 2 - d)) & 1) << bit)
    held = jnp.take(both, me ^ rel, axis=0).reshape((2,) * nbits + (2 * rows, cols))
    feats = jnp.concatenate([unit_rows(teacher_feat), unit_rows(student_feat)], axis=1)
    cross_rev = list(range(nbits - 2, -1, -1))

    def swap(pairs_up, pairs_down):
        return [(i, i ^ (1 << (pairs_down if i % 2 else pairs_up))) for i in range(n)]

    for r in range(nbits):
        last = r == nbits - 1
        dim = 0 if last else nbits - 1 - r
        keep = lax.index_in_dim(held, 0, dim, keepdims=False)
        away = lax.index_in_dim(held, 1, dim, keepdims=False)
        if last:
            pairs = [(i, i ^ 1) for i in range(n)]
        else:
            pairs = swap(up[r], down[r])
        if 2 * bot == cols:
            flat_feats = feats.reshape(-1, 2 * bot)
            payload = jnp.concatenate([flat_feats, away.reshape(-1, cols)], axis=0)
            if last:
                payload = away
            if r == min(1, nbits - 1):
                master, student, payload = lax.optimization_barrier(
                    (teacher_master, student_weight, payload)
                )
                master_new = 0.996 * master + 0.004 * student.astype(jnp.float32)
            got = lax.ppermute(payload, "dp", pairs)
            if last:
                got_held = got
                got_feats = lax.ppermute(feats, "dp", pairs)
            else:
                got_feats = got[: flat_feats.shape[0]].reshape(feats.shape)
                got_held = got[flat_feats.shape[0]:].reshape(away.shape)
        else:
            if r == min(1, nbits - 1):
                master_new = rebuilt
            got_feats, got_held = lax.ppermute((feats, away), "dp", pairs)
        if last:
            got_feats = jnp.transpose(got_feats, cross_rev + [nbits - 1, nbits])
            got_held = jnp.transpose(got_held, cross_rev + [nbits - 1, nbits])
        if last:
            halves = [feats.reshape(-1, 2 * bot), got_feats.reshape(-1, 2 * bot)]
        feats = jnp.stack([feats, got_feats])
        held = jnp.stack([keep, got_held], axis=dim)
    feats = feats.reshape(-1, 2 * bot)
    src = me ^ pos
    where = src & 1
    for d, bit in enumerate(dim_bits):
        where = (where << 1) | ((src >> bit) & 1)
    held = jnp.take(held.reshape(n, 2 * rows, cols), where, axis=0)
    sw = held[:, :rows].reshape(n * rows, cols)
    tw = held[:, rows:].reshape(n * rows, cols)
    c = lax.dynamic_slice_in_dim(center, me * cols, cols)
    t_norm = jnp.sqrt(jnp.sum(jnp.square(tw.astype(jnp.float32)), 0) + 1e-06)
    s_norm = jnp.sqrt(jnp.sum(jnp.square(sw.astype(jnp.float32)), 0) + 1e-06)

    def passes(part):
        t_cos = jnp.dot(part[:, :bot], tw, preferred_element_type=jnp.float32) / t_norm
        s_cos = jnp.dot(part[:, bot:], sw, preferred_element_type=jnp.float32) / s_norm
        t_exp = jnp.exp((t_cos - c) / 0.04)
        s_exp = jnp.exp(s_cos / 0.1)
        sums = jnp.stack([jnp.sum(t_exp, 1), jnp.sum(s_exp, 1)])
        return sums, jnp.sum(t_cos, 0), t_exp.astype(jnp.bfloat16), s_exp.astype(jnp.bfloat16)

    outs = [passes(part) for part in halves]
    totals = jnp.concatenate([o[0] for o in outs], axis=1)
    cos_sum = outs[0][1] + outs[1][1]
    exps = lax.optimization_barrier([(o[2], o[3]) for o in outs])
    totals, master_new = lax.optimization_barrier((totals, master_new))
    shape = (2,) + (2,) * nbits + (images,)
    for r in range(nbits):
        if r == nbits - 1:
            got = lax.ppermute(totals, "dp", [(i, i ^ 1) for i in range(n)]).reshape(shape)
            got = jnp.flip(jnp.transpose(got, [0, 1] + [2 + d for d in cross_rev] + [nbits + 1]), 1)
        else:
            got = lax.ppermute(totals, "dp", swap(up[r], down[r])).reshape(shape)
            got = jnp.flip(got, nbits - r)
        totals = totals + got.reshape(totals.shape)
    totals = exchange_all(totals, "tensor", lax.axis_size("tensor"))
    part_center = 0.5 * c + 0.5 * (cos_sum / (images * n))
    count = halves[0].shape[0]
    product = 0.0
    for h, (t_exp, s_exp) in enumerate(exps):
        t_total = totals[0][h * count: (h + 1) * count, None]
        s_total = totals[1][h * count: (h + 1) * count, None]
        dlog = ((s_exp.astype(jnp.float32) / s_total - t_exp.astype(jnp.float32) / t_total) / 0.1)
        product = product + lax.dot_general(
            halves[h][:, bot:], dlog.astype(jnp.bfloat16), (((0,), (0,)), ((), ())),
            preferred_element_type=jnp.float32,
        )
    wide = sw.astype(jnp.float32)
    scaled = jnp.sum(wide * product, 0) / s_norm / s_norm
    grad = (product - wide * scaled) / s_norm
    high = part_center.astype(jnp.bfloat16)
    low = (part_center - high.astype(jnp.float32)).astype(jnp.bfloat16)
    lanes = 128 if (rows * cols) % 128 == 0 and (2 * cols) % 128 == 0 else cols
    grad_rows = rows * cols // lanes
    sent = jnp.concatenate(
        [
            grad.astype(jnp.bfloat16).reshape(n, grad_rows, lanes),
            jnp.broadcast_to(jnp.stack([high, low]), (n, 2, cols)).reshape(n, -1, lanes),
        ],
        axis=1,
    )
    got = lax.all_to_all(sent, "dp", 0, 0, tiled=True)
    student_grad = got[:, :grad_rows].reshape(n, rows, cols).transpose(1, 0, 2)
    student_grad = student_grad.reshape(rows, n * cols).astype(jnp.float32)
    half = cols // lanes
    high = got[:, grad_rows: grad_rows + half].astype(jnp.float32)
    low = got[:, grad_rows + half:].astype(jnp.float32)
    return (master_new, student_grad, (high + low).reshape(n * cols))


def solution(mesh):
    placed = (P("dp", "tensor"), P("dp", "tensor"), P("dp", None), P("dp", None), P("tensor"))
    return jax.shard_map(
        shards_for(mesh),
        mesh=mesh,
        in_specs=placed,
        out_specs=(P("dp", "tensor"), P("dp", "tensor"), P("tensor")),
        check_vma=False,
    )


def shards_for(mesh):
    ndp = mesh.shape["dp"]

    def shards(teacher_master, student_weight, teacher_feat, student_feat, center):
        images_all = teacher_feat.shape[0] * ndp
        cols = center.shape[0]
        if images_all < cols and cols % ndp == 0 and ndp > 1 and ndp & (ndp - 1) == 0:
            return feature_plan(teacher_master, student_weight, teacher_feat, student_feat, center)
        return weight_plan(teacher_master, student_weight, teacher_feat, student_feat, center)

    return shards
```

```python
import jax
import jax.numpy as jnp
from jax import lax
from jax.sharding import PartitionSpec as P


def unit_rows(feat):
    wide = feat.astype(jnp.float32)
    return (wide * lax.rsqrt(jnp.sum(wide * wide, 1, keepdims=True) + 1e-06)).astype(jnp.bfloat16)


def weight_plan(teacher_master, student_weight, teacher_feat, student_feat, center):
    zt = unit_rows(teacher_feat)
    zs = unit_rows(student_feat)
    images_all = teacher_feat.shape[0] * lax.axis_size("dp")
    student_full = lax.all_gather(student_weight, "dp", axis=0, tiled=True)
    master_new = 0.996 * teacher_master + 0.004 * student_weight.astype(jnp.float32)
    weight = lax.all_gather(master_new.astype(jnp.bfloat16), "dp", axis=0, tiled=True)
    raw = jnp.dot(zt, weight, preferred_element_type=jnp.float32)
    t_norm = jnp.sqrt(jnp.sum(jnp.square(weight.astype(jnp.float32)), 0) + 1e-06)
    t_cos = raw / t_norm
    s_norm = jnp.sqrt(jnp.sum(jnp.square(student_full.astype(jnp.float32)), 0) + 1e-06)
    s_cos = jnp.dot(zs, student_full, preferred_element_type=jnp.float32) / s_norm
    t_exp = jnp.exp((t_cos - center) / 0.04)
    s_exp = jnp.exp(s_cos / 0.1)
    t_total, s_total = lax.psum(
        (jnp.sum(t_exp, 1, keepdims=True), jnp.sum(s_exp, 1, keepdims=True)), "tensor"
    )
    cos_mean = lax.psum(jnp.sum(t_cos, 0), "dp") / images_all
    new_center = 0.5 * center + 0.5 * cos_mean
    dlog = ((s_exp / s_total - t_exp / t_total) / 0.1).astype(jnp.bfloat16)
    scaled = jnp.sum(dlog.astype(jnp.float32) * s_cos, 0) / s_norm
    product = lax.dot_general(
        zs, dlog, (((0,), (0,)), ((), ())), preferred_element_type=jnp.float32
    )
    student_grad = lax.psum_scatter(
        (product - student_full.astype(jnp.float32) * scaled) / s_norm,
        "dp",
        scatter_dimension=0,
        tiled=True,
    )
    return (master_new, student_grad, new_center)


def exchange_sum(x, axis, n):
    if n & (n - 1):
        return lax.psum(x, axis)
    step = 1
    while step < n:
        x = x + lax.ppermute(x, axis, [(i, i ^ step) for i in range(n)])
        step *= 2
    return x


def exchange_all(x, axis, n):
    total = x
    for k in range(1, n):
        total = total + lax.ppermute(x, axis, [(i, (i + k) % n) for i in range(n)])
    return total


def feature_plan(teacher_master, student_weight, teacher_feat, student_feat, center):
    n = lax.axis_size("dp")
    me = lax.axis_index("dp")
    rows, width = teacher_master.shape
    bot = teacher_feat.shape[1]
    images = teacher_feat.shape[0]
    cols = width // n
    nbits = n.bit_length() - 1
    odd = me % 2
    up = list(range(1, nbits))
    down = up[::-1]
    dim_bits = [jnp.where(odd == 1, down[r], up[r]) for r in range(nbits - 1)][::-1]
    rebuilt = 0.996 * teacher_master + 0.004 * student_weight.astype(jnp.float32)
    both = jnp.stack([student_weight, rebuilt.astype(jnp.bfloat16)])
    both = both.reshape(2, rows, n, cols).transpose(2, 0, 1, 3).reshape(n, 2 * rows, cols)
    pos = jnp.arange(n)
    rel = (pos >> (nbits - 1)) & 1
    for d, bit in enumerate(dim_bits):
        rel = rel | (((pos >> (nbits - 2 - d)) & 1) << bit)
    held = jnp.take(both, me ^ rel, axis=0).reshape((2,) * nbits + (2 * rows, cols))
    feats = jnp.concatenate([unit_rows(teacher_feat), unit_rows(student_feat)], axis=1)
    cross_rev = list(range(nbits - 2, -1, -1))

    def swap(pairs_up, pairs_down):
        return [(i, i ^ (1 << (pairs_down if i % 2 else pairs_up))) for i in range(n)]

    for r in range(nbits):
        last = r == nbits - 1
        dim = 0 if last else nbits - 1 - r
        keep = lax.index_in_dim(held, 0, dim, keepdims=False)
        away = lax.index_in_dim(held, 1, dim, keepdims=False)
        if last:
            pairs = [(i, i ^ 1) for i in range(n)]
        else:
            pairs = swap(up[r], down[r])
        if 2 * bot == cols:
            flat_feats = feats.reshape(-1, 2 * bot)
            payload = jnp.concatenate([flat_feats, away.reshape(-1, cols)], axis=0)
            if last:
                payload = away
            if r == min(1, nbits - 1):
                master, student, payload = lax.optimization_barrier(
                    (teacher_master, student_weight, payload)
                )
                master_new = 0.996 * master + 0.004 * student.astype(jnp.float32)
            got = lax.ppermute(payload, "dp", pairs)
            if last:
                got_held = got
                pieces = [lax.ppermute(feats[k], "dp", pairs) for k in range(2)]
                got_feats = jnp.stack(pieces)
            else:
                got_feats = got[: flat_feats.shape[0]].reshape(feats.shape)
                got_held = got[flat_feats.shape[0]:].reshape(away.shape)
        else:
            if r == min(1, nbits - 1):
                master_new = rebuilt
            got_feats, got_held = lax.ppermute((feats, away), "dp", pairs)
        if last:
            got_feats = jnp.transpose(got_feats, cross_rev + [nbits - 1, nbits])
            got_held = jnp.transpose(got_held, cross_rev + [nbits - 1, nbits])
        if last:
            halves = [feats.reshape(-1, 2 * bot), got_feats.reshape(-1, 2 * bot)]
        feats = jnp.stack([feats, got_feats])
        held = jnp.stack([keep, got_held], axis=dim)
    feats = feats.reshape(-1, 2 * bot)
    src = me ^ pos
    where = src & 1
    for d, bit in enumerate(dim_bits):
        where = (where << 1) | ((src >> bit) & 1)
    held = jnp.take(held.reshape(n, 2 * rows, cols), where, axis=0)
    sw = held[:, :rows].reshape(n * rows, cols)
    tw = held[:, rows:].reshape(n * rows, cols)
    c = lax.dynamic_slice_in_dim(center, me * cols, cols)
    t_norm = jnp.sqrt(jnp.sum(jnp.square(tw.astype(jnp.float32)), 0) + 1e-06)
    s_norm = jnp.sqrt(jnp.sum(jnp.square(sw.astype(jnp.float32)), 0) + 1e-06)

    def passes(part):
        t_cos = jnp.dot(part[:, :bot], tw, preferred_element_type=jnp.float32) / t_norm
        s_cos = jnp.dot(part[:, bot:], sw, preferred_element_type=jnp.float32) / s_norm
        t_exp = jnp.exp((t_cos - c) / 0.04)
        s_exp = jnp.exp(s_cos / 0.1)
        sums = jnp.stack([jnp.sum(t_exp, 1), jnp.sum(s_exp, 1)])
        return sums, jnp.sum(t_cos, 0), t_exp.astype(jnp.bfloat16), s_exp.astype(jnp.bfloat16)

    split = nbits == 3 and 2 * bot == cols
    if split:
        halves = [halves[0]] + [p.reshape(-1, 2 * bot) for p in pieces]
    outs = [passes(part) for part in halves]
    if split:
        remote = jnp.stack([o[0].reshape(2, 2, images) for o in outs[1:]], axis=2)
        totals = jnp.concatenate([outs[0][0], remote.reshape(2, -1)], axis=1)
    else:
        totals = jnp.concatenate([o[0] for o in outs], axis=1)
    cos_sum = sum(o[1] for o in outs)
    exps = lax.optimization_barrier([(o[2], o[3]) for o in outs])
    totals, master_new = lax.optimization_barrier((totals, master_new))
    shape = (2,) + (2,) * nbits + (images,)
    for r in range(nbits):
        if r == nbits - 1:
            got = lax.ppermute(totals, "dp", [(i, i ^ 1) for i in range(n)]).reshape(shape)
            got = jnp.flip(jnp.transpose(got, [0, 1] + [2 + d for d in cross_rev] + [nbits + 1]), 1)
        else:
            got = lax.ppermute(totals, "dp", swap(up[r], down[r])).reshape(shape)
            got = jnp.flip(got, nbits - r)
        totals = totals + got.reshape(totals.shape)
    totals = exchange_all(totals, "tensor", lax.axis_size("tensor"))
    part_center = 0.5 * c + 0.5 * (cos_sum / (images * n))
    count = halves[0].shape[0]
    if split:
        remote = totals[:, count:].reshape(2, 2, 2, images)
        part_totals = [totals[:, :count]] + [remote[:, :, k].reshape(2, -1) for k in range(2)]
    else:
        part_totals = [totals[:, h * count: (h + 1) * count] for h in range(len(exps))]
    product = 0.0
    for h, (t_exp, s_exp) in enumerate(exps):
        t_total = part_totals[h][0][:, None]
        s_total = part_totals[h][1][:, None]
        dlog = ((s_exp.astype(jnp.float32) / s_total - t_exp.astype(jnp.float32) / t_total) / 0.1)
        product = product + lax.dot_general(
            halves[h][:, bot:], dlog.astype(jnp.bfloat16), (((0,), (0,)), ((), ())),
            preferred_element_type=jnp.float32,
        )
    wide = sw.astype(jnp.float32)
    scaled = jnp.sum(wide * product, 0) / s_norm / s_norm
    grad = (product - wide * scaled) / s_norm
    high = part_center.astype(jnp.bfloat16)
    low = (part_center - high.astype(jnp.float32)).astype(jnp.bfloat16)
    lanes = 128 if (rows * cols) % 128 == 0 and (2 * cols) % 128 == 0 else cols
    grad_rows = rows * cols // lanes
    sent = jnp.concatenate(
        [
            grad.astype(jnp.bfloat16).reshape(n, grad_rows, lanes),
            jnp.broadcast_to(jnp.stack([high, low]), (n, 2, cols)).reshape(n, -1, lanes),
        ],
        axis=1,
    )
    got = lax.all_to_all(sent, "dp", 0, 0, tiled=True)
    student_grad = got[:, :grad_rows].reshape(n, rows, cols).transpose(1, 0, 2)
    student_grad = student_grad.reshape(rows, n * cols).astype(jnp.float32)
    half = cols // lanes
    high = got[:, grad_rows: grad_rows + half].astype(jnp.float32)
    low = got[:, grad_rows + half:].astype(jnp.float32)
    return (master_new, student_grad, (high + low).reshape(n * cols))


def solution(mesh):
    placed = (P("dp", "tensor"), P("dp", "tensor"), P("dp", None), P("dp", None), P("tensor"))
    return jax.shard_map(
        shards_for(mesh),
        mesh=mesh,
        in_specs=placed,
        out_specs=(P("dp", "tensor"), P("dp", "tensor"), P("tensor")),
        check_vma=False,
    )


def shards_for(mesh):
    ndp = mesh.shape["dp"]

    def shards(teacher_master, student_weight, teacher_feat, student_feat, center):
        images_all = teacher_feat.shape[0] * ndp
        cols = center.shape[0]
        if images_all < cols and cols % ndp == 0 and ndp > 1 and ndp & (ndp - 1) == 0:
            return feature_plan(teacher_master, student_weight, teacher_feat, student_feat, center)
        return weight_plan(teacher_master, student_weight, teacher_feat, student_feat, center)

    return shards
```
